32 devices in a mesh: outer: 4 (over y, x), inner: 8 (over z, core).
Axes of the slice: x: 2, y: 2, z: 4, core: 2. Of those that a mesh axis runs over, the one named last changes fastest.
Arguments:
- tokens: bfloat16 [4096, 2048], P(('outer', 'inner')), may hold values from -6 to 6
- cotangent: bfloat16 [4096, 2048], P(('outer', 'inner')), may hold values from -6 to 6
- routes: int32 [4096, 8], P(('outer', 'inner')), may hold values from 0 to 31, all different within a row; in each aligned block of 128 rows (0 to 127, 128 to 255, ...) at most 36 rows name the same one
- router_weight: bfloat16 [2048, 32], replicated, may hold values from -0.125 to 0.125
- gate_saved: bfloat16 [32, 1152, 768], P(('outer', 'inner')), may hold values from -6 to 6
- up_saved: bfloat16 [32, 1152, 768], P(('outer', 'inner')), may hold values from -6 to 6
- gate_weight: bfloat16 [32, 2048, 768], P(('outer', 'inner')), may hold values from -0.125 to 0.125
- up_weight: bfloat16 [32, 2048, 768], P(('outer', 'inner')), may hold values from -0.125 to 0.125
- down_weight: bfloat16 [32, 768, 2048], P(('outer', 'inner')), may hold values from -0.21875 to 0.21875
Outputs:
- grad_tokens: bfloat16 [4096, 2048], P(('outer', 'inner'))
- grad_gate: bfloat16 [32, 2048, 768], P(('outer', 'inner'))
- grad_up: bfloat16 [32, 2048, 768], P(('outer', 'inner'))
- grad_down: bfloat16 [32, 768, 2048], P(('outer', 'inner'))
- grad_router: float32 [2048, 32], replicated
The draws below stay inside these ranges and needn't reach their ends.
Inputs may be any that keep to these rules, and one draw needn't show every extreme that they name: `routes`: each row names 8 different experts. Among the rows of one device no expert is named more than 36 times, and in every draw some expert is named exactly 36 times by the rows of some device.
All inputs are finite; a program needn't handle non-finite values.
Results may differ from the reference program's by a relative error of at most 0.01.
Values may be sent and summed in bfloat16 or wider, within the bound.
No kernel may reach another device: no remote copies, remote signals or barrier semaphores. Data moves between devices by JAX's collectives and lax.ppermute only.
A program may use at most 192 MiB of HBM per device.

```python
import math
import jax
import jax.numpy as jnp
import numpy as np
from jax import lax

D = 2048
FF = 768
TOP = 8
TOK_DEV = 128
EXPERTS = 32
CAP = 36
SLOTS = 1152
TOKENS = 4096
N_OUTER = 4
N_INNER = 8


def block_levels(stream_key, shape, split, low, top_value):
    factor_of = 1.0
    for dim, shards_of in split:
        heights = jax.random.uniform(jax.random.fold_in(jax.random.fold_in(stream_key, 6), dim), (shards_of,), jnp.float32, low / len(split), top_value / len(split))
        factor_of = factor_of * jnp.repeat(jnp.exp(heights), shape[dim] // shards_of).reshape((-1,) + (1,) * (len(shape) - 1 - dim))
    return factor_of


def deal_out(rng, own, number, rows, number_of, top, reach, slope):
    ranking = jax.random.permutation(rng, number_of)
    crowded, ordinary = shares(number_of, rows * top, reach, slope, True), shares(number_of, rows * top, reach, slope, False)
    places = jnp.arange(number_of)

    def named(sizes, offset_by):
        used = int((sizes > 0).sum())
        fixed = max(1, used // 4)
        shifted = fixed + (places - fixed + offset_by * (used - fixed)) % max(1, number_of - fixed)
        return jnp.zeros((number_of,), jnp.int32).at[ranking[jnp.where(places < fixed, places, shifted)]].set(jnp.asarray(sizes, jnp.int32))

    sizes = jnp.where(number % 4 == 0, named(crowded, number // 4), named(ordinary, number - number // 4 - 1))
    mixed = jax.random.permutation(jax.random.fold_in(own, 3), number_of)
    giver, taker = mixed[0:number_of // 2 * 2:2], mixed[1:number_of // 2 * 2:2]
    room = jnp.minimum(sizes[giver] - 1, reach - sizes[taker]) // 2
    room = jnp.where((giver == ranking[0]) | (taker == ranking[0]) | (sizes[taker] == 0), 0, jnp.maximum(room, 0))
    shifted = jax.random.randint(jax.random.fold_in(own, 4), (number_of // 2,), 0, 1 << 20) % (room + 1)
    sizes = sizes.at[giver].add(-shifted).at[taker].add(shifted)
    labels = jnp.searchsorted(jnp.cumsum(sizes), jnp.arange(rows * top), side="right").astype(jnp.int32)
    table = labels.reshape(top, rows).T
    table = table[jax.random.permutation(jax.random.fold_in(own, 1), rows)]
    offset_by = jax.random.randint(jax.random.fold_in(own, 2), (rows, 1), 0, top)
    return jnp.take_along_axis(table, (jnp.arange(top)[None, :] + offset_by) % top, axis=1)


def shares(count, total, bound, slope, full):
    loads = [(1 << 20) // math.isqrt(rank ** slope) + 1 for rank in range(1, count + 1)]
    largest = bound if full else min(bound, max(-(-total // count), total * loads[0] // sum(loads)))
    least = 1 if total - largest >= count - 1 else 0
    given, surplus = [largest] + [least] * (count - 1), total - largest - least * (count - 1)
    while surplus > 0:
        movable = [i for i in range(1, count) if given[i] < largest] or [i for i in range(1, count) if given[i] < bound]
        pool, left = sum([loads[i] for i in movable]), surplus
        for i in movable:
            extra = min(bound - given[i], max(1, left * loads[i] // pool), surplus)
            given[i] = given[i] + extra
            surplus = surplus - extra
    return np.array(given)


def noise(rng, extent, deviation, limit, split=(), held_as=jnp.bfloat16):
    loudness = block_levels(rng, extent, split, -0.22, 0.18) if split else 1.0
    drawn = jax.random.normal(rng, extent, jnp.float32) * deviation * loudness
    return jnp.minimum(jnp.maximum(drawn, -limit), limit).astype(held_as)


def setup_inputs(seed: int = 0) -> dict:
    keys = jax.random.split(jax.random.key(seed), 10)
    tokens = noise(keys[0], (TOKENS, D), 1.0, 6.0, ((0, 32),))
    cotangent = noise(keys[1], (TOKENS, D), 1.0, 6.0, ((0, 32),))
    routes_keys = jax.random.split(jax.random.fold_in(keys[2], 1), TOKENS // TOK_DEV)
    routes_turns = jax.random.permutation(jax.random.fold_in(keys[2], 3), TOKENS // TOK_DEV)
    routes = jax.vmap(lambda own, number: deal_out(jax.random.fold_in(keys[2], 2), own, number, TOK_DEV, EXPERTS, TOP, CAP, 2))(routes_keys, routes_turns).reshape((TOKENS, TOP))
    router_weight = noise(keys[3], (D, EXPERTS), D ** -0.5, 0.125)
    gate_saved = noise(keys[4], (EXPERTS, SLOTS, FF), 1.0, 6.0, ((0, 32),))
    up_saved = noise(keys[5], (EXPERTS, SLOTS, FF), 1.0, 6.0, ((0, 32),))
    gate_weight = noise(keys[6], (EXPERTS, D, FF), D ** -0.5, 0.125, ((0, 32),))
    up_weight = noise(keys[7], (EXPERTS, D, FF), D ** -0.5, 0.125, ((0, 32),))
    down_weight = noise(keys[8], (EXPERTS, FF, D), FF ** -0.5, 0.21875, ((0, 32),))
    return dict(tokens=tokens, cotangent=cotangent, routes=routes, router_weight=router_weight, gate_saved=gate_saved, up_saved=up_saved, gate_weight=gate_weight, up_weight=up_weight, down_weight=down_weight)


contract_rows = (((0,), (0,)), ((), ()))
contract_cols = (((1,), (1,)), ((), ()))

def route_tables(routes, experts, capacity):
    flat_routes = routes.reshape(-1)
    onehot = (flat_routes[:, None] == jnp.arange(experts, dtype=jnp.int32)[None, :]).astype(jnp.int32)
    earlier = jnp.cumsum(onehot, axis=0) - onehot
    position = lax.optimization_barrier(jnp.sum(earlier * onehot, axis=1))
    target = (flat_routes * capacity + position).astype(jnp.int32)
    slot_table = (jnp.arange(experts * capacity, dtype=jnp.int32)[:, None] == target[None, :]).astype(jnp.bfloat16)
    token_table = lax.optimization_barrier(jnp.sum(slot_table.reshape(experts * capacity, routes.shape[0], routes.shape[1]), axis=2))
    return (slot_table, token_table)

def route_probs(tokens, routes, router_weight):
    router_logits = jnp.dot(tokens, router_weight, preferred_element_type=jnp.float32)
    picked = routes[:, :, None] == jnp.arange(router_weight.shape[1], dtype=jnp.int32)[None, None, :]
    chosen = lax.optimization_barrier(jnp.sum(jnp.where(picked, router_logits[:, None, :], jnp.float32(0.0)), axis=2))
    exp_terms = jnp.exp(chosen)
    return (picked, exp_terms / lax.optimization_barrier(jnp.sum(exp_terms, axis=1, keepdims=True)))

def dispatch_block(tokens, cotangent, routes, router_weight, capacity):
    picked, probs = route_probs(tokens, routes, router_weight)
    slot_table, token_table = route_tables(routes, router_weight.shape[1], capacity)
    send_tokens = jnp.dot(token_table, tokens, preferred_element_type=jnp.float32).astype(jnp.bfloat16)
    send_cot = jnp.dot(token_table, cotangent, preferred_element_type=jnp.float32).astype(jnp.bfloat16)
    probs_low = probs.astype(jnp.bfloat16).reshape(-1)
    send_weight = jnp.dot(slot_table, probs_low, preferred_element_type=jnp.float32).astype(jnp.bfloat16)
    return (picked, probs, slot_table, token_table, send_tokens, send_cot, send_weight)

def slot_dot(cot_rows, out_rows):
    return lax.optimization_barrier(jnp.sum(cot_rows.astype(jnp.float32) * out_rows.astype(jnp.float32), axis=1)).astype(jnp.bfloat16)

def expert_backward(input_rows, cot_rows, weight_rows, gate_pre, up_pre, gate_matrix, up_matrix, down_matrix):
    gate_value = gate_pre.astype(jnp.float32)
    up_value = up_pre.astype(jnp.float32)
    sigmoid_gate = jax.nn.sigmoid(gate_value)
    silu_gate = gate_value * sigmoid_gate
    hidden = (silu_gate * up_value).astype(jnp.bfloat16)
    expert_out = jnp.dot(hidden, down_matrix, preferred_element_type=jnp.float32).astype(jnp.bfloat16)
    scaled_cot = (weight_rows.astype(jnp.float32)[:, None] * cot_rows.astype(jnp.float32)).astype(jnp.bfloat16)
    grad_hidden = lax.dot_general(scaled_cot, down_matrix, contract_cols, preferred_element_type=jnp.float32)
    grad_gate_pre = (grad_hidden * up_value * sigmoid_gate * (1.0 + gate_value * (1.0 - sigmoid_gate))).astype(jnp.bfloat16)
    grad_up_pre = (grad_hidden * silu_gate).astype(jnp.bfloat16)
    grad_rows = (lax.dot_general(grad_gate_pre, gate_matrix, contract_cols, preferred_element_type=jnp.float32) + lax.dot_general(grad_up_pre, up_matrix, contract_cols, preferred_element_type=jnp.float32)).astype(jnp.bfloat16)
    grad_gate_w = lax.dot_general(input_rows, grad_gate_pre, contract_rows, preferred_element_type=jnp.float32).astype(jnp.bfloat16)
    grad_up_w = lax.dot_general(input_rows, grad_up_pre, contract_rows, preferred_element_type=jnp.float32).astype(jnp.bfloat16)
    grad_down_w = lax.dot_general(hidden, scaled_cot, contract_rows, preferred_element_type=jnp.float32).astype(jnp.bfloat16)
    return (grad_rows, expert_out, grad_gate_w, grad_up_w, grad_down_w)

def finish_block(tokens, router_weight, picked, probs, slot_table, token_table, back_rows, route_dot):
    grad_sum = lax.dot_general(token_table, back_rows, contract_rows, preferred_element_type=jnp.float32)
    route_grad = lax.dot_general(slot_table, route_dot, contract_rows, preferred_element_type=jnp.float32).reshape(probs.shape)
    inner_term = lax.optimization_barrier(jnp.sum(probs * route_grad, axis=1, keepdims=True))
    chosen_grad = probs * (route_grad - inner_term)
    logit_grad = lax.optimization_barrier(jnp.sum(jnp.where(picked, chosen_grad[:, :, None], jnp.float32(0.0)), axis=1)).astype(jnp.bfloat16)
    grad_tokens = (grad_sum + lax.dot_general(logit_grad, router_weight, contract_cols, preferred_element_type=jnp.float32)).astype(jnp.bfloat16)
    router_part = lax.dot_general(tokens, logit_grad, contract_rows, preferred_element_type=jnp.float32)
    return (grad_tokens, router_part)

def reference(tokens, cotangent, routes, router_weight, gate_saved, up_saved, gate_weight, up_weight, down_weight):
    sources = N_OUTER * N_INNER
    split_tokens = tokens.reshape(sources, TOK_DEV, D)
    split_cot = cotangent.reshape(sources, TOK_DEV, D)
    split_routes = routes.reshape(sources, TOK_DEV, TOP)

    def first_phase(block):
        outcome = dispatch_block(block[0], block[1], block[2], router_weight, CAP)
        return (outcome[4], outcome[5], outcome[6])
    send_tokens, send_cot, send_weight = lax.map(first_phase, (split_tokens, split_cot, split_routes))

    def to_experts(array):
        tail = array.shape[2:]
        grid = array.reshape((sources, EXPERTS, CAP) + tail)
        return jnp.swapaxes(grid, 0, 1).reshape((EXPERTS, sources * CAP) + tail)

    def to_sources(array):
        tail = array.shape[2:]
        grid = array.reshape((EXPERTS, sources, CAP) + tail)
        return jnp.swapaxes(grid, 0, 1).reshape((sources, EXPERTS * CAP) + tail)

    def expert_phase(packed):
        grad_rows, expert_out, grad_gate_w, grad_up_w, grad_down_w = expert_backward(*packed)
        return (grad_rows, slot_dot(packed[1], expert_out), grad_gate_w, grad_up_w, grad_down_w)
    grad_rows, route_dot, grad_gate, grad_up, grad_down = lax.map(expert_phase, (to_experts(send_tokens), to_experts(send_cot), to_experts(send_weight), gate_saved, up_saved, gate_weight, up_weight, down_weight))
    back_rows = to_sources(grad_rows)
    back_dot = to_sources(route_dot)

    def last_phase(block):
        picked, probs = route_probs(block[0], block[1], router_weight)
        slot_table, token_table = route_tables(block[1], EXPERTS, CAP)
        return finish_block(block[0], router_weight, picked, probs, slot_table, token_table, block[2], block[3])
    grad_blocks, router_parts = lax.map(last_phase, (split_tokens, split_routes, back_rows, back_dot))
    grad_router = lax.optimization_barrier(jnp.sum(router_parts, axis=0)) * (1.0 / math.sqrt(TOKENS))
    return (grad_blocks.reshape(TOKENS, D), grad_gate, grad_up, grad_down, grad_router)
```

```python
import math

import jax
import jax.numpy as jnp
from jax import lax
from jax.sharding import PartitionSpec as P

contract_rows = (((0,), (0,)), ((), ()))
contract_cols = (((1,), (1,)), ((), ()))


def route_tables(routes, experts, capacity):
    flat_routes = routes.reshape(-1)
    onehot = (flat_routes[:, None] == jnp.arange(experts, dtype=jnp.int32)[None, :]).astype(
        jnp.int32
    )
    earlier = jnp.cumsum(onehot, axis=0) - onehot
    position = jnp.sum(earlier * onehot, axis=1)
    target = flat_routes * capacity + position
    slot_table = (
        jnp.arange(experts * capacity, dtype=jnp.int32)[:, None] == target[None, :]
    ).astype(jnp.bfloat16)
    token_table = jnp.sum(
        slot_table.reshape(experts * capacity, routes.shape[0], routes.shape[1]), axis=2
    )
    return (slot_table, token_table)


def route_probs(tokens, routes, router_weight):
    router_logits = jnp.dot(tokens, router_weight, preferred_element_type=jnp.float32)
    picked = (
        routes[:, :, None] == jnp.arange(router_weight.shape[1], dtype=jnp.int32)[None, None, :]
    )
    chosen = jnp.sum(jnp.where(picked, router_logits[:, None, :], jnp.float32(0.0)), axis=2)
    exp_terms = jnp.exp(chosen)
    return (picked, exp_terms / jnp.sum(exp_terms, axis=1, keepdims=True))


def dispatch_block(tokens, cotangent, routes, router_weight, capacity):
    picked, probs = route_probs(tokens, routes, router_weight)
    slot_table, token_table = route_tables(routes, router_weight.shape[1], capacity)
    send_tokens = jnp.dot(token_table, tokens, preferred_element_type=jnp.float32).astype(
        jnp.bfloat16
    )
    send_cot = jnp.dot(token_table, cotangent, preferred_element_type=jnp.float32).astype(
        jnp.bfloat16
    )
    probs_low = probs.astype(jnp.bfloat16).reshape(-1)
    send_weight = jnp.dot(slot_table, probs_low, preferred_element_type=jnp.float32).astype(
        jnp.bfloat16
    )
    return (picked, probs, slot_table, token_table, send_tokens, send_cot, send_weight)


def slot_dot(cot_rows, out_rows):
    return jnp.sum(cot_rows.astype(jnp.float32) * out_rows.astype(jnp.float32), axis=1).astype(
        jnp.bfloat16
    )


def expert_backward(
    input_rows, cot_rows, weight_rows, gate_pre, up_pre, gate_matrix, up_matrix, down_matrix
):
    gate_value = gate_pre.astype(jnp.float32)
    up_value = up_pre.astype(jnp.float32)
    sigmoid_gate = jax.nn.sigmoid(gate_value)
    silu_gate = gate_value * sigmoid_gate
    hidden = (silu_gate * up_value).astype(jnp.bfloat16)
    expert_out = jnp.dot(hidden, down_matrix, preferred_element_type=jnp.float32).astype(
        jnp.bfloat16
    )
    scaled_cot = (weight_rows.astype(jnp.float32)[:, None] * cot_rows.astype(jnp.float32)).astype(
        jnp.bfloat16
    )
    grad_hidden = lax.dot_general(
        scaled_cot, down_matrix, contract_cols, preferred_element_type=jnp.float32
    )
    grad_gate_pre = (
        grad_hidden * up_value * sigmoid_gate * (1.0 + gate_value * (1.0 - sigmoid_gate))
    ).astype(jnp.bfloat16)
    grad_up_pre = (grad_hidden * silu_gate).astype(jnp.bfloat16)
    grad_rows = (
        lax.dot_general(
            grad_gate_pre, gate_matrix, contract_cols, preferred_element_type=jnp.float32
        )
        + lax.dot_general(grad_up_pre, up_matrix, contract_cols, preferred_element_type=jnp.float32)
    ).astype(jnp.bfloat16)
    grad_gate_w = lax.dot_general(
        input_rows, grad_gate_pre, contract_rows, preferred_element_type=jnp.float32
    ).astype(jnp.bfloat16)
    grad_up_w = lax.dot_general(
        input_rows, grad_up_pre, contract_rows, preferred_element_type=jnp.float32
    ).astype(jnp.bfloat16)
    grad_down_w = lax.dot_general(
        hidden, scaled_cot, contract_rows, preferred_element_type=jnp.float32
    ).astype(jnp.bfloat16)
    return (grad_rows, expert_out, grad_gate_w, grad_up_w, grad_down_w)


def finish_block(
    tokens, router_weight, picked, probs, slot_table, token_table, back_rows, route_dot
):
    grad_sum = lax.dot_general(
        token_table, back_rows, contract_rows, preferred_element_type=jnp.float32
    )
    route_grad = lax.dot_general(
        slot_table, route_dot, contract_rows, preferred_element_type=jnp.float32
    ).reshape(probs.shape)
    inner_term = jnp.sum(probs * route_grad, axis=1, keepdims=True)
    chosen_grad = probs * (route_grad - inner_term)
    logit_grad = jnp.sum(
        jnp.where(picked, chosen_grad[:, :, None], jnp.float32(0.0)), axis=1
    ).astype(jnp.bfloat16)
    grad_tokens = (
        grad_sum
        + lax.dot_general(
            logit_grad, router_weight, contract_cols, preferred_element_type=jnp.float32
        )
    ).astype(jnp.bfloat16)
    router_part = lax.dot_general(
        tokens, logit_grad, contract_rows, preferred_element_type=jnp.float32
    )
    return (grad_tokens, router_part)


def body(
    tokens,
    cotangent,
    routes,
    router_weight,
    gate_saved,
    up_saved,
    gate_weight,
    up_weight,
    down_weight,
):
    experts = router_weight.shape[1]
    width = tokens.shape[1]
    capacity = gate_saved.shape[1] // experts
    outer_size = lax.axis_size("outer")
    inner_size = lax.axis_size("inner")
    picked, probs, slot_table, token_table, send_tokens, send_cot, send_weight = dispatch_block(
        tokens, cotangent, routes, router_weight, capacity
    )
    grid_tokens = send_tokens.reshape(experts, capacity, width)
    grid_cot = send_cot.reshape(experts, capacity, width)
    grid_weight = send_weight.reshape(experts, capacity)
    got_tokens, got_cot, got_weight = (
        lax.all_to_all(grid_tokens, ("outer", "inner"), split_axis=0, concat_axis=0, tiled=True),
        lax.all_to_all(grid_cot, ("outer", "inner"), split_axis=0, concat_axis=0, tiled=True),
        lax.all_to_all(grid_weight, ("outer", "inner"), split_axis=0, concat_axis=0, tiled=True),
    )
    cot_rows = got_cot.reshape(-1, width)
    grad_rows, expert_out, grad_gate_w, grad_up_w, grad_down_w = expert_backward(
        got_tokens.reshape(-1, width),
        cot_rows,
        got_weight.reshape(-1),
        gate_saved[0],
        up_saved[0],
        gate_weight[0],
        up_weight[0],
        down_weight[0],
    )
    back_grad = grad_rows.reshape(experts, capacity, width)
    slot_route_dot = slot_dot(cot_rows, expert_out).reshape(experts, capacity)
    back_rows, back_dot = (
        lax.all_to_all(back_grad, ("outer", "inner"), split_axis=0, concat_axis=0, tiled=True),
        lax.all_to_all(slot_route_dot, ("outer", "inner"), split_axis=0, concat_axis=0, tiled=True),
    )
    route_dot = back_dot.reshape(-1)
    grad_tokens, router_part = finish_block(
        tokens,
        router_weight,
        picked,
        probs,
        slot_table,
        token_table,
        back_rows.reshape(-1, width),
        route_dot,
    )
    total_tokens = tokens.shape[0] * outer_size * inner_size
    grad_router = lax.psum(router_part, ("outer", "inner")) * (1.0 / math.sqrt(total_tokens))
    return (grad_tokens, grad_gate_w[None], grad_up_w[None], grad_down_w[None], grad_router)


def solution(mesh):
    in_specs = (
        P(("outer", "inner"), None),
        P(("outer", "inner"), None),
        P(("outer", "inner"), None),
        P(),
        P(("outer", "inner"), None, None),
        P(("outer", "inner"), None, None),
        P(("outer", "inner"), None, None),
        P(("outer", "inner"), None, None),
        P(("outer", "inner"), None, None),
    )
    out_specs = (
        P(("outer", "inner"), None),
        P(("outer", "inner"), None, None),
        P(("outer", "inner"), None, None),
        P(("outer", "inner"), None, None),
        P(),
    )
    return jax.shard_map(body, mesh=mesh, in_specs=in_specs, out_specs=out_specs, check_vma=False)
```

```python
import math

import jax
import jax.numpy as jnp
from jax import lax
from jax.sharding import PartitionSpec as P

contract_rows = (((0,), (0,)), ((), ()))
contract_cols = (((1,), (1,)), ((), ()))


def route_tables(routes, experts, capacity):
    flat_routes = routes.reshape(-1)
    onehot = (flat_routes[:, None] == jnp.arange(experts, dtype=jnp.int32)[None, :]).astype(
        jnp.int32
    )
    pairs = flat_routes.shape[0]
    lower = (
        jnp.arange(pairs, dtype=jnp.int32)[:, None] > jnp.arange(pairs, dtype=jnp.int32)[None, :]
    ).astype(jnp.bfloat16)
    earlier = jnp.dot(
        lower, onehot.astype(jnp.bfloat16), preferred_element_type=jnp.float32
    ).astype(jnp.int32)
    position = jnp.sum(earlier * onehot, axis=1)
    target = flat_routes * capacity + position
    slot_table = (
        jnp.arange(experts * capacity, dtype=jnp.int32)[:, None] == target[None, :]
    ).astype(jnp.bfloat16)
    token_table = jnp.sum(
        slot_table.reshape(experts * capacity, routes.shape[0], routes.shape[1]), axis=2
    )
    return (slot_table, token_table)


def route_probs(tokens, routes, router_weight):
    router_logits = jnp.dot(tokens, router_weight, preferred_element_type=jnp.float32)
    picked = (
        routes[:, :, None] == jnp.arange(router_weight.shape[1], dtype=jnp.int32)[None, None, :]
    )
    chosen = jnp.sum(jnp.where(picked, router_logits[:, None, :], jnp.float32(0.0)), axis=2)
    exp_terms = jnp.exp(chosen)
    return (picked, exp_terms / jnp.sum(exp_terms, axis=1, keepdims=True))


def dispatch_block(tokens, cotangent, routes, router_weight, capacity):
    picked, probs = route_probs(tokens, routes, router_weight)
    slot_table, token_table = route_tables(routes, router_weight.shape[1], capacity)
    send_tokens = jnp.dot(token_table, tokens, preferred_element_type=jnp.float32).astype(
        jnp.bfloat16
    )
    send_cot = jnp.dot(token_table, cotangent, preferred_element_type=jnp.float32).astype(
        jnp.bfloat16
    )
    probs_low = probs.astype(jnp.bfloat16).reshape(-1)
    send_weight = jnp.dot(slot_table, probs_low, preferred_element_type=jnp.float32).astype(
        jnp.bfloat16
    )
    return (picked, probs, slot_table, token_table, send_tokens, send_cot, send_weight)


def slot_dot(cot_rows, out_rows):
    return jnp.sum(cot_rows.astype(jnp.float32) * out_rows.astype(jnp.float32), axis=1).astype(
        jnp.bfloat16
    )


def expert_backward(
    input_rows, cot_rows, weight_rows, gate_pre, up_pre, gate_matrix, up_matrix, down_matrix
):
    gate_value = gate_pre.astype(jnp.float32)
    up_value = up_pre.astype(jnp.float32)
    sigmoid_gate = jax.nn.sigmoid(gate_value)
    silu_gate = gate_value * sigmoid_gate
    hidden = (silu_gate * up_value).astype(jnp.bfloat16)
    expert_out = jnp.dot(hidden, down_matrix, preferred_element_type=jnp.float32).astype(
        jnp.bfloat16
    )
    scaled_cot = (weight_rows.astype(jnp.float32)[:, None] * cot_rows.astype(jnp.float32)).astype(
        jnp.bfloat16
    )
    grad_hidden = lax.dot_general(
        scaled_cot, down_matrix, contract_cols, preferred_element_type=jnp.float32
    )
    grad_gate_pre = (
        grad_hidden * up_value * sigmoid_gate * (1.0 + gate_value * (1.0 - sigmoid_gate))
    ).astype(jnp.bfloat16)
    grad_up_pre = (grad_hidden * silu_gate).astype(jnp.bfloat16)
    grad_rows = (
        lax.dot_general(
            grad_gate_pre, gate_matrix, contract_cols, preferred_element_type=jnp.float32
        )
        + lax.dot_general(grad_up_pre, up_matrix, contract_cols, preferred_element_type=jnp.float32)
    ).astype(jnp.bfloat16)
    grad_gate_w = lax.dot_general(
        input_rows, grad_gate_pre, contract_rows, preferred_element_type=jnp.float32
    ).astype(jnp.bfloat16)
    grad_up_w = lax.dot_general(
        input_rows, grad_up_pre, contract_rows, preferred_element_type=jnp.float32
    ).astype(jnp.bfloat16)
    grad_down_w = lax.dot_general(
        hidden, scaled_cot, contract_rows, preferred_element_type=jnp.float32
    ).astype(jnp.bfloat16)
    return (grad_rows, expert_out, grad_gate_w, grad_up_w, grad_down_w)


def finish_block(
    tokens, router_weight, picked, probs, slot_table, token_table, back_rows, route_dot
):
    grad_sum = lax.dot_general(
        token_table, back_rows, contract_rows, preferred_element_type=jnp.float32
    )
    route_grad = lax.dot_general(
        slot_table, route_dot, contract_rows, preferred_element_type=jnp.float32
    ).reshape(probs.shape)
    inner_term = jnp.sum(probs * route_grad, axis=1, keepdims=True)
    chosen_grad = probs * (route_grad - inner_term)
    logit_grad = jnp.sum(
        jnp.where(picked, chosen_grad[:, :, None], jnp.float32(0.0)), axis=1
    ).astype(jnp.bfloat16)
    grad_tokens = (
        grad_sum
        + lax.dot_general(
            logit_grad, router_weight, contract_cols, preferred_element_type=jnp.float32
        )
    ).astype(jnp.bfloat16)
    router_part = lax.dot_general(
        tokens, logit_grad, contract_rows, preferred_element_type=jnp.float32
    )
    return (grad_tokens, router_part)


def body(
    tokens,
    cotangent,
    routes,
    router_weight,
    gate_saved,
    up_saved,
    gate_weight,
    up_weight,
    down_weight,
):
    experts = router_weight.shape[1]
    width = tokens.shape[1]
    capacity = gate_saved.shape[1] // experts
    outer_size = lax.axis_size("outer")
    inner_size = lax.axis_size("inner")
    axes = ("outer", "inner")
    picked, probs = route_probs(tokens, routes, router_weight)
    slot_table, token_table = route_tables(routes, experts, capacity)
    both = jnp.concatenate([tokens, cotangent], axis=1)
    grid_both = jnp.dot(
        token_table.reshape(experts, capacity, -1), both, preferred_element_type=jnp.float32
    ).astype(jnp.bfloat16)
    probs_low = probs.astype(jnp.bfloat16).reshape(-1)
    send_weight = jnp.dot(slot_table, probs_low, preferred_element_type=jnp.float32).astype(
        jnp.bfloat16
    )
    grid_weight = send_weight.reshape(experts, capacity)
    got_both = lax.all_to_all(grid_both, axes, split_axis=0, concat_axis=0, tiled=True)
    got_weight = lax.all_to_all(grid_weight, axes, split_axis=0, concat_axis=0, tiled=True)
    got_both = got_both.reshape(-1, 2 * width)
    input_rows = got_both[:, :width]
    cot_rows = got_both[:, width:]
    grad_rows, expert_out, grad_gate_w, grad_up_w, grad_down_w = expert_backward(
        input_rows,
        cot_rows,
        got_weight.reshape(-1),
        gate_saved[0],
        up_saved[0],
        gate_weight[0],
        up_weight[0],
        down_weight[0],
    )
    slot_route_dot = slot_dot(cot_rows, expert_out).reshape(experts, capacity)
    back_dot = lax.all_to_all(slot_route_dot, axes, split_axis=0, concat_axis=0, tiled=True)
    route_dot = back_dot.reshape(-1)
    route_grad = lax.dot_general(
        slot_table, route_dot, contract_rows, preferred_element_type=jnp.float32
    ).reshape(probs.shape)
    inner_term = jnp.sum(probs * route_grad, axis=1, keepdims=True)
    chosen_grad = probs * (route_grad - inner_term)
    logit_grad = jnp.sum(
        jnp.where(picked, chosen_grad[:, :, None], jnp.float32(0.0)), axis=1
    ).astype(jnp.bfloat16)
    router_part = lax.dot_general(
        tokens, logit_grad, contract_rows, preferred_element_type=jnp.float32
    )
    total_tokens = tokens.shape[0] * outer_size * inner_size
    grad_router = lax.psum(router_part, axes) * (1.0 / math.sqrt(total_tokens))
    back_grad = grad_rows.reshape(experts, capacity, width)
    grad_router, back_grad = lax.optimization_barrier((grad_router, back_grad))
    back_rows = lax.all_to_all(back_grad, axes, split_axis=0, concat_axis=0, tiled=True)
    grad_sum = lax.dot_general(
        token_table, back_rows.reshape(-1, width), contract_rows, preferred_element_type=jnp.float32
    )
    grad_tokens = (
        grad_sum
        + lax.dot_general(
            logit_grad, router_weight, contract_cols, preferred_element_type=jnp.float32
        )
    ).astype(jnp.bfloat16)
    return (grad_tokens, grad_gate_w[None], grad_up_w[None], grad_down_w[None], grad_router)


def solution(mesh):
    in_specs = (
        P(("outer", "inner"), None),
        P(("outer", "inner"), None),
        P(("outer", "inner"), None),
        P(),
        P(("outer", "inner"), None, None),
        P(("outer", "inner"), None, None),
        P(("outer", "inner"), None, None),
        P(("outer", "inner"), None, None),
        P(("outer", "inner"), None, None),
    )
    out_specs = (
        P(("outer", "inner"), None),
        P(("outer", "inner"), None, None),
        P(("outer", "inner"), None, None),
        P(("outer", "inner"), None, None),
        P(),
    )
    return jax.shard_map(body, mesh=mesh, in_specs=in_specs, out_specs=out_specs, check_vma=False)
```

```python
import math

import jax
import jax.numpy as jnp
from jax import lax
from jax.sharding import PartitionSpec as P

contract_rows = (((0,), (0,)), ((), ()))
contract_cols = (((1,), (1,)), ((), ()))


def route_tables(routes, experts, capacity):
    flat_routes = routes.reshape(-1)
    onehot = (flat_routes[:, None] == jnp.arange(experts, dtype=jnp.int32)[None, :]).astype(
        jnp.int32
    )
    pairs = flat_routes.shape[0]
    lower = (
        jnp.arange(pairs, dtype=jnp.int32)[:, None] > jnp.arange(pairs, dtype=jnp.int32)[None, :]
    ).astype(jnp.bfloat16)
    earlier = jnp.dot(
        lower, onehot.astype(jnp.bfloat16), preferred_element_type=jnp.float32
    ).astype(jnp.int32)
    position = jnp.sum(earlier * onehot, axis=1)
    target = flat_routes * capacity + position
    slot_table = (
        jnp.arange(experts * capacity, dtype=jnp.int32)[:, None] == target[None, :]
    ).astype(jnp.bfloat16)
    token_table = jnp.sum(
        slot_table.reshape(experts * capacity, routes.shape[0], routes.shape[1]), axis=2
    )
    return (slot_table, token_table)


def route_probs(tokens, routes, router_weight):
    router_logits = jnp.dot(tokens, router_weight, preferred_element_type=jnp.float32)
    picked = (
        routes[:, :, None] == jnp.arange(router_weight.shape[1], dtype=jnp.int32)[None, None, :]
    )
    chosen = jnp.sum(jnp.where(picked, router_logits[:, None, :], jnp.float32(0.0)), axis=2)
    exp_terms = jnp.exp(chosen)
    return (picked, exp_terms / jnp.sum(exp_terms, axis=1, keepdims=True))


def dispatch_block(tokens, cotangent, routes, router_weight, capacity):
    picked, probs = route_probs(tokens, routes, router_weight)
    slot_table, token_table = route_tables(routes, router_weight.shape[1], capacity)
    send_tokens = jnp.dot(token_table, tokens, preferred_element_type=jnp.float32).astype(
        jnp.bfloat16
    )
    send_cot = jnp.dot(token_table, cotangent, preferred_element_type=jnp.float32).astype(
        jnp.bfloat16
    )
    probs_low = probs.astype(jnp.bfloat16).reshape(-1)
    send_weight = jnp.dot(slot_table, probs_low, preferred_element_type=jnp.float32).astype(
        jnp.bfloat16
    )
    return (picked, probs, slot_table, token_table, send_tokens, send_cot, send_weight)


def slot_dot(cot_rows, out_rows):
    return jnp.sum(cot_rows.astype(jnp.float32) * out_rows.astype(jnp.float32), axis=1).astype(
        jnp.bfloat16
    )


def expert_backward(
    input_rows, cot_rows, weight_rows, gate_pre, up_pre, gate_matrix, up_matrix, down_matrix
):
    gate_value = gate_pre.astype(jnp.float32)
    up_value = up_pre.astype(jnp.float32)
    sigmoid_gate = jax.nn.sigmoid(gate_value)
    silu_gate = gate_value * sigmoid_gate
    hidden = (silu_gate * up_value).astype(jnp.bfloat16)
    expert_out = jnp.dot(hidden, down_matrix, preferred_element_type=jnp.float32).astype(
        jnp.bfloat16
    )
    scaled_cot = (weight_rows.astype(jnp.float32)[:, None] * cot_rows.astype(jnp.float32)).astype(
        jnp.bfloat16
    )
    grad_hidden = lax.dot_general(
        scaled_cot, down_matrix, contract_cols, preferred_element_type=jnp.float32
    )
    grad_gate_pre = (
        grad_hidden * up_value * sigmoid_gate * (1.0 + gate_value * (1.0 - sigmoid_gate))
    ).astype(jnp.bfloat16)
    grad_up_pre = (grad_hidden * silu_gate).astype(jnp.bfloat16)
    grad_rows = (
        lax.dot_general(
            grad_gate_pre, gate_matrix, contract_cols, preferred_element_type=jnp.float32
        )
        + lax.dot_general(grad_up_pre, up_matrix, contract_cols, preferred_element_type=jnp.float32)
    ).astype(jnp.bfloat16)
    grad_gate_w = lax.dot_general(
        input_rows, grad_gate_pre, contract_rows, preferred_element_type=jnp.float32
    ).astype(jnp.bfloat16)
    grad_up_w = lax.dot_general(
        input_rows, grad_up_pre, contract_rows, preferred_element_type=jnp.float32
    ).astype(jnp.bfloat16)
    grad_down_w = lax.dot_general(
        hidden, scaled_cot, contract_rows, preferred_element_type=jnp.float32
    ).astype(jnp.bfloat16)
    return (grad_rows, expert_out, grad_gate_w, grad_up_w, grad_down_w)


def finish_block(
    tokens, router_weight, picked, probs, slot_table, token_table, back_rows, route_dot
):
    grad_sum = lax.dot_general(
        token_table, back_rows, contract_rows, preferred_element_type=jnp.float32
    )
    route_grad = lax.dot_general(
        slot_table, route_dot, contract_rows, preferred_element_type=jnp.float32
    ).reshape(probs.shape)
    inner_term = jnp.sum(probs * route_grad, axis=1, keepdims=True)
    chosen_grad = probs * (route_grad - inner_term)
    logit_grad = jnp.sum(
        jnp.where(picked, chosen_grad[:, :, None], jnp.float32(0.0)), axis=1
    ).astype(jnp.bfloat16)
    grad_tokens = (
        grad_sum
        + lax.dot_general(
            logit_grad, router_weight, contract_cols, preferred_element_type=jnp.float32
        )
    ).astype(jnp.bfloat16)
    router_part = lax.dot_general(
        tokens, logit_grad, contract_rows, preferred_element_type=jnp.float32
    )
    return (grad_tokens, router_part)


def body(
    tokens,
    cotangent,
    routes,
    router_weight,
    gate_saved,
    up_saved,
    gate_weight,
    up_weight,
    down_weight,
):
    experts = router_weight.shape[1]
    width = tokens.shape[1]
    capacity = gate_saved.shape[1] // experts
    outer_size = lax.axis_size("outer")
    inner_size = lax.axis_size("inner")
    axes = ("outer", "inner")
    picked, probs = route_probs(tokens, routes, router_weight)
    slot_table, token_table = route_tables(routes, experts, capacity)
    both = jnp.concatenate([tokens, cotangent], axis=1)
    grid_both = jnp.dot(
        token_table.reshape(experts, capacity, -1), both, preferred_element_type=jnp.float32
    ).astype(jnp.bfloat16)
    probs_low = probs.astype(jnp.bfloat16).reshape(-1)
    send_weight = jnp.dot(slot_table, probs_low, preferred_element_type=jnp.float32).astype(
        jnp.bfloat16
    )
    grid_weight = send_weight.reshape(experts, capacity)
    got_both = lax.all_to_all(grid_both, axes, split_axis=0, concat_axis=0, tiled=True)
    got_weight = lax.all_to_all(grid_weight, axes, split_axis=0, concat_axis=0, tiled=True)
    got_both = got_both.reshape(-1, 2 * width)
    input_rows = got_both[:, :width]
    cot_rows = got_both[:, width:]
    grad_rows, expert_out, grad_gate_w, grad_up_w, grad_down_w = expert_backward(
        input_rows,
        cot_rows,
        got_weight.reshape(-1),
        gate_saved[0],
        up_saved[0],
        gate_weight[0],
        up_weight[0],
        down_weight[0],
    )
    slot_route_dot = slot_dot(cot_rows, expert_out).reshape(experts, capacity)
    back_dot = lax.all_to_all(slot_route_dot, axes, split_axis=0, concat_axis=0, tiled=True)
    route_dot = back_dot.reshape(-1)
    route_grad = lax.dot_general(
        slot_table, route_dot, contract_rows, preferred_element_type=jnp.float32
    ).reshape(probs.shape)
    inner_term = jnp.sum(probs * route_grad, axis=1, keepdims=True)
    chosen_grad = probs * (route_grad - inner_term)
    logit_grad = jnp.sum(
        jnp.where(picked, chosen_grad[:, :, None], jnp.float32(0.0)), axis=1
    ).astype(jnp.bfloat16)
    router_part = lax.dot_general(
        tokens, logit_grad, contract_rows, preferred_element_type=jnp.float32
    )
    total_tokens = tokens.shape[0] * outer_size * inner_size
    devices = outer_size * inner_size
    part_rows = router_part.reshape(devices, -1)
    got_parts = lax.all_to_all(part_rows, axes, split_axis=0, concat_axis=0, tiled=True)
    chunk_sum = jnp.sum(got_parts, axis=0, keepdims=True)
    spread = jnp.broadcast_to(chunk_sum, part_rows.shape)
    got_sums = lax.all_to_all(spread, axes, split_axis=0, concat_axis=0, tiled=True)
    grad_router = got_sums.reshape(router_part.shape) * (1.0 / math.sqrt(total_tokens))
    back_grad = grad_rows.reshape(experts, capacity, width)
    grad_router, back_grad = lax.optimization_barrier((grad_router, back_grad))
    back_rows = lax.all_to_all(back_grad, axes, split_axis=0, concat_axis=0, tiled=True)
    grad_sum = lax.dot_general(
        token_table, back_rows.reshape(-1, width), contract_rows, preferred_element_type=jnp.float32
    )
    grad_tokens = (
        grad_sum
        + lax.dot_general(
            logit_grad, router_weight, contract_cols, preferred_element_type=jnp.float32
        )
    ).astype(jnp.bfloat16)
    return (grad_tokens, grad_gate_w[None], grad_up_w[None], grad_down_w[None], grad_router)


def solution(mesh):
    in_specs = (
        P(("outer", "inner"), None),
        P(("outer", "inner"), None),
        P(("outer", "inner"), None),
        P(),
        P(("outer", "inner"), None, None),
        P(("outer", "inner"), None, None),
        P(("outer", "inner"), None, None),
        P(("outer", "inner"), None, None),
        P(("outer", "inner"), None, None),
    )
    out_specs = (
        P(("outer", "inner"), None),
        P(("outer", "inner"), None, None),
        P(("outer", "inner"), None, None),
        P(("outer", "inner"), None, None),
        P(),
    )
    return jax.shard_map(body, mesh=mesh, in_specs=in_specs, out_specs=out_specs, check_vma=False)
```

```python
import math

import jax
import jax.numpy as jnp
from jax import lax
from jax.sharding import PartitionSpec as P

contract_rows = (((0,), (0,)), ((), ()))
contract_cols = (((1,), (1,)), ((), ()))


def route_tables(routes, experts, capacity):
    flat_routes = routes.reshape(-1)
    onehot = (flat_routes[:, None] == jnp.arange(experts, dtype=jnp.int32)[None, :]).astype(
        jnp.int32
    )
    pairs = flat_routes.shape[0]
    lower = (
        jnp.arange(pairs, dtype=jnp.int32)[:, None] > jnp.arange(pairs, dtype=jnp.int32)[None, :]
    ).astype(jnp.bfloat16)
    earlier = jnp.dot(
        lower, onehot.astype(jnp.bfloat16), preferred_element_type=jnp.float32
    ).astype(jnp.int32)
    position = jnp.sum(earlier * onehot, axis=1)
    target = flat_routes * capacity + position
    slot_table = (
        jnp.arange(experts * capacity, dtype=jnp.int32)[:, None] == target[None, :]
    ).astype(jnp.bfloat16)
    token_table = jnp.sum(
        slot_table.reshape(experts * capacity, routes.shape[0], routes.shape[1]), axis=2
    )
    return (slot_table, token_table)


def route_probs(tokens, routes, router_weight):
    router_logits = jnp.dot(tokens, router_weight, preferred_element_type=jnp.float32)
    picked = (
        routes[:, :, None] == jnp.arange(router_weight.shape[1], dtype=jnp.int32)[None, None, :]
    )
    chosen = jnp.sum(jnp.where(picked, router_logits[:, None, :], jnp.float32(0.0)), axis=2)
    exp_terms = jnp.exp(chosen)
    return (picked, exp_terms / jnp.sum(exp_terms, axis=1, keepdims=True))


def dispatch_block(tokens, cotangent, routes, router_weight, capacity):
    picked, probs = route_probs(tokens, routes, router_weight)
    slot_table, token_table = route_tables(routes, router_weight.shape[1], capacity)
    send_tokens = jnp.dot(token_table, tokens, preferred_element_type=jnp.float32).astype(
        jnp.bfloat16
    )
    send_cot = jnp.dot(token_table, cotangent, preferred_element_type=jnp.float32).astype(
        jnp.bfloat16
    )
    probs_low = probs.astype(jnp.bfloat16).reshape(-1)
    send_weight = jnp.dot(slot_table, probs_low, preferred_element_type=jnp.float32).astype(
        jnp.bfloat16
    )
    return (picked, probs, slot_table, token_table, send_tokens, send_cot, send_weight)


def slot_dot(cot_rows, out_rows):
    return jnp.sum(cot_rows.astype(jnp.float32) * out_rows.astype(jnp.float32), axis=1).astype(
        jnp.bfloat16
    )


def expert_backward(
    input_rows, cot_rows, weight_rows, gate_pre, up_pre, gate_matrix, up_matrix, down_matrix
):
    gate_value = gate_pre.astype(jnp.float32)
    up_value = up_pre.astype(jnp.float32)
    sigmoid_gate = jax.nn.sigmoid(gate_value)
    silu_gate = gate_value * sigmoid_gate
    hidden = (silu_gate * up_value).astype(jnp.bfloat16)
    expert_out = jnp.dot(hidden, down_matrix, preferred_element_type=jnp.float32).astype(
        jnp.bfloat16
    )
    scaled_cot = (weight_rows.astype(jnp.float32)[:, None] * cot_rows.astype(jnp.float32)).astype(
        jnp.bfloat16
    )
    grad_hidden = lax.dot_general(
        scaled_cot, down_matrix, contract_cols, preferred_element_type=jnp.float32
    )
    grad_gate_pre = (
        grad_hidden * up_value * sigmoid_gate * (1.0 + gate_value * (1.0 - sigmoid_gate))
    ).astype(jnp.bfloat16)
    grad_up_pre = (grad_hidden * silu_gate).astype(jnp.bfloat16)
    grad_rows = (
        lax.dot_general(
            grad_gate_pre, gate_matrix, contract_cols, preferred_element_type=jnp.float32
        )
        + lax.dot_general(grad_up_pre, up_matrix, contract_cols, preferred_element_type=jnp.float32)
    ).astype(jnp.bfloat16)
    grad_gate_w = lax.dot_general(
        input_rows, grad_gate_pre, contract_rows, preferred_element_type=jnp.float32
    ).astype(jnp.bfloat16)
    grad_up_w = lax.dot_general(
        input_rows, grad_up_pre, contract_rows, preferred_element_type=jnp.float32
    ).astype(jnp.bfloat16)
    grad_down_w = lax.dot_general(
        hidden, scaled_cot, contract_rows, preferred_element_type=jnp.float32
    ).astype(jnp.bfloat16)
    return (grad_rows, expert_out, grad_gate_w, grad_up_w, grad_down_w)


def finish_block(
    tokens, router_weight, picked, probs, slot_table, token_table, back_rows, route_dot
):
    grad_sum = lax.dot_general(
        token_table, back_rows, contract_rows, preferred_element_type=jnp.float32
    )
    route_grad = lax.dot_general(
        slot_table, route_dot, contract_rows, preferred_element_type=jnp.float32
    ).reshape(probs.shape)
    inner_term = jnp.sum(probs * route_grad, axis=1, keepdims=True)
    chosen_grad = probs * (route_grad - inner_term)
    logit_grad = jnp.sum(
        jnp.where(picked, chosen_grad[:, :, None], jnp.float32(0.0)), axis=1
    ).astype(jnp.bfloat16)
    grad_tokens = (
        grad_sum
        + lax.dot_general(
            logit_grad, router_weight, contract_cols, preferred_element_type=jnp.float32
        )
    ).astype(jnp.bfloat16)
    router_part = lax.dot_general(
        tokens, logit_grad, contract_rows, preferred_element_type=jnp.float32
    )
    return (grad_tokens, router_part)


def expert_from_cot(cot_rows, weight_rows, gate_pre, up_pre, gate_matrix, up_matrix, down_matrix):
    gate_value = gate_pre.astype(jnp.float32)
    up_value = up_pre.astype(jnp.float32)
    sigmoid_gate = jax.nn.sigmoid(gate_value)
    silu_gate = gate_value * sigmoid_gate
    hidden = (silu_gate * up_value).astype(jnp.bfloat16)
    expert_out = jnp.dot(hidden, down_matrix, preferred_element_type=jnp.float32).astype(
        jnp.bfloat16
    )
    scaled_cot = (weight_rows.astype(jnp.float32)[:, None] * cot_rows.astype(jnp.float32)).astype(
        jnp.bfloat16
    )
    grad_hidden = lax.dot_general(
        scaled_cot, down_matrix, contract_cols, preferred_element_type=jnp.float32
    )
    grad_gate_pre = (
        grad_hidden * up_value * sigmoid_gate * (1.0 + gate_value * (1.0 - sigmoid_gate))
    ).astype(jnp.bfloat16)
    grad_up_pre = (grad_hidden * silu_gate).astype(jnp.bfloat16)
    grad_rows = (
        lax.dot_general(
            grad_gate_pre, gate_matrix, contract_cols, preferred_element_type=jnp.float32
        )
        + lax.dot_general(grad_up_pre, up_matrix, contract_cols, preferred_element_type=jnp.float32)
    ).astype(jnp.bfloat16)
    grad_down_w = lax.dot_general(
        hidden, scaled_cot, contract_rows, preferred_element_type=jnp.float32
    ).astype(jnp.bfloat16)
    return (grad_rows, expert_out, grad_gate_pre, grad_up_pre, grad_down_w)


def body(
    tokens,
    cotangent,
    routes,
    router_weight,
    gate_saved,
    up_saved,
    gate_weight,
    up_weight,
    down_weight,
):
    experts = router_weight.shape[1]
    width = tokens.shape[1]
    capacity = gate_saved.shape[1] // experts
    outer_size = lax.axis_size("outer")
    inner_size = lax.axis_size("inner")
    axes = ("outer", "inner")
    picked, probs = route_probs(tokens, routes, router_weight)
    slot_table, token_table = route_tables(routes, experts, capacity)
    grid_table = token_table.reshape(experts, capacity, -1)
    probs_low = probs.astype(jnp.bfloat16).reshape(-1)
    send_weight = jnp.dot(slot_table, probs_low, preferred_element_type=jnp.float32).astype(
        jnp.bfloat16
    )
    got_weight = lax.all_to_all(
        send_weight.reshape(experts, capacity), axes, split_axis=0, concat_axis=0, tiled=True
    )
    grid_cot = jnp.dot(grid_table, cotangent, preferred_element_type=jnp.float32).astype(
        jnp.bfloat16
    )
    got_cot = lax.all_to_all(grid_cot, axes, split_axis=0, concat_axis=0, tiled=True)
    grid_tokens = jnp.dot(grid_table, tokens, preferred_element_type=jnp.float32).astype(
        jnp.bfloat16
    )
    got_cot, grid_tokens = lax.optimization_barrier((got_cot, grid_tokens))
    got_tokens = lax.all_to_all(grid_tokens, axes, split_axis=0, concat_axis=0, tiled=True)
    cot_rows = got_cot.reshape(-1, width)
    grad_rows, expert_out, grad_gate_pre, grad_up_pre, grad_down_w = expert_from_cot(
        cot_rows,
        got_weight.reshape(-1),
        gate_saved[0],
        up_saved[0],
        gate_weight[0],
        up_weight[0],
        down_weight[0],
    )
    slot_route_dot = slot_dot(cot_rows, expert_out).reshape(experts, capacity)
    back_dot = lax.all_to_all(slot_route_dot, axes, split_axis=0, concat_axis=0, tiled=True)
    route_dot = back_dot.reshape(-1)
    route_grad = lax.dot_general(
        slot_table, route_dot, contract_rows, preferred_element_type=jnp.float32
    ).reshape(probs.shape)
    inner_term = jnp.sum(probs * route_grad, axis=1, keepdims=True)
    chosen_grad = probs * (route_grad - inner_term)
    logit_grad = jnp.sum(
        jnp.where(picked, chosen_grad[:, :, None], jnp.float32(0.0)), axis=1
    ).astype(jnp.bfloat16)
    router_part = lax.dot_general(
        tokens, logit_grad, contract_rows, preferred_element_type=jnp.float32
    )
    total_tokens = tokens.shape[0] * outer_size * inner_size
    devices = outer_size * inner_size
    part_rows = router_part.reshape(devices, -1)
    got_parts = lax.all_to_all(part_rows, axes, split_axis=0, concat_axis=0, tiled=True)
    chunk_sum = jnp.sum(got_parts, axis=0, keepdims=True)
    spread = jnp.broadcast_to(chunk_sum, part_rows.shape)
    got_sums = lax.all_to_all(spread, axes, split_axis=0, concat_axis=0, tiled=True)
    grad_router = got_sums.reshape(router_part.shape) * (1.0 / math.sqrt(total_tokens))
    back_grad = grad_rows.reshape(experts, capacity, width)
    back_grad, got_tokens = lax.optimization_barrier((back_grad, got_tokens))
    back_rows = lax.all_to_all(back_grad, axes, split_axis=0, concat_axis=0, tiled=True)
    input_rows = got_tokens.reshape(-1, width)
    grad_gate_w = lax.dot_general(
        input_rows, grad_gate_pre, contract_rows, preferred_element_type=jnp.float32
    ).astype(jnp.bfloat16)
    grad_up_w = lax.dot_general(
        input_rows, grad_up_pre, contract_rows, preferred_element_type=jnp.float32
    ).astype(jnp.bfloat16)
    grad_sum = lax.dot_general(
        grid_table, back_rows, (((0, 1), (0, 1)), ((), ())), preferred_element_type=jnp.float32
    )
    grad_tokens = (
        grad_sum
        + lax.dot_general(
            logit_grad, router_weight, contract_cols, preferred_element_type=jnp.float32
        )
    ).astype(jnp.bfloat16)
    return (grad_tokens, grad_gate_w[None], grad_up_w[None], grad_down_w[None], grad_router)


def solution(mesh):
    in_specs = (
        P(("outer", "inner"), None),
        P(("outer", "inner"), None),
        P(("outer", "inner"), None),
        P(),
        P(("outer", "inner"), None, None),
        P(("outer", "inner"), None, None),
        P(("outer", "inner"), None, None),
        P(("outer", "inner"), None, None),
        P(("outer", "inner"), None, None),
    )
    out_specs = (
        P(("outer", "inner"), None),
        P(("outer", "inner"), None, None),
        P(("outer", "inner"), None, None),
        P(("outer", "inner"), None, None),
        P(),
    )
    return jax.shard_map(body, mesh=mesh, in_specs=in_specs, out_specs=out_specs, check_vma=False)
```

```python
import math

import jax
import jax.numpy as jnp
from jax import lax
from jax.sharding import PartitionSpec as P

contract_rows = (((0,), (0,)), ((), ()))
contract_cols = (((1,), (1,)), ((), ()))


def route_tables(routes, experts, capacity):
    flat_routes = routes.reshape(-1)
    onehot = (flat_routes[:, None] == jnp.arange(experts, dtype=jnp.int32)[None, :]).astype(
        jnp.int32
    )
    pairs = flat_routes.shape[0]
    lower = (
        jnp.arange(pairs, dtype=jnp.int32)[:, None] > jnp.arange(pairs, dtype=jnp.int32)[None, :]
    ).astype(jnp.bfloat16)
    earlier = jnp.dot(
        lower, onehot.astype(jnp.bfloat16), preferred_element_type=jnp.float32
    ).astype(jnp.int32)
    position = jnp.sum(earlier * onehot, axis=1)
    target = flat_routes * capacity + position
    slot_table = (
        jnp.arange(experts * capacity, dtype=jnp.int32)[:, None] == target[None, :]
    ).astype(jnp.bfloat16)
    token_table = jnp.sum(
        slot_table.reshape(experts * capacity, routes.shape[0], routes.shape[1]), axis=2
    )
    return (slot_table, token_table)


def route_probs(tokens, routes, router_weight):
    router_logits = jnp.dot(tokens, router_weight, preferred_element_type=jnp.float32)
    picked = (
        routes[:, :, None] == jnp.arange(router_weight.shape[1], dtype=jnp.int32)[None, None, :]
    )
    chosen = jnp.sum(jnp.where(picked, router_logits[:, None, :], jnp.float32(0.0)), axis=2)
    exp_terms = jnp.exp(chosen)
    return (picked, exp_terms / jnp.sum(exp_terms, axis=1, keepdims=True))


def dispatch_block(tokens, cotangent, routes, router_weight, capacity):
    picked, probs = route_probs(tokens, routes, router_weight)
    slot_table, token_table = route_tables(routes, router_weight.shape[1], capacity)
    send_tokens = jnp.dot(token_table, tokens, preferred_element_type=jnp.float32).astype(
        jnp.bfloat16
    )
    send_cot = jnp.dot(token_table, cotangent, preferred_element_type=jnp.float32).astype(
        jnp.bfloat16
    )
    probs_low = probs.astype(jnp.bfloat16).reshape(-1)
    send_weight = jnp.dot(slot_table, probs_low, preferred_element_type=jnp.float32).astype(
        jnp.bfloat16
    )
    return (picked, probs, slot_table, token_table, send_tokens, send_cot, send_weight)


def slot_dot(cot_rows, out_rows):
    return jnp.sum(cot_rows.astype(jnp.float32) * out_rows.astype(jnp.float32), axis=1).astype(
        jnp.bfloat16
    )


def expert_backward(
    input_rows, cot_rows, weight_rows, gate_pre, up_pre, gate_matrix, up_matrix, down_matrix
):
    gate_value = gate_pre.astype(jnp.float32)
    up_value = up_pre.astype(jnp.float32)
    sigmoid_gate = jax.nn.sigmoid(gate_value)
    silu_gate = gate_value * sigmoid_gate
    hidden = (silu_gate * up_value).astype(jnp.bfloat16)
    expert_out = jnp.dot(hidden, down_matrix, preferred_element_type=jnp.float32).astype(
        jnp.bfloat16
    )
    scaled_cot = (weight_rows.astype(jnp.float32)[:, None] * cot_rows.astype(jnp.float32)).astype(
        jnp.bfloat16
    )
    grad_hidden = lax.dot_general(
        scaled_cot, down_matrix, contract_cols, preferred_element_type=jnp.float32
    )
    grad_gate_pre = (
        grad_hidden * up_value * sigmoid_gate * (1.0 + gate_value * (1.0 - sigmoid_gate))
    ).astype(jnp.bfloat16)
    grad_up_pre = (grad_hidden * silu_gate).astype(jnp.bfloat16)
    grad_rows = (
        lax.dot_general(
            grad_gate_pre, gate_matrix, contract_cols, preferred_element_type=jnp.float32
        )
        + lax.dot_general(grad_up_pre, up_matrix, contract_cols, preferred_element_type=jnp.float32)
    ).astype(jnp.bfloat16)
    grad_gate_w = lax.dot_general(
        input_rows, grad_gate_pre, contract_rows, preferred_element_type=jnp.float32
    ).astype(jnp.bfloat16)
    grad_up_w = lax.dot_general(
        input_rows, grad_up_pre, contract_rows, preferred_element_type=jnp.float32
    ).astype(jnp.bfloat16)
    grad_down_w = lax.dot_general(
        hidden, scaled_cot, contract_rows, preferred_element_type=jnp.float32
    ).astype(jnp.bfloat16)
    return (grad_rows, expert_out, grad_gate_w, grad_up_w, grad_down_w)


def finish_block(
    tokens, router_weight, picked, probs, slot_table, token_table, back_rows, route_dot
):
    grad_sum = lax.dot_general(
        token_table, back_rows, contract_rows, preferred_element_type=jnp.float32
    )
    route_grad = lax.dot_general(
        slot_table, route_dot, contract_rows, preferred_element_type=jnp.float32
    ).reshape(probs.shape)
    inner_term = jnp.sum(probs * route_grad, axis=1, keepdims=True)
    chosen_grad = probs * (route_grad - inner_term)
    logit_grad = jnp.sum(
        jnp.where(picked, chosen_grad[:, :, None], jnp.float32(0.0)), axis=1
    ).astype(jnp.bfloat16)
    grad_tokens = (
        grad_sum
        + lax.dot_general(
            logit_grad, router_weight, contract_cols, preferred_element_type=jnp.float32
        )
    ).astype(jnp.bfloat16)
    router_part = lax.dot_general(
        tokens, logit_grad, contract_rows, preferred_element_type=jnp.float32
    )
    return (grad_tokens, router_part)


def expert_from_cot(cot_rows, weight_rows, gate_pre, up_pre, gate_matrix, up_matrix, down_matrix):
    gate_value = gate_pre.astype(jnp.float32)
    up_value = up_pre.astype(jnp.float32)
    sigmoid_gate = jax.nn.sigmoid(gate_value)
    silu_gate = gate_value * sigmoid_gate
    hidden = (silu_gate * up_value).astype(jnp.bfloat16)
    expert_out = jnp.dot(hidden, down_matrix, preferred_element_type=jnp.float32).astype(
        jnp.bfloat16
    )
    scaled_cot = (weight_rows.astype(jnp.float32)[:, None] * cot_rows.astype(jnp.float32)).astype(
        jnp.bfloat16
    )
    grad_hidden = lax.dot_general(
        scaled_cot, down_matrix, contract_cols, preferred_element_type=jnp.float32
    )
    grad_gate_pre = (
        grad_hidden * up_value * sigmoid_gate * (1.0 + gate_value * (1.0 - sigmoid_gate))
    ).astype(jnp.bfloat16)
    grad_up_pre = (grad_hidden * silu_gate).astype(jnp.bfloat16)
    grad_rows = (
        lax.dot_general(
            grad_gate_pre, gate_matrix, contract_cols, preferred_element_type=jnp.float32
        )
        + lax.dot_general(grad_up_pre, up_matrix, contract_cols, preferred_element_type=jnp.float32)
    ).astype(jnp.bfloat16)
    grad_down_w = lax.dot_general(
        hidden, scaled_cot, contract_rows, preferred_element_type=jnp.float32
    ).astype(jnp.bfloat16)
    return (grad_rows, expert_out, grad_gate_pre, grad_up_pre, grad_down_w)


def body(
    tokens,
    cotangent,
    routes,
    router_weight,
    gate_saved,
    up_saved,
    gate_weight,
    up_weight,
    down_weight,
):
    experts = router_weight.shape[1]
    width = tokens.shape[1]
    capacity = gate_saved.shape[1] // experts
    outer_size = lax.axis_size("outer")
    inner_size = lax.axis_size("inner")
    axes = ("outer", "inner")
    picked, probs = route_probs(tokens, routes, router_weight)
    slot_table, token_table = route_tables(routes, experts, capacity)
    grid_table = token_table.reshape(experts, capacity, -1)
    probs_low = probs.astype(jnp.bfloat16).reshape(-1)
    send_weight = jnp.dot(slot_table, probs_low, preferred_element_type=jnp.float32).astype(
        jnp.bfloat16
    )
    got_weight = lax.all_to_all(
        send_weight.reshape(experts, capacity), axes, split_axis=0, concat_axis=0, tiled=True
    )
    grid_cot = jnp.dot(grid_table, cotangent, preferred_element_type=jnp.float32).astype(
        jnp.bfloat16
    )
    got_weight, grid_cot = lax.optimization_barrier((got_weight, grid_cot))
    got_cot = lax.all_to_all(grid_cot, axes, split_axis=0, concat_axis=0, tiled=True)
    grid_tokens = jnp.dot(grid_table, tokens, preferred_element_type=jnp.float32).astype(
        jnp.bfloat16
    )
    got_cot, grid_tokens = lax.optimization_barrier((got_cot, grid_tokens))
    got_tokens = lax.all_to_all(grid_tokens, axes, split_axis=0, concat_axis=0, tiled=True)
    cot_rows = got_cot.reshape(-1, width)
    grad_rows, expert_out, grad_gate_pre, grad_up_pre, grad_down_w = expert_from_cot(
        cot_rows,
        got_weight.reshape(-1),
        gate_saved[0],
        up_saved[0],
        gate_weight[0],
        up_weight[0],
        down_weight[0],
    )
    slot_route_dot = slot_dot(cot_rows, expert_out).reshape(experts, capacity)
    slot_route_dot, got_tokens = lax.optimization_barrier((slot_route_dot, got_tokens))
    back_dot = lax.all_to_all(slot_route_dot, axes, split_axis=0, concat_axis=0, tiled=True)
    route_dot = back_dot.reshape(-1)
    route_grad = lax.dot_general(
        slot_table, route_dot, contract_rows, preferred_element_type=jnp.float32
    ).reshape(probs.shape)
    inner_term = jnp.sum(probs * route_grad, axis=1, keepdims=True)
    chosen_grad = probs * (route_grad - inner_term)
    logit_grad = jnp.sum(
        jnp.where(picked, chosen_grad[:, :, None], jnp.float32(0.0)), axis=1
    ).astype(jnp.bfloat16)
    router_part = lax.dot_general(
        tokens, logit_grad, contract_rows, preferred_element_type=jnp.float32
    )
    total_tokens = tokens.shape[0] * outer_size * inner_size
    devices = outer_size * inner_size
    part_rows = router_part.reshape(devices, -1)
    got_parts = lax.all_to_all(part_rows, axes, split_axis=0, concat_axis=0, tiled=True)
    chunk_sum = jnp.sum(got_parts, axis=0, keepdims=True)
    spread = jnp.broadcast_to(chunk_sum, part_rows.shape)
    got_sums = lax.all_to_all(spread, axes, split_axis=0, concat_axis=0, tiled=True)
    grad_router = got_sums.reshape(router_part.shape) * (1.0 / math.sqrt(total_tokens))
    back_grad = grad_rows.reshape(experts, capacity, width)
    back_grad, grad_router = lax.optimization_barrier((back_grad, grad_router))
    back_rows = lax.all_to_all(back_grad, axes, split_axis=0, concat_axis=0, tiled=True)
    input_rows = got_tokens.reshape(-1, width)
    grad_gate_w = lax.dot_general(
        input_rows, grad_gate_pre, contract_rows, preferred_element_type=jnp.float32
    ).astype(jnp.bfloat16)
    grad_up_w = lax.dot_general(
        input_rows, grad_up_pre, contract_rows, preferred_element_type=jnp.float32
    ).astype(jnp.bfloat16)
    grad_sum = lax.dot_general(
        grid_table, back_rows, (((0, 1), (0, 1)), ((), ())), preferred_element_type=jnp.float32
    )
    grad_tokens = (
        grad_sum
        + lax.dot_general(
            logit_grad, router_weight, contract_cols, preferred_element_type=jnp.float32
        )
    ).astype(jnp.bfloat16)
    return (grad_tokens, grad_gate_w[None], grad_up_w[None], grad_down_w[None], grad_router)


def solution(mesh):
    in_specs = (
        P(("outer", "inner"), None),
        P(("outer", "inner"), None),
        P(("outer", "inner"), None),
        P(),
        P(("outer", "inner"), None, None),
        P(("outer", "inner"), None, None),
        P(("outer", "inner"), None, None),
        P(("outer", "inner"), None, None),
        P(("outer", "inner"), None, None),
    )
    out_specs = (
        P(("outer", "inner"), None),
        P(("outer", "inner"), None, None),
        P(("outer", "inner"), None, None),
        P(("outer", "inner"), None, None),
        P(),
    )
    return jax.shard_map(body, mesh=mesh, in_specs=in_specs, out_specs=out_specs, check_vma=False)
```

```python
import math

import jax
import jax.numpy as jnp
from jax import lax
from jax.sharding import PartitionSpec as P

contract_rows = (((0,), (0,)), ((), ()))
contract_cols = (((1,), (1,)), ((), ()))


def route_tables(routes, experts, capacity):
    flat_routes = routes.reshape(-1)
    onehot = (flat_routes[:, None] == jnp.arange(experts, dtype=jnp.int32)[None, :]).astype(
        jnp.int32
    )
    pairs = flat_routes.shape[0]
    lower = (
        jnp.arange(pairs, dtype=jnp.int32)[:, None] > jnp.arange(pairs, dtype=jnp.int32)[None, :]
    ).astype(jnp.bfloat16)
    earlier = jnp.dot(
        lower, onehot.astype(jnp.bfloat16), preferred_element_type=jnp.float32
    ).astype(jnp.int32)
    position = jnp.sum(earlier * onehot, axis=1)
    target = flat_routes * capacity + position
    slot_table = (
        jnp.arange(experts * capacity, dtype=jnp.int32)[:, None] == target[None, :]
    ).astype(jnp.bfloat16)
    token_table = jnp.sum(
        slot_table.reshape(experts * capacity, routes.shape[0], routes.shape[1]), axis=2
    )
    return (slot_table, token_table)


def route_probs(tokens, routes, router_weight):
    router_logits = jnp.dot(tokens, router_weight, preferred_element_type=jnp.float32)
    picked = (
        routes[:, :, None] == jnp.arange(router_weight.shape[1], dtype=jnp.int32)[None, None, :]
    )
    chosen = jnp.sum(jnp.where(picked, router_logits[:, None, :], jnp.float32(0.0)), axis=2)
    exp_terms = jnp.exp(chosen)
    return (picked, exp_terms / jnp.sum(exp_terms, axis=1, keepdims=True))


def dispatch_block(tokens, cotangent, routes, router_weight, capacity):
    picked, probs = route_probs(tokens, routes, router_weight)
    slot_table, token_table = route_tables(routes, router_weight.shape[1], capacity)
    send_tokens = jnp.dot(token_table, tokens, preferred_element_type=jnp.float32).astype(
        jnp.bfloat16
    )
    send_cot = jnp.dot(token_table, cotangent, preferred_element_type=jnp.float32).astype(
        jnp.bfloat16
    )
    probs_low = probs.astype(jnp.bfloat16).reshape(-1)
    send_weight = jnp.dot(slot_table, probs_low, preferred_element_type=jnp.float32).astype(
        jnp.bfloat16
    )
    return (picked, probs, slot_table, token_table, send_tokens, send_cot, send_weight)


def slot_dot(cot_rows, out_rows):
    return jnp.sum(cot_rows.astype(jnp.float32) * out_rows.astype(jnp.float32), axis=1).astype(
        jnp.bfloat16
    )


def expert_backward(
    input_rows, cot_rows, weight_rows, gate_pre, up_pre, gate_matrix, up_matrix, down_matrix
):
    gate_value = gate_pre.astype(jnp.float32)
    up_value = up_pre.astype(jnp.float32)
    sigmoid_gate = jax.nn.sigmoid(gate_value)
    silu_gate = gate_value * sigmoid_gate
    hidden = (silu_gate * up_value).astype(jnp.bfloat16)
    expert_out = jnp.dot(hidden, down_matrix, preferred_element_type=jnp.float32).astype(
        jnp.bfloat16
    )
    scaled_cot = (weight_rows.astype(jnp.float32)[:, None] * cot_rows.astype(jnp.float32)).astype(
        jnp.bfloat16
    )
    grad_hidden = lax.dot_general(
        scaled_cot, down_matrix, contract_cols, preferred_element_type=jnp.float32
    )
    grad_gate_pre = (
        grad_hidden * up_value * sigmoid_gate * (1.0 + gate_value * (1.0 - sigmoid_gate))
    ).astype(jnp.bfloat16)
    grad_up_pre = (grad_hidden * silu_gate).astype(jnp.bfloat16)
    grad_rows = (
        lax.dot_general(
            grad_gate_pre, gate_matrix, contract_cols, preferred_element_type=jnp.float32
        )
        + lax.dot_general(grad_up_pre, up_matrix, contract_cols, preferred_element_type=jnp.float32)
    ).astype(jnp.bfloat16)
    grad_gate_w = lax.dot_general(
        input_rows, grad_gate_pre, contract_rows, preferred_element_type=jnp.float32
    ).astype(jnp.bfloat16)
    grad_up_w = lax.dot_general(
        input_rows, grad_up_pre, contract_rows, preferred_element_type=jnp.float32
    ).astype(jnp.bfloat16)
    grad_down_w = lax.dot_general(
        hidden, scaled_cot, contract_rows, preferred_element_type=jnp.float32
    ).astype(jnp.bfloat16)
    return (grad_rows, expert_out, grad_gate_w, grad_up_w, grad_down_w)


def finish_block(
    tokens, router_weight, picked, probs, slot_table, token_table, back_rows, route_dot
):
    grad_sum = lax.dot_general(
        token_table, back_rows, contract_rows, preferred_element_type=jnp.float32
    )
    route_grad = lax.dot_general(
        slot_table, route_dot, contract_rows, preferred_element_type=jnp.float32
    ).reshape(probs.shape)
    inner_term = jnp.sum(probs * route_grad, axis=1, keepdims=True)
    chosen_grad = probs * (route_grad - inner_term)
    logit_grad = jnp.sum(
        jnp.where(picked, chosen_grad[:, :, None], jnp.float32(0.0)), axis=1
    ).astype(jnp.bfloat16)
    grad_tokens = (
        grad_sum
        + lax.dot_general(
            logit_grad, router_weight, contract_cols, preferred_element_type=jnp.float32
        )
    ).astype(jnp.bfloat16)
    router_part = lax.dot_general(
        tokens, logit_grad, contract_rows, preferred_element_type=jnp.float32
    )
    return (grad_tokens, router_part)


def expert_from_cot(cot_rows, weight_rows, gate_pre, up_pre, gate_matrix, up_matrix, down_matrix):
    last = (((2,), (0,)), ((), ()))
    last_t = (((2,), (1,)), ((), ()))
    grid_rows = (((0, 1), (0, 1)), ((), ()))
    gate_value = gate_pre.astype(jnp.float32)
    up_value = up_pre.astype(jnp.float32)
    sigmoid_gate = jax.nn.sigmoid(gate_value)
    silu_gate = gate_value * sigmoid_gate
    hidden = (silu_gate * up_value).astype(jnp.bfloat16)
    expert_out = lax.dot_general(
        hidden, down_matrix, last, preferred_element_type=jnp.float32
    ).astype(jnp.bfloat16)
    scaled_cot = (
        weight_rows.astype(jnp.float32)[:, :, None] * cot_rows.astype(jnp.float32)
    ).astype(jnp.bfloat16)
    grad_hidden = lax.dot_general(
        scaled_cot, down_matrix, last_t, preferred_element_type=jnp.float32
    )
    grad_gate_pre = (
        grad_hidden * up_value * sigmoid_gate * (1.0 + gate_value * (1.0 - sigmoid_gate))
    ).astype(jnp.bfloat16)
    grad_up_pre = (grad_hidden * silu_gate).astype(jnp.bfloat16)
    grad_rows = (
        lax.dot_general(grad_gate_pre, gate_matrix, last_t, preferred_element_type=jnp.float32)
        + lax.dot_general(grad_up_pre, up_matrix, last_t, preferred_element_type=jnp.float32)
    ).astype(jnp.bfloat16)
    grad_down_w = lax.dot_general(
        hidden, scaled_cot, grid_rows, preferred_element_type=jnp.float32
    ).astype(jnp.bfloat16)
    return (grad_rows, expert_out, grad_gate_pre, grad_up_pre, grad_down_w)


def body(
    tokens,
    cotangent,
    routes,
    router_weight,
    gate_saved,
    up_saved,
    gate_weight,
    up_weight,
    down_weight,
):
    experts = router_weight.shape[1]
    width = tokens.shape[1]
    capacity = gate_saved.shape[1] // experts
    outer_size = lax.axis_size("outer")
    inner_size = lax.axis_size("inner")
    axes = ("outer", "inner")
    picked, probs = route_probs(tokens, routes, router_weight)
    slot_table, token_table = route_tables(routes, experts, capacity)
    grid_table = token_table.reshape(experts, capacity, -1)
    probs_low = probs.astype(jnp.bfloat16).reshape(-1)
    send_weight = jnp.dot(slot_table, probs_low, preferred_element_type=jnp.float32).astype(
        jnp.bfloat16
    )
    got_weight = lax.all_to_all(
        send_weight.reshape(experts, capacity), axes, split_axis=0, concat_axis=0, tiled=True
    )
    grid_cot = jnp.dot(grid_table, cotangent, preferred_element_type=jnp.float32).astype(
        jnp.bfloat16
    )
    got_weight, grid_cot = lax.optimization_barrier((got_weight, grid_cot))
    got_cot = lax.all_to_all(grid_cot, axes, split_axis=0, concat_axis=0, tiled=True)
    grid_tokens = jnp.dot(grid_table, tokens, preferred_element_type=jnp.float32).astype(
        jnp.bfloat16
    )
    got_cot, grid_tokens = lax.optimization_barrier((got_cot, grid_tokens))
    got_tokens = lax.all_to_all(grid_tokens, axes, split_axis=0, concat_axis=0, tiled=True)
    cot_rows = got_cot
    grad_rows, expert_out, grad_gate_pre, grad_up_pre, grad_down_w = expert_from_cot(
        cot_rows,
        got_weight,
        gate_saved[0].reshape(experts, capacity, -1),
        up_saved[0].reshape(experts, capacity, -1),
        gate_weight[0],
        up_weight[0],
        down_weight[0],
    )
    slot_route_dot = jnp.sum(
        cot_rows.astype(jnp.float32) * expert_out.astype(jnp.float32), axis=2
    ).astype(jnp.bfloat16)
    slot_route_dot, got_tokens = lax.optimization_barrier((slot_route_dot, got_tokens))
    back_dot = lax.all_to_all(slot_route_dot, axes, split_axis=0, concat_axis=0, tiled=True)
    route_dot = back_dot.reshape(-1)
    route_grad = lax.dot_general(
        slot_table, route_dot, contract_rows, preferred_element_type=jnp.float32
    ).reshape(probs.shape)
    inner_term = jnp.sum(probs * route_grad, axis=1, keepdims=True)
    chosen_grad = probs * (route_grad - inner_term)
    logit_grad = jnp.sum(
        jnp.where(picked, chosen_grad[:, :, None], jnp.float32(0.0)), axis=1
    ).astype(jnp.bfloat16)
    router_part = lax.dot_general(
        tokens, logit_grad, contract_rows, preferred_element_type=jnp.float32
    )
    total_tokens = tokens.shape[0] * outer_size * inner_size
    devices = outer_size * inner_size
    part_rows = router_part.reshape(devices, -1)
    got_parts = lax.all_to_all(part_rows, axes, split_axis=0, concat_axis=0, tiled=True)
    chunk_sum = jnp.sum(got_parts, axis=0, keepdims=True)
    spread = jnp.broadcast_to(chunk_sum, part_rows.shape)
    got_sums = lax.all_to_all(spread, axes, split_axis=0, concat_axis=0, tiled=True)
    grad_router = got_sums.reshape(router_part.shape) * (1.0 / math.sqrt(total_tokens))
    back_grad = grad_rows
    back_grad, grad_router = lax.optimization_barrier((back_grad, grad_router))
    back_rows = lax.all_to_all(back_grad, axes, split_axis=0, concat_axis=0, tiled=True)
    input_rows = got_tokens
    grid_rows = (((0, 1), (0, 1)), ((), ()))
    grad_gate_w = lax.dot_general(
        input_rows, grad_gate_pre, grid_rows, preferred_element_type=jnp.float32
    ).astype(jnp.bfloat16)
    grad_up_w = lax.dot_general(
        input_rows, grad_up_pre, grid_rows, preferred_element_type=jnp.float32
    ).astype(jnp.bfloat16)
    grad_sum = lax.dot_general(
        grid_table, back_rows, (((0, 1), (0, 1)), ((), ())), preferred_element_type=jnp.float32
    )
    grad_tokens = (
        grad_sum
        + lax.dot_general(
            logit_grad, router_weight, contract_cols, preferred_element_type=jnp.float32
        )
    ).astype(jnp.bfloat16)
    return (grad_tokens, grad_gate_w[None], grad_up_w[None], grad_down_w[None], grad_router)


def solution(mesh):
    in_specs = (
        P(("outer", "inner"), None),
        P(("outer", "inner"), None),
        P(("outer", "inner"), None),
        P(),
        P(("outer", "inner"), None, None),
        P(("outer", "inner"), None, None),
        P(("outer", "inner"), None, None),
        P(("outer", "inner"), None, None),
        P(("outer", "inner"), None, None),
    )
    out_specs = (
        P(("outer", "inner"), None),
        P(("outer", "inner"), None, None),
        P(("outer", "inner"), None, None),
        P(("outer", "inner"), None, None),
        P(),
    )
    return jax.shard_map(body, mesh=mesh, in_specs=in_specs, out_specs=out_specs, check_vma=False)
```

```python
import math

import jax
import jax.numpy as jnp
from jax import lax
from jax.sharding import PartitionSpec as P

contract_rows = (((0,), (0,)), ((), ()))
contract_cols = (((1,), (1,)), ((), ()))


def route_tables(routes, experts, capacity):
    flat_routes = routes.reshape(-1)
    onehot = (flat_routes[:, None] == jnp.arange(experts, dtype=jnp.int32)[None, :]).astype(
        jnp.int32
    )
    pairs = flat_routes.shape[0]
    lower = (
        jnp.arange(pairs, dtype=jnp.int32)[:, None] > jnp.arange(pairs, dtype=jnp.int32)[None, :]
    ).astype(jnp.bfloat16)
    earlier = jnp.dot(
        lower, onehot.astype(jnp.bfloat16), preferred_element_type=jnp.float32
    ).astype(jnp.int32)
    position = jnp.sum(earlier * onehot, axis=1)
    target = flat_routes * capacity + position
    slot_table = (
        jnp.arange(experts * capacity, dtype=jnp.int32)[:, None] == target[None, :]
    ).astype(jnp.bfloat16)
    token_table = jnp.sum(
        slot_table.reshape(experts * capacity, routes.shape[0], routes.shape[1]), axis=2
    )
    return (slot_table, token_table)


def route_probs(tokens, routes, router_weight):
    router_logits = jnp.dot(tokens, router_weight, preferred_element_type=jnp.float32)
    picked = (
        routes[:, :, None] == jnp.arange(router_weight.shape[1], dtype=jnp.int32)[None, None, :]
    )
    chosen = jnp.sum(jnp.where(picked, router_logits[:, None, :], jnp.float32(0.0)), axis=2)
    exp_terms = jnp.exp(chosen)
    return (picked, exp_terms / jnp.sum(exp_terms, axis=1, keepdims=True))


def dispatch_block(tokens, cotangent, routes, router_weight, capacity):
    picked, probs = route_probs(tokens, routes, router_weight)
    slot_table, token_table = route_tables(routes, router_weight.shape[1], capacity)
    send_tokens = jnp.dot(token_table, tokens, preferred_element_type=jnp.float32).astype(
        jnp.bfloat16
    )
    send_cot = jnp.dot(token_table, cotangent, preferred_element_type=jnp.float32).astype(
        jnp.bfloat16
    )
    probs_low = probs.astype(jnp.bfloat16).reshape(-1)
    send_weight = jnp.dot(slot_table, probs_low, preferred_element_type=jnp.float32).astype(
        jnp.bfloat16
    )
    return (picked, probs, slot_table, token_table, send_tokens, send_cot, send_weight)


def slot_dot(cot_rows, out_rows):
    return jnp.sum(cot_rows.astype(jnp.float32) * out_rows.astype(jnp.float32), axis=1).astype(
        jnp.bfloat16
    )


def expert_backward(
    input_rows, cot_rows, weight_rows, gate_pre, up_pre, gate_matrix, up_matrix, down_matrix
):
    gate_value = gate_pre.astype(jnp.float32)
    up_value = up_pre.astype(jnp.float32)
    sigmoid_gate = jax.nn.sigmoid(gate_value)
    silu_gate = gate_value * sigmoid_gate
    hidden = (silu_gate * up_value).astype(jnp.bfloat16)
    expert_out = jnp.dot(hidden, down_matrix, preferred_element_type=jnp.float32).astype(
        jnp.bfloat16
    )
    scaled_cot = (weight_rows.astype(jnp.float32)[:, None] * cot_rows.astype(jnp.float32)).astype(
        jnp.bfloat16
    )
    grad_hidden = lax.dot_general(
        scaled_cot, down_matrix, contract_cols, preferred_element_type=jnp.float32
    )
    grad_gate_pre = (
        grad_hidden * up_value * sigmoid_gate * (1.0 + gate_value * (1.0 - sigmoid_gate))
    ).astype(jnp.bfloat16)
    grad_up_pre = (grad_hidden * silu_gate).astype(jnp.bfloat16)
    grad_rows = (
        lax.dot_general(
            grad_gate_pre, gate_matrix, contract_cols, preferred_element_type=jnp.float32
        )
        + lax.dot_general(grad_up_pre, up_matrix, contract_cols, preferred_element_type=jnp.float32)
    ).astype(jnp.bfloat16)
    grad_gate_w = lax.dot_general(
        input_rows, grad_gate_pre, contract_rows, preferred_element_type=jnp.float32
    ).astype(jnp.bfloat16)
    grad_up_w = lax.dot_general(
        input_rows, grad_up_pre, contract_rows, preferred_element_type=jnp.float32
    ).astype(jnp.bfloat16)
    grad_down_w = lax.dot_general(
        hidden, scaled_cot, contract_rows, preferred_element_type=jnp.float32
    ).astype(jnp.bfloat16)
    return (grad_rows, expert_out, grad_gate_w, grad_up_w, grad_down_w)


def finish_block(
    tokens, router_weight, picked, probs, slot_table, token_table, back_rows, route_dot
):
    grad_sum = lax.dot_general(
        token_table, back_rows, contract_rows, preferred_element_type=jnp.float32
    )
    route_grad = lax.dot_general(
        slot_table, route_dot, contract_rows, preferred_element_type=jnp.float32
    ).reshape(probs.shape)
    inner_term = jnp.sum(probs * route_grad, axis=1, keepdims=True)
    chosen_grad = probs * (route_grad - inner_term)
    logit_grad = jnp.sum(
        jnp.where(picked, chosen_grad[:, :, None], jnp.float32(0.0)), axis=1
    ).astype(jnp.bfloat16)
    grad_tokens = (
        grad_sum
        + lax.dot_general(
            logit_grad, router_weight, contract_cols, preferred_element_type=jnp.float32
        )
    ).astype(jnp.bfloat16)
    router_part = lax.dot_general(
        tokens, logit_grad, contract_rows, preferred_element_type=jnp.float32
    )
    return (grad_tokens, router_part)


def expert_from_cot(cot_rows, weight_rows, gate_pre, up_pre, gate_matrix, up_matrix, down_matrix):
    last = (((2,), (0,)), ((), ()))
    last_t = (((2,), (1,)), ((), ()))
    grid_rows = (((0, 1), (0, 1)), ((), ()))
    gate_value = gate_pre.astype(jnp.float32)
    up_value = up_pre.astype(jnp.float32)
    sigmoid_gate = jax.nn.sigmoid(gate_value)
    silu_gate = gate_value * sigmoid_gate
    hidden = (silu_gate * up_value).astype(jnp.bfloat16)
    expert_out = lax.dot_general(
        hidden, down_matrix, last, preferred_element_type=jnp.float32
    ).astype(jnp.bfloat16)
    scaled_cot = (
        weight_rows.astype(jnp.float32)[:, :, None] * cot_rows.astype(jnp.float32)
    ).astype(jnp.bfloat16)
    grad_hidden = lax.dot_general(
        scaled_cot, down_matrix, last_t, preferred_element_type=jnp.float32
    )
    grad_gate_pre = (
        grad_hidden * up_value * sigmoid_gate * (1.0 + gate_value * (1.0 - sigmoid_gate))
    ).astype(jnp.bfloat16)
    grad_up_pre = (grad_hidden * silu_gate).astype(jnp.bfloat16)
    grad_rows = (
        lax.dot_general(grad_gate_pre, gate_matrix, last_t, preferred_element_type=jnp.float32)
        + lax.dot_general(grad_up_pre, up_matrix, last_t, preferred_element_type=jnp.float32)
    ).astype(jnp.bfloat16)
    grad_down_w = lax.dot_general(
        hidden, scaled_cot, grid_rows, preferred_element_type=jnp.float32
    ).astype(jnp.bfloat16)
    return (grad_rows, expert_out, grad_gate_pre, grad_up_pre, grad_down_w)


def body(
    tokens,
    cotangent,
    routes,
    router_weight,
    gate_saved,
    up_saved,
    gate_weight,
    up_weight,
    down_weight,
):
    experts = router_weight.shape[1]
    width = tokens.shape[1]
    capacity = gate_saved.shape[1] // experts
    outer_size = lax.axis_size("outer")
    inner_size = lax.axis_size("inner")
    axes = ("outer", "inner")
    picked, probs = route_probs(tokens, routes, router_weight)
    slot_table, token_table = route_tables(routes, experts, capacity)
    grid_table = token_table.reshape(experts, capacity, -1)
    probs_low = probs.astype(jnp.bfloat16).reshape(-1)
    send_weight = jnp.dot(slot_table, probs_low, preferred_element_type=jnp.float32).astype(
        jnp.bfloat16
    )
    got_weight = lax.all_to_all(
        send_weight.reshape(experts, capacity), axes, split_axis=0, concat_axis=0, tiled=True
    )
    grid_cot = jnp.dot(grid_table, cotangent, preferred_element_type=jnp.float32).astype(
        jnp.bfloat16
    )
    got_weight, grid_cot = lax.optimization_barrier((got_weight, grid_cot))
    got_cot = lax.all_to_all(grid_cot, axes, split_axis=0, concat_axis=0, tiled=True)
    grid_tokens = jnp.dot(grid_table, tokens, preferred_element_type=jnp.float32).astype(
        jnp.bfloat16
    )
    got_cot, grid_tokens = lax.optimization_barrier((got_cot, grid_tokens))
    half = width // 2
    got_tokens_a = lax.all_to_all(
        grid_tokens[:, :, :half], axes, split_axis=0, concat_axis=0, tiled=True
    )
    got_tokens_b = lax.all_to_all(
        grid_tokens[:, :, half:], axes, split_axis=0, concat_axis=0, tiled=True
    )
    cot_rows = got_cot
    grad_rows, expert_out, grad_gate_pre, grad_up_pre, grad_down_w = expert_from_cot(
        cot_rows,
        got_weight,
        gate_saved[0].reshape(experts, capacity, -1),
        up_saved[0].reshape(experts, capacity, -1),
        gate_weight[0],
        up_weight[0],
        down_weight[0],
    )
    slot_route_dot = jnp.sum(
        cot_rows.astype(jnp.float32) * expert_out.astype(jnp.float32), axis=2
    ).astype(jnp.bfloat16)
    slot_route_dot, got_tokens_b = lax.optimization_barrier((slot_route_dot, got_tokens_b))
    back_dot = lax.all_to_all(slot_route_dot, axes, split_axis=0, concat_axis=0, tiled=True)
    route_dot = back_dot.reshape(-1)
    route_grad = lax.dot_general(
        slot_table, route_dot, contract_rows, preferred_element_type=jnp.float32
    ).reshape(probs.shape)
    inner_term = jnp.sum(probs * route_grad, axis=1, keepdims=True)
    chosen_grad = probs * (route_grad - inner_term)
    logit_grad = jnp.sum(
        jnp.where(picked, chosen_grad[:, :, None], jnp.float32(0.0)), axis=1
    ).astype(jnp.bfloat16)
    router_part = lax.dot_general(
        tokens, logit_grad, contract_rows, preferred_element_type=jnp.float32
    )
    total_tokens = tokens.shape[0] * outer_size * inner_size
    devices = outer_size * inner_size
    part_rows = router_part.reshape(devices, -1)
    got_parts = lax.all_to_all(part_rows, axes, split_axis=0, concat_axis=0, tiled=True)
    chunk_sum = jnp.sum(got_parts, axis=0, keepdims=True)
    spread = jnp.broadcast_to(chunk_sum, part_rows.shape)
    got_sums = lax.all_to_all(spread, axes, split_axis=0, concat_axis=0, tiled=True)
    grad_router = got_sums.reshape(router_part.shape) * (1.0 / math.sqrt(total_tokens))
    back_grad = grad_rows
    back_grad, grad_router = lax.optimization_barrier((back_grad, grad_router))
    back_rows = lax.all_to_all(back_grad, axes, split_axis=0, concat_axis=0, tiled=True)
    grid_rows = (((0, 1), (0, 1)), ((), ()))

    def by_rows(pre):
        return jnp.concatenate(
            [
                lax.dot_general(got_tokens_a, pre, grid_rows, preferred_element_type=jnp.float32),
                lax.dot_general(got_tokens_b, pre, grid_rows, preferred_element_type=jnp.float32),
            ],
            axis=0,
        ).astype(jnp.bfloat16)

    grad_gate_w = by_rows(grad_gate_pre)
    grad_up_w = by_rows(grad_up_pre)
    grad_sum = lax.dot_general(
        grid_table, back_rows, (((0, 1), (0, 1)), ((), ())), preferred_element_type=jnp.float32
    )
    grad_tokens = (
        grad_sum
        + lax.dot_general(
            logit_grad, router_weight, contract_cols, preferred_element_type=jnp.float32
        )
    ).astype(jnp.bfloat16)
    return (grad_tokens, grad_gate_w[None], grad_up_w[None], grad_down_w[None], grad_router)


def solution(mesh):
    in_specs = (
        P(("outer", "inner"), None),
        P(("outer", "inner"), None),
        P(("outer", "inner"), None),
        P(),
        P(("outer", "inner"), None, None),
        P(("outer", "inner"), None, None),
        P(("outer", "inner"), None, None),
        P(("outer", "inner"), None, None),
        P(("outer", "inner"), None, None),
    )
    out_specs = (
        P(("outer", "inner"), None),
        P(("outer", "inner"), None, None),
        P(("outer", "inner"), None, None),
        P(("outer", "inner"), None, None),
        P(),
    )
    return jax.shard_map(body, mesh=mesh, in_specs=in_specs, out_specs=out_specs, check_vma=False)
```

```python
import math

import jax
import jax.numpy as jnp
from jax import lax
from jax.sharding import PartitionSpec as P

contract_rows = (((0,), (0,)), ((), ()))
contract_cols = (((1,), (1,)), ((), ()))


def route_tables(routes, experts, capacity):
    flat_routes = routes.reshape(-1)
    onehot = (flat_routes[:, None] == jnp.arange(experts, dtype=jnp.int32)[None, :]).astype(
        jnp.int32
    )
    pairs = flat_routes.shape[0]
    lower = (
        jnp.arange(pairs, dtype=jnp.int32)[:, None] > jnp.arange(pairs, dtype=jnp.int32)[None, :]
    ).astype(jnp.bfloat16)
    earlier = jnp.dot(
        lower, onehot.astype(jnp.bfloat16), preferred_element_type=jnp.float32
    ).astype(jnp.int32)
    position = jnp.sum(earlier * onehot, axis=1)
    target = flat_routes * capacity + position
    slot_table = (
        jnp.arange(experts * capacity, dtype=jnp.int32)[:, None] == target[None, :]
    ).astype(jnp.bfloat16)
    token_table = jnp.sum(
        slot_table.reshape(experts * capacity, routes.shape[0], routes.shape[1]), axis=2
    )
    return (slot_table, token_table)


def route_probs(tokens, routes, router_weight):
    router_logits = jnp.dot(tokens, router_weight, preferred_element_type=jnp.float32)
    picked = (
        routes[:, :, None] == jnp.arange(router_weight.shape[1], dtype=jnp.int32)[None, None, :]
    )
    chosen = jnp.sum(jnp.where(picked, router_logits[:, None, :], jnp.float32(0.0)), axis=2)
    exp_terms = jnp.exp(chosen)
    return (picked, exp_terms / jnp.sum(exp_terms, axis=1, keepdims=True))


def dispatch_block(tokens, cotangent, routes, router_weight, capacity):
    picked, probs = route_probs(tokens, routes, router_weight)
    slot_table, token_table = route_tables(routes, router_weight.shape[1], capacity)
    send_tokens = jnp.dot(token_table, tokens, preferred_element_type=jnp.float32).astype(
        jnp.bfloat16
    )
    send_cot = jnp.dot(token_table, cotangent, preferred_element_type=jnp.float32).astype(
        jnp.bfloat16
    )
    probs_low = probs.astype(jnp.bfloat16).reshape(-1)
    send_weight = jnp.dot(slot_table, probs_low, preferred_element_type=jnp.float32).astype(
        jnp.bfloat16
    )
    return (picked, probs, slot_table, token_table, send_tokens, send_cot, send_weight)


def slot_dot(cot_rows, out_rows):
    return jnp.sum(cot_rows.astype(jnp.float32) * out_rows.astype(jnp.float32), axis=1).astype(
        jnp.bfloat16
    )


def expert_backward(
    input_rows, cot_rows, weight_rows, gate_pre, up_pre, gate_matrix, up_matrix, down_matrix
):
    gate_value = gate_pre.astype(jnp.float32)
    up_value = up_pre.astype(jnp.float32)
    sigmoid_gate = jax.nn.sigmoid(gate_value)
    silu_gate = gate_value * sigmoid_gate
    hidden = (silu_gate * up_value).astype(jnp.bfloat16)
    expert_out = jnp.dot(hidden, down_matrix, preferred_element_type=jnp.float32).astype(
        jnp.bfloat16
    )
    scaled_cot = (weight_rows.astype(jnp.float32)[:, None] * cot_rows.astype(jnp.float32)).astype(
        jnp.bfloat16
    )
    grad_hidden = lax.dot_general(
        scaled_cot, down_matrix, contract_cols, preferred_element_type=jnp.float32
    )
    grad_gate_pre = (
        grad_hidden * up_value * sigmoid_gate * (1.0 + gate_value * (1.0 - sigmoid_gate))
    ).astype(jnp.bfloat16)
    grad_up_pre = (grad_hidden * silu_gate).astype(jnp.bfloat16)
    grad_rows = (
        lax.dot_general(
            grad_gate_pre, gate_matrix, contract_cols, preferred_element_type=jnp.float32
        )
        + lax.dot_general(grad_up_pre, up_matrix, contract_cols, preferred_element_type=jnp.float32)
    ).astype(jnp.bfloat16)
    grad_gate_w = lax.dot_general(
        input_rows, grad_gate_pre, contract_rows, preferred_element_type=jnp.float32
    ).astype(jnp.bfloat16)
    grad_up_w = lax.dot_general(
        input_rows, grad_up_pre, contract_rows, preferred_element_type=jnp.float32
    ).astype(jnp.bfloat16)
    grad_down_w = lax.dot_general(
        hidden, scaled_cot, contract_rows, preferred_element_type=jnp.float32
    ).astype(jnp.bfloat16)
    return (grad_rows, expert_out, grad_gate_w, grad_up_w, grad_down_w)


def finish_block(
    tokens, router_weight, picked, probs, slot_table, token_table, back_rows, route_dot
):
    grad_sum = lax.dot_general(
        token_table, back_rows, contract_rows, preferred_element_type=jnp.float32
    )
    route_grad = lax.dot_general(
        slot_table, route_dot, contract_rows, preferred_element_type=jnp.float32
    ).reshape(probs.shape)
    inner_term = jnp.sum(probs * route_grad, axis=1, keepdims=True)
    chosen_grad = probs * (route_grad - inner_term)
    logit_grad = jnp.sum(
        jnp.where(picked, chosen_grad[:, :, None], jnp.float32(0.0)), axis=1
    ).astype(jnp.bfloat16)
    grad_tokens = (
        grad_sum
        + lax.dot_general(
            logit_grad, router_weight, contract_cols, preferred_element_type=jnp.float32
        )
    ).astype(jnp.bfloat16)
    router_part = lax.dot_general(
        tokens, logit_grad, contract_rows, preferred_element_type=jnp.float32
    )
    return (grad_tokens, router_part)


def expert_from_cot(cot_rows, weight_rows, gate_pre, up_pre, gate_matrix, up_matrix, down_matrix):
    last = (((2,), (0,)), ((), ()))
    last_t = (((2,), (1,)), ((), ()))
    grid_rows = (((0, 1), (0, 1)), ((), ()))
    gate_value = gate_pre.astype(jnp.float32)
    up_value = up_pre.astype(jnp.float32)
    sigmoid_gate = jax.nn.sigmoid(gate_value)
    silu_gate = gate_value * sigmoid_gate
    hidden = (silu_gate * up_value).astype(jnp.bfloat16)
    expert_out = lax.dot_general(
        hidden, down_matrix, last, preferred_element_type=jnp.float32
    ).astype(jnp.bfloat16)
    scaled_cot = (
        weight_rows.astype(jnp.float32)[:, :, None] * cot_rows.astype(jnp.float32)
    ).astype(jnp.bfloat16)
    grad_hidden = lax.dot_general(
        scaled_cot, down_matrix, last_t, preferred_element_type=jnp.float32
    )
    grad_gate_pre = (
        grad_hidden * up_value * sigmoid_gate * (1.0 + gate_value * (1.0 - sigmoid_gate))
    ).astype(jnp.bfloat16)
    grad_up_pre = (grad_hidden * silu_gate).astype(jnp.bfloat16)
    grad_rows = (
        lax.dot_general(grad_gate_pre, gate_matrix, last_t, preferred_element_type=jnp.float32)
        + lax.dot_general(grad_up_pre, up_matrix, last_t, preferred_element_type=jnp.float32)
    ).astype(jnp.bfloat16)
    grad_down_w = lax.dot_general(
        hidden, scaled_cot, grid_rows, preferred_element_type=jnp.float32
    ).astype(jnp.bfloat16)
    return (grad_rows, expert_out, grad_gate_pre, grad_up_pre, grad_down_w)


def body(
    tokens,
    cotangent,
    routes,
    router_weight,
    gate_saved,
    up_saved,
    gate_weight,
    up_weight,
    down_weight,
):
    experts = router_weight.shape[1]
    width = tokens.shape[1]
    capacity = gate_saved.shape[1] // experts
    outer_size = lax.axis_size("outer")
    inner_size = lax.axis_size("inner")
    devices = outer_size * inner_size
    axes = ("outer", "inner")
    picked, probs = route_probs(tokens, routes, router_weight)
    slot_table, token_table = route_tables(routes, experts, capacity)
    grid_table = token_table.reshape(experts, capacity, -1)
    probs_low = probs.astype(jnp.bfloat16).reshape(-1)
    send_weight = jnp.dot(slot_table, probs_low, preferred_element_type=jnp.float32).astype(
        jnp.bfloat16
    )
    got_weight = lax.all_to_all(
        send_weight.reshape(experts, capacity), axes, split_axis=0, concat_axis=0, tiled=True
    )
    grid_cot = jnp.dot(grid_table, cotangent, preferred_element_type=jnp.float32).astype(
        jnp.bfloat16
    )
    got_weight, grid_cot = lax.optimization_barrier((got_weight, grid_cot))
    got_cot = lax.all_to_all(grid_cot, axes, split_axis=0, concat_axis=0, tiled=True)
    grid_tokens = jnp.dot(grid_table, tokens, preferred_element_type=jnp.float32).astype(
        jnp.bfloat16
    )
    got_cot, grid_tokens = lax.optimization_barrier((got_cot, grid_tokens))
    half = width // 2
    got_tokens_a = lax.all_to_all(
        grid_tokens[:, :, :half], axes, split_axis=0, concat_axis=0, tiled=True
    )
    cot_rows = got_cot
    grad_rows, expert_out, grad_gate_pre, grad_up_pre, grad_down_w = expert_from_cot(
        cot_rows,
        got_weight,
        gate_saved[0].reshape(experts, capacity, -1),
        up_saved[0].reshape(experts, capacity, -1),
        gate_weight[0],
        up_weight[0],
        down_weight[0],
    )
    slot_route_dot = jnp.sum(
        cot_rows.astype(jnp.float32) * expert_out.astype(jnp.float32), axis=2
    ).astype(jnp.bfloat16)
    dot_row = jnp.pad(slot_route_dot, ((0, 0), (0, half - capacity)))[:, None, :]
    send_b = jnp.concatenate([grid_tokens[:, :, half:], dot_row], axis=1)
    got_b = lax.all_to_all(send_b, axes, split_axis=0, concat_axis=0, tiled=True)
    got_tokens_b = got_b[:, :capacity, :]
    route_dot = got_b[:, capacity, :capacity].reshape(-1)
    route_grad = lax.dot_general(
        slot_table, route_dot, contract_rows, preferred_element_type=jnp.float32
    ).reshape(probs.shape)
    inner_term = jnp.sum(probs * route_grad, axis=1, keepdims=True)
    chosen_grad = probs * (route_grad - inner_term)
    logit_grad = jnp.sum(
        jnp.where(picked, chosen_grad[:, :, None], jnp.float32(0.0)), axis=1
    ).astype(jnp.bfloat16)
    router_part = lax.dot_general(
        tokens, logit_grad, contract_rows, preferred_element_type=jnp.float32
    )
    part_rows = router_part.reshape(devices, 1, -1)
    part_high = part_rows.astype(jnp.bfloat16)
    part_low = (part_rows - part_high.astype(jnp.float32)).astype(jnp.bfloat16)
    send_back = jnp.concatenate([grad_rows, part_high, part_low], axis=1)
    got_back = lax.all_to_all(send_back, axes, split_axis=0, concat_axis=0, tiled=True)
    back_rows = got_back[:, :capacity, :]
    got_parts = got_back[:, capacity, :].astype(jnp.float32) + got_back[:, capacity + 1, :].astype(
        jnp.float32
    )
    chunk_sum = jnp.sum(got_parts, axis=0, keepdims=True)
    spread = jnp.broadcast_to(chunk_sum, got_parts.shape)
    got_sums = lax.all_to_all(spread, axes, split_axis=0, concat_axis=0, tiled=True)
    total_tokens = tokens.shape[0] * devices
    grad_router = got_sums.reshape(router_part.shape) * (1.0 / math.sqrt(total_tokens))
    grid_rows = (((0, 1), (0, 1)), ((), ()))

    def by_rows(pre):
        return jnp.concatenate(
            [
                lax.dot_general(got_tokens_a, pre, grid_rows, preferred_element_type=jnp.float32),
                lax.dot_general(got_tokens_b, pre, grid_rows, preferred_element_type=jnp.float32),
            ],
            axis=0,
        ).astype(jnp.bfloat16)

    grad_gate_w = by_rows(grad_gate_pre)
    grad_up_w = by_rows(grad_up_pre)
    grad_sum = lax.dot_general(
        grid_table, back_rows, (((0, 1), (0, 1)), ((), ())), preferred_element_type=jnp.float32
    )
    grad_tokens = (
        grad_sum
        + lax.dot_general(
            logit_grad, router_weight, contract_cols, preferred_element_type=jnp.float32
        )
    ).astype(jnp.bfloat16)
    return (grad_tokens, grad_gate_w[None], grad_up_w[None], grad_down_w[None], grad_router)


def solution(mesh):
    in_specs = (
        P(("outer", "inner"), None),
        P(("outer", "inner"), None),
        P(("outer", "inner"), None),
        P(),
        P(("outer", "inner"), None, None),
        P(("outer", "inner"), None, None),
        P(("outer", "inner"), None, None),
        P(("outer", "inner"), None, None),
        P(("outer", "inner"), None, None),
    )
    out_specs = (
        P(("outer", "inner"), None),
        P(("outer", "inner"), None, None),
        P(("outer", "inner"), None, None),
        P(("outer", "inner"), None, None),
        P(),
    )
    return jax.shard_map(body, mesh=mesh, in_specs=in_specs, out_specs=out_specs, check_vma=False)
```

```python
import math

import jax
import jax.numpy as jnp
from jax import lax
from jax.sharding import PartitionSpec as P

contract_rows = (((0,), (0,)), ((), ()))
contract_cols = (((1,), (1,)), ((), ()))


def route_tables(routes, experts, capacity):
    flat_routes = routes.reshape(-1)
    onehot = (flat_routes[:, None] == jnp.arange(experts, dtype=jnp.int32)[None, :]).astype(
        jnp.int32
    )
    pairs = flat_routes.shape[0]
    lower = (
        jnp.arange(pairs, dtype=jnp.int32)[:, None] > jnp.arange(pairs, dtype=jnp.int32)[None, :]
    ).astype(jnp.bfloat16)
    earlier = jnp.dot(
        lower, onehot.astype(jnp.bfloat16), preferred_element_type=jnp.float32
    ).astype(jnp.int32)
    position = jnp.sum(earlier * onehot, axis=1)
    target = flat_routes * capacity + position
    slot_table = (
        jnp.arange(experts * capacity, dtype=jnp.int32)[:, None] == target[None, :]
    ).astype(jnp.bfloat16)
    token_table = jnp.sum(
        slot_table.reshape(experts * capacity, routes.shape[0], routes.shape[1]), axis=2
    )
    return (slot_table, token_table)


def route_probs(tokens, routes, router_weight):
    router_logits = jnp.dot(tokens, router_weight, preferred_element_type=jnp.float32)
    picked = (
        routes[:, :, None] == jnp.arange(router_weight.shape[1], dtype=jnp.int32)[None, None, :]
    )
    chosen = jnp.sum(jnp.where(picked, router_logits[:, None, :], jnp.float32(0.0)), axis=2)
    exp_terms = jnp.exp(chosen)
    return (picked, exp_terms / jnp.sum(exp_terms, axis=1, keepdims=True))


def dispatch_block(tokens, cotangent, routes, router_weight, capacity):
    picked, probs = route_probs(tokens, routes, router_weight)
    slot_table, token_table = route_tables(routes, router_weight.shape[1], capacity)
    send_tokens = jnp.dot(token_table, tokens, preferred_element_type=jnp.float32).astype(
        jnp.bfloat16
    )
    send_cot = jnp.dot(token_table, cotangent, preferred_element_type=jnp.float32).astype(
        jnp.bfloat16
    )
    probs_low = probs.astype(jnp.bfloat16).reshape(-1)
    send_weight = jnp.dot(slot_table, probs_low, preferred_element_type=jnp.float32).astype(
        jnp.bfloat16
    )
    return (picked, probs, slot_table, token_table, send_tokens, send_cot, send_weight)


def slot_dot(cot_rows, out_rows):
    return jnp.sum(cot_rows.astype(jnp.float32) * out_rows.astype(jnp.float32), axis=1).astype(
        jnp.bfloat16
    )


def expert_backward(
    input_rows, cot_rows, weight_rows, gate_pre, up_pre, gate_matrix, up_matrix, down_matrix
):
    gate_value = gate_pre.astype(jnp.float32)
    up_value = up_pre.astype(jnp.float32)
    sigmoid_gate = jax.nn.sigmoid(gate_value)
    silu_gate = gate_value * sigmoid_gate
    hidden = (silu_gate * up_value).astype(jnp.bfloat16)
    expert_out = jnp.dot(hidden, down_matrix, preferred_element_type=jnp.float32).astype(
        jnp.bfloat16
    )
    scaled_cot = (weight_rows.astype(jnp.float32)[:, None] * cot_rows.astype(jnp.float32)).astype(
        jnp.bfloat16
    )
    grad_hidden = lax.dot_general(
        scaled_cot, down_matrix, contract_cols, preferred_element_type=jnp.float32
    )
    grad_gate_pre = (
        grad_hidden * up_value * sigmoid_gate * (1.0 + gate_value * (1.0 - sigmoid_gate))
    ).astype(jnp.bfloat16)
    grad_up_pre = (grad_hidden * silu_gate).astype(jnp.bfloat16)
    grad_rows = (
        lax.dot_general(
            grad_gate_pre, gate_matrix, contract_cols, preferred_element_type=jnp.float32
        )
        + lax.dot_general(grad_up_pre, up_matrix, contract_cols, preferred_element_type=jnp.float32)
    ).astype(jnp.bfloat16)
    grad_gate_w = lax.dot_general(
        input_rows, grad_gate_pre, contract_rows, preferred_element_type=jnp.float32
    ).astype(jnp.bfloat16)
    grad_up_w = lax.dot_general(
        input_rows, grad_up_pre, contract_rows, preferred_element_type=jnp.float32
    ).astype(jnp.bfloat16)
    grad_down_w = lax.dot_general(
        hidden, scaled_cot, contract_rows, preferred_element_type=jnp.float32
    ).astype(jnp.bfloat16)
    return (grad_rows, expert_out, grad_gate_w, grad_up_w, grad_down_w)


def finish_block(
    tokens, router_weight, picked, probs, slot_table, token_table, back_rows, route_dot
):
    grad_sum = lax.dot_general(
        token_table, back_rows, contract_rows, preferred_element_type=jnp.float32
    )
    route_grad = lax.dot_general(
        slot_table, route_dot, contract_rows, preferred_element_type=jnp.float32
    ).reshape(probs.shape)
    inner_term = jnp.sum(probs * route_grad, axis=1, keepdims=True)
    chosen_grad = probs * (route_grad - inner_term)
    logit_grad = jnp.sum(
        jnp.where(picked, chosen_grad[:, :, None], jnp.float32(0.0)), axis=1
    ).astype(jnp.bfloat16)
    grad_tokens = (
        grad_sum
        + lax.dot_general(
            logit_grad, router_weight, contract_cols, preferred_element_type=jnp.float32
        )
    ).astype(jnp.bfloat16)
    router_part = lax.dot_general(
        tokens, logit_grad, contract_rows, preferred_element_type=jnp.float32
    )
    return (grad_tokens, router_part)


def expert_from_cot(cot_rows, weight_rows, gate_pre, up_pre, gate_matrix, up_matrix, down_matrix):
    last = (((2,), (0,)), ((), ()))
    last_t = (((2,), (1,)), ((), ()))
    grid_rows = (((0, 1), (0, 1)), ((), ()))
    gate_value = gate_pre.astype(jnp.float32)
    up_value = up_pre.astype(jnp.float32)
    sigmoid_gate = jax.nn.sigmoid(gate_value)
    silu_gate = gate_value * sigmoid_gate
    hidden = (silu_gate * up_value).astype(jnp.bfloat16)
    expert_out = lax.dot_general(
        hidden, down_matrix, last, preferred_element_type=jnp.float32
    ).astype(jnp.bfloat16)
    scaled_cot = (
        weight_rows.astype(jnp.float32)[:, :, None] * cot_rows.astype(jnp.float32)
    ).astype(jnp.bfloat16)
    grad_hidden = lax.dot_general(
        scaled_cot, down_matrix, last_t, preferred_element_type=jnp.float32
    )
    grad_gate_pre = (
        grad_hidden * up_value * sigmoid_gate * (1.0 + gate_value * (1.0 - sigmoid_gate))
    ).astype(jnp.bfloat16)
    grad_up_pre = (grad_hidden * silu_gate).astype(jnp.bfloat16)
    grad_rows = (
        lax.dot_general(grad_gate_pre, gate_matrix, last_t, preferred_element_type=jnp.float32)
        + lax.dot_general(grad_up_pre, up_matrix, last_t, preferred_element_type=jnp.float32)
    ).astype(jnp.bfloat16)
    grad_down_w = lax.dot_general(
        hidden, scaled_cot, grid_rows, preferred_element_type=jnp.float32
    ).astype(jnp.bfloat16)
    return (grad_rows, expert_out, grad_gate_pre, grad_up_pre, grad_down_w)


def body(
    tokens,
    cotangent,
    routes,
    router_weight,
    gate_saved,
    up_saved,
    gate_weight,
    up_weight,
    down_weight,
):
    experts = router_weight.shape[1]
    width = tokens.shape[1]
    capacity = gate_saved.shape[1] // experts
    outer_size = lax.axis_size("outer")
    inner_size = lax.axis_size("inner")
    devices = outer_size * inner_size
    axes = ("outer", "inner")
    picked, probs = route_probs(tokens, routes, router_weight)
    slot_table, token_table = route_tables(routes, experts, capacity)
    grid_table = token_table.reshape(experts, capacity, -1)
    probs_low = probs.astype(jnp.bfloat16).reshape(-1)
    send_weight = jnp.dot(slot_table, probs_low, preferred_element_type=jnp.float32).astype(
        jnp.bfloat16
    )
    got_weight = lax.all_to_all(
        send_weight.reshape(experts, capacity), axes, split_axis=0, concat_axis=0, tiled=True
    )
    grid_cot = jnp.dot(grid_table, cotangent, preferred_element_type=jnp.float32).astype(
        jnp.bfloat16
    )
    got_weight, grid_cot = lax.optimization_barrier((got_weight, grid_cot))
    got_cot = lax.all_to_all(grid_cot, axes, split_axis=0, concat_axis=0, tiled=True)
    grid_tokens = jnp.dot(grid_table, tokens, preferred_element_type=jnp.float32).astype(
        jnp.bfloat16
    )
    got_cot, grid_tokens = lax.optimization_barrier((got_cot, grid_tokens))
    half = width // 2
    got_tokens_a = lax.all_to_all(
        grid_tokens[:, :, :half], axes, split_axis=0, concat_axis=0, tiled=True
    )
    cot_rows = got_cot
    grad_rows, expert_out, grad_gate_pre, grad_up_pre, grad_down_w = expert_from_cot(
        cot_rows,
        got_weight,
        gate_saved[0].reshape(experts, capacity, -1),
        up_saved[0].reshape(experts, capacity, -1),
        gate_weight[0],
        up_weight[0],
        down_weight[0],
    )
    slot_route_dot = jnp.sum(
        cot_rows.astype(jnp.float32) * expert_out.astype(jnp.float32), axis=2
    ).astype(jnp.bfloat16)
    dot_row = jnp.pad(slot_route_dot, ((0, 0), (0, half - capacity)))[:, None, :]
    send_b = jnp.concatenate([grid_tokens[:, :, half:], dot_row], axis=1)
    got_b = lax.all_to_all(send_b, axes, split_axis=0, concat_axis=0, tiled=True)
    got_tokens_b = got_b[:, :capacity, :]
    route_dot = got_b[:, capacity, :capacity].reshape(-1)
    route_grad = lax.dot_general(
        slot_table, route_dot, contract_rows, preferred_element_type=jnp.float32
    ).reshape(probs.shape)
    inner_term = jnp.sum(probs * route_grad, axis=1, keepdims=True)
    chosen_grad = probs * (route_grad - inner_term)
    logit_grad = jnp.sum(
        jnp.where(picked, chosen_grad[:, :, None], jnp.float32(0.0)), axis=1
    ).astype(jnp.bfloat16)
    router_part = lax.dot_general(
        tokens, logit_grad, contract_rows, preferred_element_type=jnp.float32
    )
    part_rows = router_part.reshape(devices, 1, -1)
    part_rounded = lax.reduce_precision(part_rows, exponent_bits=8, mantissa_bits=7)
    part_high = part_rounded.astype(jnp.bfloat16)
    part_low = (part_rows - part_rounded).astype(jnp.bfloat16)
    send_back = jnp.concatenate([grad_rows, part_high, part_low], axis=1)
    got_back = lax.all_to_all(send_back, axes, split_axis=0, concat_axis=0, tiled=True)
    back_rows = got_back[:, :capacity, :]
    got_parts = got_back[:, capacity, :].astype(jnp.float32) + got_back[:, capacity + 1, :].astype(
        jnp.float32
    )
    chunk_sum = jnp.sum(got_parts, axis=0, keepdims=True)
    spread = jnp.broadcast_to(chunk_sum, got_parts.shape)
    got_sums = lax.all_to_all(spread, axes, split_axis=0, concat_axis=0, tiled=True)
    total_tokens = tokens.shape[0] * devices
    grad_router = got_sums.reshape(router_part.shape) * (1.0 / math.sqrt(total_tokens))
    grid_rows = (((0, 1), (0, 1)), ((), ()))

    def by_rows(pre):
        return jnp.concatenate(
            [
                lax.dot_general(got_tokens_a, pre, grid_rows, preferred_element_type=jnp.float32),
                lax.dot_general(got_tokens_b, pre, grid_rows, preferred_element_type=jnp.float32),
            ],
            axis=0,
        ).astype(jnp.bfloat16)

    grad_gate_w = by_rows(grad_gate_pre)
    grad_up_w = by_rows(grad_up_pre)
    grad_sum = lax.dot_general(
        grid_table, back_rows, (((0, 1), (0, 1)), ((), ())), preferred_element_type=jnp.float32
    )
    grad_tokens = (
        grad_sum
        + lax.dot_general(
            logit_grad, router_weight, contract_cols, preferred_element_type=jnp.float32
        )
    ).astype(jnp.bfloat16)
    return (grad_tokens, grad_gate_w[None], grad_up_w[None], grad_down_w[None], grad_router)


def solution(mesh):
    in_specs = (
        P(("outer", "inner"), None),
        P(("outer", "inner"), None),
        P(("outer", "inner"), None),
        P(),
        P(("outer", "inner"), None, None),
        P(("outer", "inner"), None, None),
        P(("outer", "inner"), None, None),
        P(("outer", "inner"), None, None),
        P(("outer", "inner"), None, None),
    )
    out_specs = (
        P(("outer", "inner"), None),
        P(("outer", "inner"), None, None),
        P(("outer", "inner"), None, None),
        P(("outer", "inner"), None, None),
        P(),
    )
    return jax.shard_map(body, mesh=mesh, in_specs=in_specs, out_specs=out_specs, check_vma=False)
```

```python
import math

import jax
import jax.numpy as jnp
from jax import lax
from jax.sharding import PartitionSpec as P

contract_rows = (((0,), (0,)), ((), ()))
contract_cols = (((1,), (1,)), ((), ()))


def route_tables(routes, experts, capacity):
    flat_routes = routes.reshape(-1)
    onehot = (flat_routes[:, None] == jnp.arange(experts, dtype=jnp.int32)[None, :]).astype(
        jnp.int32
    )
    pairs = flat_routes.shape[0]
    lower = (
        jnp.arange(pairs, dtype=jnp.int32)[:, None] > jnp.arange(pairs, dtype=jnp.int32)[None, :]
    ).astype(jnp.bfloat16)
    earlier = jnp.dot(
        lower, onehot.astype(jnp.bfloat16), preferred_element_type=jnp.float32
    ).astype(jnp.int32)
    position = jnp.sum(earlier * onehot, axis=1)
    target = flat_routes * capacity + position
    slot_table = (
        jnp.arange(experts * capacity, dtype=jnp.int32)[:, None] == target[None, :]
    ).astype(jnp.bfloat16)
    token_table = jnp.sum(
        slot_table.reshape(experts * capacity, routes.shape[0], routes.shape[1]), axis=2
    )
    return (slot_table, token_table)


def route_probs(tokens, routes, router_weight):
    router_logits = jnp.dot(tokens, router_weight, preferred_element_type=jnp.float32)
    picked = (
        routes[:, :, None] == jnp.arange(router_weight.shape[1], dtype=jnp.int32)[None, None, :]
    )
    chosen = jnp.sum(jnp.where(picked, router_logits[:, None, :], jnp.float32(0.0)), axis=2)
    exp_terms = jnp.exp(chosen)
    return (picked, exp_terms / jnp.sum(exp_terms, axis=1, keepdims=True))


def dispatch_block(tokens, cotangent, routes, router_weight, capacity):
    picked, probs = route_probs(tokens, routes, router_weight)
    slot_table, token_table = route_tables(routes, router_weight.shape[1], capacity)
    send_tokens = jnp.dot(token_table, tokens, preferred_element_type=jnp.float32).astype(
        jnp.bfloat16
    )
    send_cot = jnp.dot(token_table, cotangent, preferred_element_type=jnp.float32).astype(
        jnp.bfloat16
    )
    probs_low = probs.astype(jnp.bfloat16).reshape(-1)
    send_weight = jnp.dot(slot_table, probs_low, preferred_element_type=jnp.float32).astype(
        jnp.bfloat16
    )
    return (picked, probs, slot_table, token_table, send_tokens, send_cot, send_weight)


def slot_dot(cot_rows, out_rows):
    return jnp.sum(cot_rows.astype(jnp.float32) * out_rows.astype(jnp.float32), axis=1).astype(
        jnp.bfloat16
    )


def expert_backward(
    input_rows, cot_rows, weight_rows, gate_pre, up_pre, gate_matrix, up_matrix, down_matrix
):
    gate_value = gate_pre.astype(jnp.float32)
    up_value = up_pre.astype(jnp.float32)
    sigmoid_gate = jax.nn.sigmoid(gate_value)
    silu_gate = gate_value * sigmoid_gate
    hidden = (silu_gate * up_value).astype(jnp.bfloat16)
    expert_out = jnp.dot(hidden, down_matrix, preferred_element_type=jnp.float32).astype(
        jnp.bfloat16
    )
    scaled_cot = (weight_rows.astype(jnp.float32)[:, None] * cot_rows.astype(jnp.float32)).astype(
        jnp.bfloat16
    )
    grad_hidden = lax.dot_general(
        scaled_cot, down_matrix, contract_cols, preferred_element_type=jnp.float32
    )
    grad_gate_pre = (
        grad_hidden * up_value * sigmoid_gate * (1.0 + gate_value * (1.0 - sigmoid_gate))
    ).astype(jnp.bfloat16)
    grad_up_pre = (grad_hidden * silu_gate).astype(jnp.bfloat16)
    grad_rows = (
        lax.dot_general(
            grad_gate_pre, gate_matrix, contract_cols, preferred_element_type=jnp.float32
        )
        + lax.dot_general(grad_up_pre, up_matrix, contract_cols, preferred_element_type=jnp.float32)
    ).astype(jnp.bfloat16)
    grad_gate_w = lax.dot_general(
        input_rows, grad_gate_pre, contract_rows, preferred_element_type=jnp.float32
    ).astype(jnp.bfloat16)
    grad_up_w = lax.dot_general(
        input_rows, grad_up_pre, contract_rows, preferred_element_type=jnp.float32
    ).astype(jnp.bfloat16)
    grad_down_w = lax.dot_general(
        hidden, scaled_cot, contract_rows, preferred_element_type=jnp.float32
    ).astype(jnp.bfloat16)
    return (grad_rows, expert_out, grad_gate_w, grad_up_w, grad_down_w)


def finish_block(
    tokens, router_weight, picked, probs, slot_table, token_table, back_rows, route_dot
):
    grad_sum = lax.dot_general(
        token_table, back_rows, contract_rows, preferred_element_type=jnp.float32
    )
    route_grad = lax.dot_general(
        slot_table, route_dot, contract_rows, preferred_element_type=jnp.float32
    ).reshape(probs.shape)
    inner_term = jnp.sum(probs * route_grad, axis=1, keepdims=True)
    chosen_grad = probs * (route_grad - inner_term)
    logit_grad = jnp.sum(
        jnp.where(picked, chosen_grad[:, :, None], jnp.float32(0.0)), axis=1
    ).astype(jnp.bfloat16)
    grad_tokens = (
        grad_sum
        + lax.dot_general(
            logit_grad, router_weight, contract_cols, preferred_element_type=jnp.float32
        )
    ).astype(jnp.bfloat16)
    router_part = lax.dot_general(
        tokens, logit_grad, contract_rows, preferred_element_type=jnp.float32
    )
    return (grad_tokens, router_part)


def expert_from_cot(cot_rows, weight_rows, gate_pre, up_pre, gate_matrix, up_matrix, down_matrix):
    last = (((2,), (0,)), ((), ()))
    last_t = (((2,), (1,)), ((), ()))
    grid_rows = (((0, 1), (0, 1)), ((), ()))
    gate_value = gate_pre.astype(jnp.float32)
    up_value = up_pre.astype(jnp.float32)
    sigmoid_gate = jax.nn.sigmoid(gate_value)
    silu_gate = gate_value * sigmoid_gate
    hidden = (silu_gate * up_value).astype(jnp.bfloat16)
    expert_out = lax.dot_general(
        hidden, down_matrix, last, preferred_element_type=jnp.float32
    ).astype(jnp.bfloat16)
    scaled_cot = (
        weight_rows.astype(jnp.float32)[:, :, None] * cot_rows.astype(jnp.float32)
    ).astype(jnp.bfloat16)
    grad_hidden = lax.dot_general(
        scaled_cot, down_matrix, last_t, preferred_element_type=jnp.float32
    )
    grad_gate_pre = (
        grad_hidden * up_value * sigmoid_gate * (1.0 + gate_value * (1.0 - sigmoid_gate))
    ).astype(jnp.bfloat16)
    grad_up_pre = (grad_hidden * silu_gate).astype(jnp.bfloat16)
    grad_rows = (
        lax.dot_general(grad_gate_pre, gate_matrix, last_t, preferred_element_type=jnp.float32)
        + lax.dot_general(grad_up_pre, up_matrix, last_t, preferred_element_type=jnp.float32)
    ).astype(jnp.bfloat16)
    grad_down_w = lax.dot_general(
        hidden, scaled_cot, grid_rows, preferred_element_type=jnp.float32
    ).astype(jnp.bfloat16)
    return (grad_rows, expert_out, grad_gate_pre, grad_up_pre, grad_down_w)


def body(
    tokens,
    cotangent,
    routes,
    router_weight,
    gate_saved,
    up_saved,
    gate_weight,
    up_weight,
    down_weight,
):
    experts = router_weight.shape[1]
    width = tokens.shape[1]
    capacity = gate_saved.shape[1] // experts
    outer_size = lax.axis_size("outer")
    inner_size = lax.axis_size("inner")
    devices = outer_size * inner_size
    axes = ("outer", "inner")
    picked, probs = route_probs(tokens, routes, router_weight)
    slot_table, token_table = route_tables(routes, experts, capacity)
    grid_table = token_table.reshape(experts, capacity, -1)
    probs_low = probs.astype(jnp.bfloat16).reshape(-1)
    send_weight = jnp.dot(slot_table, probs_low, preferred_element_type=jnp.float32).astype(
        jnp.bfloat16
    )
    weight_row = jnp.pad(send_weight.reshape(experts, capacity), ((0, 0), (0, width - capacity)))
    grid_cot = jnp.dot(grid_table, cotangent, preferred_element_type=jnp.float32).astype(
        jnp.bfloat16
    )
    send_cot = jnp.concatenate([grid_cot, weight_row[:, None, :]], axis=1)
    got_cot_w = lax.all_to_all(send_cot, axes, split_axis=0, concat_axis=0, tiled=True)
    got_cot = got_cot_w[:, :capacity, :]
    got_weight = got_cot_w[:, capacity, :capacity]
    grid_tokens = jnp.dot(grid_table, tokens, preferred_element_type=jnp.float32).astype(
        jnp.bfloat16
    )
    got_cot, grid_tokens = lax.optimization_barrier((got_cot, grid_tokens))
    half = width // 2
    got_tokens_a = lax.all_to_all(
        grid_tokens[:, :, :half], axes, split_axis=0, concat_axis=0, tiled=True
    )
    cot_rows = got_cot
    grad_rows, expert_out, grad_gate_pre, grad_up_pre, grad_down_w = expert_from_cot(
        cot_rows,
        got_weight,
        gate_saved[0].reshape(experts, capacity, -1),
        up_saved[0].reshape(experts, capacity, -1),
        gate_weight[0],
        up_weight[0],
        down_weight[0],
    )
    slot_route_dot = jnp.sum(
        cot_rows.astype(jnp.float32) * expert_out.astype(jnp.float32), axis=2
    ).astype(jnp.bfloat16)
    dot_row = jnp.pad(slot_route_dot, ((0, 0), (0, half - capacity)))[:, None, :]
    send_b = jnp.concatenate([grid_tokens[:, :, half:], dot_row], axis=1)
    send_b, got_tokens_a = lax.optimization_barrier((send_b, got_tokens_a))
    got_b = lax.all_to_all(send_b, axes, split_axis=0, concat_axis=0, tiled=True)
    got_tokens_b = got_b[:, :capacity, :]
    route_dot = got_b[:, capacity, :capacity].reshape(-1)
    route_grad = lax.dot_general(
        slot_table, route_dot, contract_rows, preferred_element_type=jnp.float32
    ).reshape(probs.shape)
    inner_term = jnp.sum(probs * route_grad, axis=1, keepdims=True)
    chosen_grad = probs * (route_grad - inner_term)
    logit_grad = jnp.sum(
        jnp.where(picked, chosen_grad[:, :, None], jnp.float32(0.0)), axis=1
    ).astype(jnp.bfloat16)
    router_part = lax.dot_general(
        tokens, logit_grad, contract_rows, preferred_element_type=jnp.float32
    )
    part_rows = router_part.reshape(devices, 1, -1)
    part_rounded = lax.reduce_precision(part_rows, exponent_bits=8, mantissa_bits=7)
    part_high = part_rounded.astype(jnp.bfloat16)
    part_low = (part_rows - part_rounded).astype(jnp.bfloat16)
    send_back = jnp.concatenate([grad_rows, part_high, part_low], axis=1)
    got_back = lax.all_to_all(send_back, axes, split_axis=0, concat_axis=0, tiled=True)
    back_rows = got_back[:, :capacity, :]
    got_parts = got_back[:, capacity, :].astype(jnp.float32) + got_back[:, capacity + 1, :].astype(
        jnp.float32
    )
    chunk_sum = jnp.sum(got_parts, axis=0, keepdims=True)
    spread = jnp.broadcast_to(chunk_sum, got_parts.shape)
    got_sums = lax.all_to_all(spread, axes, split_axis=0, concat_axis=0, tiled=True)
    total_tokens = tokens.shape[0] * devices
    grad_router = got_sums.reshape(router_part.shape) * (1.0 / math.sqrt(total_tokens))
    grid_rows = (((0, 1), (0, 1)), ((), ()))

    def by_rows(pre):
        return jnp.concatenate(
            [
                lax.dot_general(got_tokens_a, pre, grid_rows, preferred_element_type=jnp.float32),
                lax.dot_general(got_tokens_b, pre, grid_rows, preferred_element_type=jnp.float32),
            ],
            axis=0,
        ).astype(jnp.bfloat16)

    grad_gate_w = by_rows(grad_gate_pre)
    grad_up_w = by_rows(grad_up_pre)
    grad_sum = lax.dot_general(
        grid_table, back_rows, (((0, 1), (0, 1)), ((), ())), preferred_element_type=jnp.float32
    )
    grad_tokens = (
        grad_sum
        + lax.dot_general(
            logit_grad, router_weight, contract_cols, preferred_element_type=jnp.float32
        )
    ).astype(jnp.bfloat16)
    return (grad_tokens, grad_gate_w[None], grad_up_w[None], grad_down_w[None], grad_router)


def solution(mesh):
    in_specs = (
        P(("outer", "inner"), None),
        P(("outer", "inner"), None),
        P(("outer", "inner"), None),
        P(),
        P(("outer", "inner"), None, None),
        P(("outer", "inner"), None, None),
        P(("outer", "inner"), None, None),
        P(("outer", "inner"), None, None),
        P(("outer", "inner"), None, None),
    )
    out_specs = (
        P(("outer", "inner"), None),
        P(("outer", "inner"), None, None),
        P(("outer", "inner"), None, None),
        P(("outer", "inner"), None, None),
        P(),
    )
    return jax.shard_map(body, mesh=mesh, in_specs=in_specs, out_specs=out_specs, check_vma=False)
```

```python
import math

import jax
import jax.numpy as jnp
from jax import lax
from jax.sharding import PartitionSpec as P

contract_rows = (((0,), (0,)), ((), ()))
contract_cols = (((1,), (1,)), ((), ()))


def route_tables(routes, experts, capacity):
    flat_routes = routes.reshape(-1)
    onehot = (flat_routes[:, None] == jnp.arange(experts, dtype=jnp.int32)[None, :]).astype(
        jnp.int32
    )
    pairs = flat_routes.shape[0]
    lower = (
        jnp.arange(pairs, dtype=jnp.int32)[:, None] > jnp.arange(pairs, dtype=jnp.int32)[None, :]
    ).astype(jnp.bfloat16)
    earlier = jnp.dot(
        lower, onehot.astype(jnp.bfloat16), preferred_element_type=jnp.float32
    ).astype(jnp.int32)
    position = jnp.sum(earlier * onehot, axis=1)
    target = flat_routes * capacity + position
    slot_table = (
        jnp.arange(experts * capacity, dtype=jnp.int32)[:, None] == target[None, :]
    ).astype(jnp.bfloat16)
    token_table = jnp.sum(
        slot_table.reshape(experts * capacity, routes.shape[0], routes.shape[1]), axis=2
    )
    return (slot_table, token_table)


def route_probs(tokens, routes, router_weight):
    router_logits = jnp.dot(tokens, router_weight, preferred_element_type=jnp.float32)
    picked = (
        routes[:, :, None] == jnp.arange(router_weight.shape[1], dtype=jnp.int32)[None, None, :]
    )
    chosen = jnp.sum(jnp.where(picked, router_logits[:, None, :], jnp.float32(0.0)), axis=2)
    exp_terms = jnp.exp(chosen)
    return (picked, exp_terms / jnp.sum(exp_terms, axis=1, keepdims=True))


def dispatch_block(tokens, cotangent, routes, router_weight, capacity):
    picked, probs = route_probs(tokens, routes, router_weight)
    slot_table, token_table = route_tables(routes, router_weight.shape[1], capacity)
    send_tokens = jnp.dot(token_table, tokens, preferred_element_type=jnp.float32).astype(
        jnp.bfloat16
    )
    send_cot = jnp.dot(token_table, cotangent, preferred_element_type=jnp.float32).astype(
        jnp.bfloat16
    )
    probs_low = probs.astype(jnp.bfloat16).reshape(-1)
    send_weight = jnp.dot(slot_table, probs_low, preferred_element_type=jnp.float32).astype(
        jnp.bfloat16
    )
    return (picked, probs, slot_table, token_table, send_tokens, send_cot, send_weight)


def slot_dot(cot_rows, out_rows):
    return jnp.sum(cot_rows.astype(jnp.float32) * out_rows.astype(jnp.float32), axis=1).astype(
        jnp.bfloat16
    )


def expert_backward(
    input_rows, cot_rows, weight_rows, gate_pre, up_pre, gate_matrix, up_matrix, down_matrix
):
    gate_value = gate_pre.astype(jnp.float32)
    up_value = up_pre.astype(jnp.float32)
    sigmoid_gate = jax.nn.sigmoid(gate_value)
    silu_gate = gate_value * sigmoid_gate
    hidden = (silu_gate * up_value).astype(jnp.bfloat16)
    expert_out = jnp.dot(hidden, down_matrix, preferred_element_type=jnp.float32).astype(
        jnp.bfloat16
    )
    scaled_cot = (weight_rows.astype(jnp.float32)[:, None] * cot_rows.astype(jnp.float32)).astype(
        jnp.bfloat16
    )
    grad_hidden = lax.dot_general(
        scaled_cot, down_matrix, contract_cols, preferred_element_type=jnp.float32
    )
    grad_gate_pre = (
        grad_hidden * up_value * sigmoid_gate * (1.0 + gate_value * (1.0 - sigmoid_gate))
    ).astype(jnp.bfloat16)
    grad_up_pre = (grad_hidden * silu_gate).astype(jnp.bfloat16)
    grad_rows = (
        lax.dot_general(
            grad_gate_pre, gate_matrix, contract_cols, preferred_element_type=jnp.float32
        )
        + lax.dot_general(grad_up_pre, up_matrix, contract_cols, preferred_element_type=jnp.float32)
    ).astype(jnp.bfloat16)
    grad_gate_w = lax.dot_general(
        input_rows, grad_gate_pre, contract_rows, preferred_element_type=jnp.float32
    ).astype(jnp.bfloat16)
    grad_up_w = lax.dot_general(
        input_rows, grad_up_pre, contract_rows, preferred_element_type=jnp.float32
    ).astype(jnp.bfloat16)
    grad_down_w = lax.dot_general(
        hidden, scaled_cot, contract_rows, preferred_element_type=jnp.float32
    ).astype(jnp.bfloat16)
    return (grad_rows, expert_out, grad_gate_w, grad_up_w, grad_down_w)


def finish_block(
    tokens, router_weight, picked, probs, slot_table, token_table, back_rows, route_dot
):
    grad_sum = lax.dot_general(
        token_table, back_rows, contract_rows, preferred_element_type=jnp.float32
    )
    route_grad = lax.dot_general(
        slot_table, route_dot, contract_rows, preferred_element_type=jnp.float32
    ).reshape(probs.shape)
    inner_term = jnp.sum(probs * route_grad, axis=1, keepdims=True)
    chosen_grad = probs * (route_grad - inner_term)
    logit_grad = jnp.sum(
        jnp.where(picked, chosen_grad[:, :, None], jnp.float32(0.0)), axis=1
    ).astype(jnp.bfloat16)
    grad_tokens = (
        grad_sum
        + lax.dot_general(
            logit_grad, router_weight, contract_cols, preferred_element_type=jnp.float32
        )
    ).astype(jnp.bfloat16)
    router_part = lax.dot_general(
        tokens, logit_grad, contract_rows, preferred_element_type=jnp.float32
    )
    return (grad_tokens, router_part)


def expert_local(gate_pre, up_pre, down_matrix):
    last = (((2,), (0,)), ((), ()))
    gate_value = gate_pre.astype(jnp.float32)
    sigmoid_gate = jax.nn.sigmoid(gate_value)
    hidden = (gate_value * sigmoid_gate * up_pre.astype(jnp.float32)).astype(jnp.bfloat16)
    expert_out = lax.dot_general(
        hidden, down_matrix, last, preferred_element_type=jnp.float32
    ).astype(jnp.bfloat16)
    return hidden, expert_out


def expert_from_cot(
    cot_rows, weight_rows, gate_pre, up_pre, gate_matrix, up_matrix, down_matrix, hidden
):
    last_t = (((2,), (1,)), ((), ()))
    grid_rows = (((0, 1), (0, 1)), ((), ()))
    gate_value = gate_pre.astype(jnp.float32)
    up_value = up_pre.astype(jnp.float32)
    sigmoid_gate = jax.nn.sigmoid(gate_value)
    silu_gate = gate_value * sigmoid_gate
    scaled_cot = (
        weight_rows.astype(jnp.float32)[:, :, None] * cot_rows.astype(jnp.float32)
    ).astype(jnp.bfloat16)
    grad_hidden = lax.dot_general(
        scaled_cot, down_matrix, last_t, preferred_element_type=jnp.float32
    )
    grad_gate_pre = (
        grad_hidden * up_value * sigmoid_gate * (1.0 + gate_value * (1.0 - sigmoid_gate))
    ).astype(jnp.bfloat16)
    grad_up_pre = (grad_hidden * silu_gate).astype(jnp.bfloat16)
    grad_rows = (
        lax.dot_general(grad_gate_pre, gate_matrix, last_t, preferred_element_type=jnp.float32)
        + lax.dot_general(grad_up_pre, up_matrix, last_t, preferred_element_type=jnp.float32)
    ).astype(jnp.bfloat16)
    grad_down_w = lax.dot_general(
        hidden, scaled_cot, grid_rows, preferred_element_type=jnp.float32
    ).astype(jnp.bfloat16)
    return (grad_rows, grad_gate_pre, grad_up_pre, grad_down_w)


def body(
    tokens,
    cotangent,
    routes,
    router_weight,
    gate_saved,
    up_saved,
    gate_weight,
    up_weight,
    down_weight,
):
    experts = router_weight.shape[1]
    width = tokens.shape[1]
    capacity = gate_saved.shape[1] // experts
    outer_size = lax.axis_size("outer")
    inner_size = lax.axis_size("inner")
    devices = outer_size * inner_size
    axes = ("outer", "inner")
    picked, probs = route_probs(tokens, routes, router_weight)
    slot_table, token_table = route_tables(routes, experts, capacity)
    grid_table = token_table.reshape(experts, capacity, -1)
    probs_low = probs.astype(jnp.bfloat16).reshape(-1)
    send_weight = jnp.dot(slot_table, probs_low, preferred_element_type=jnp.float32).astype(
        jnp.bfloat16
    )
    weight_row = jnp.pad(send_weight.reshape(experts, capacity), ((0, 0), (0, width - capacity)))
    grid_cot = jnp.dot(grid_table, cotangent, preferred_element_type=jnp.float32).astype(
        jnp.bfloat16
    )
    send_cot = jnp.concatenate([grid_cot, weight_row[:, None, :]], axis=1)
    got_cot_w = lax.all_to_all(send_cot, axes, split_axis=0, concat_axis=0, tiled=True)
    gate_grid = gate_saved[0].reshape(experts, capacity, -1)
    up_grid = up_saved[0].reshape(experts, capacity, -1)
    hidden, expert_out = expert_local(gate_grid, up_grid, down_weight[0])
    got_cot_w, hidden, expert_out = lax.optimization_barrier((got_cot_w, hidden, expert_out))
    got_cot = got_cot_w[:, :capacity, :]
    got_weight = got_cot_w[:, capacity, :capacity]
    grid_tokens = jnp.dot(grid_table, tokens, preferred_element_type=jnp.float32).astype(
        jnp.bfloat16
    )
    got_cot, grid_tokens = lax.optimization_barrier((got_cot, grid_tokens))
    half = width // 2
    got_tokens_a = lax.all_to_all(
        grid_tokens[:, :, :half], axes, split_axis=0, concat_axis=0, tiled=True
    )
    cot_rows = got_cot
    grad_rows, grad_gate_pre, grad_up_pre, grad_down_w = expert_from_cot(
        cot_rows,
        got_weight,
        gate_grid,
        up_grid,
        gate_weight[0],
        up_weight[0],
        down_weight[0],
        hidden,
    )
    slot_route_dot = jnp.sum(
        cot_rows.astype(jnp.float32) * expert_out.astype(jnp.float32), axis=2
    ).astype(jnp.bfloat16)
    dot_row = jnp.pad(slot_route_dot, ((0, 0), (0, half - capacity)))[:, None, :]
    send_b = jnp.concatenate([grid_tokens[:, :, half:], dot_row], axis=1)
    got_b = lax.all_to_all(send_b, axes, split_axis=0, concat_axis=0, tiled=True)
    got_tokens_b = got_b[:, :capacity, :]
    route_dot = got_b[:, capacity, :capacity].reshape(-1)
    route_grad = lax.dot_general(
        slot_table, route_dot, contract_rows, preferred_element_type=jnp.float32
    ).reshape(probs.shape)
    inner_term = jnp.sum(probs * route_grad, axis=1, keepdims=True)
    chosen_grad = probs * (route_grad - inner_term)
    logit_grad = jnp.sum(
        jnp.where(picked, chosen_grad[:, :, None], jnp.float32(0.0)), axis=1
    ).astype(jnp.bfloat16)
    router_part = lax.dot_general(
        tokens, logit_grad, contract_rows, preferred_element_type=jnp.float32
    )
    part_rows = router_part.reshape(devices, 1, -1)
    part_rounded = lax.reduce_precision(part_rows, exponent_bits=8, mantissa_bits=7)
    part_high = part_rounded.astype(jnp.bfloat16)
    part_low = (part_rows - part_rounded).astype(jnp.bfloat16)
    send_back = jnp.concatenate([grad_rows, part_high, part_low], axis=1)
    got_back = lax.all_to_all(send_back, axes, split_axis=0, concat_axis=0, tiled=True)
    back_rows = got_back[:, :capacity, :]
    got_parts = got_back[:, capacity, :].astype(jnp.float32) + got_back[:, capacity + 1, :].astype(
        jnp.float32
    )
    chunk_sum = jnp.sum(got_parts, axis=0, keepdims=True)
    spread = jnp.broadcast_to(chunk_sum, got_parts.shape)
    got_sums = lax.all_to_all(spread, axes, split_axis=0, concat_axis=0, tiled=True)
    total_tokens = tokens.shape[0] * devices
    grad_router = got_sums.reshape(router_part.shape) * (1.0 / math.sqrt(total_tokens))
    grid_rows = (((0, 1), (0, 1)), ((), ()))

    def by_rows(pre):
        return jnp.concatenate(
            [
                lax.dot_general(got_tokens_a, pre, grid_rows, preferred_element_type=jnp.float32),
                lax.dot_general(got_tokens_b, pre, grid_rows, preferred_element_type=jnp.float32),
            ],
            axis=0,
        ).astype(jnp.bfloat16)

    grad_gate_w = by_rows(grad_gate_pre)
    grad_up_w = by_rows(grad_up_pre)
    grad_sum = lax.dot_general(
        grid_table, back_rows, (((0, 1), (0, 1)), ((), ())), preferred_element_type=jnp.float32
    )
    grad_tokens = (
        grad_sum
        + lax.dot_general(
            logit_grad, router_weight, contract_cols, preferred_element_type=jnp.float32
        )
    ).astype(jnp.bfloat16)
    return (grad_tokens, grad_gate_w[None], grad_up_w[None], grad_down_w[None], grad_router)


def solution(mesh):
    in_specs = (
        P(("outer", "inner"), None),
        P(("outer", "inner"), None),
        P(("outer", "inner"), None),
        P(),
        P(("outer", "inner"), None, None),
        P(("outer", "inner"), None, None),
        P(("outer", "inner"), None, None),
        P(("outer", "inner"), None, None),
        P(("outer", "inner"), None, None),
    )
    out_specs = (
        P(("outer", "inner"), None),
        P(("outer", "inner"), None, None),
        P(("outer", "inner"), None, None),
        P(("outer", "inner"), None, None),
        P(),
    )
    return jax.shard_map(body, mesh=mesh, in_specs=in_specs, out_specs=out_specs, check_vma=False)
```

```python
import math

import jax
import jax.numpy as jnp
from jax import lax
from jax.sharding import PartitionSpec as P

contract_rows = (((0,), (0,)), ((), ()))
contract_cols = (((1,), (1,)), ((), ()))


def route_tables(routes, experts, capacity):
    flat_routes = routes.reshape(-1)
    onehot = (flat_routes[:, None] == jnp.arange(experts, dtype=jnp.int32)[None, :]).astype(
        jnp.int32
    )
    pairs = flat_routes.shape[0]
    lower = (
        jnp.arange(pairs, dtype=jnp.int32)[:, None] > jnp.arange(pairs, dtype=jnp.int32)[None, :]
    ).astype(jnp.bfloat16)
    earlier = jnp.dot(
        lower, onehot.astype(jnp.bfloat16), preferred_element_type=jnp.float32
    ).astype(jnp.int32)
    position = jnp.sum(earlier * onehot, axis=1)
    target = flat_routes * capacity + position
    slot_table = (
        jnp.arange(experts * capacity, dtype=jnp.int32)[:, None] == target[None, :]
    ).astype(jnp.bfloat16)
    pair_token = jnp.arange(pairs, dtype=jnp.int32) // routes.shape[1]
    token_code = jnp.stack(
        [pair_token // 16, pair_token % 16, jnp.ones_like(pair_token)], axis=1
    ).astype(jnp.bfloat16)
    slot_code = jnp.dot(slot_table, token_code, preferred_element_type=jnp.float32)
    slot_token = (slot_code[:, 0] * 16.0 + slot_code[:, 1]).astype(jnp.int32)
    filled = slot_code[:, 2] > 0.5
    token_table = (
        (slot_token[:, None] == jnp.arange(routes.shape[0], dtype=jnp.int32)[None, :])
        & filled[:, None]
    ).astype(jnp.bfloat16)
    return (slot_table, token_table)


def route_probs(tokens, routes, router_weight):
    router_logits = jnp.dot(tokens, router_weight, preferred_element_type=jnp.float32)
    picked = (
        routes[:, :, None] == jnp.arange(router_weight.shape[1], dtype=jnp.int32)[None, None, :]
    )
    chosen = jnp.sum(jnp.where(picked, router_logits[:, None, :], jnp.float32(0.0)), axis=2)
    exp_terms = jnp.exp(chosen)
    return (picked, exp_terms / jnp.sum(exp_terms, axis=1, keepdims=True))


def dispatch_block(tokens, cotangent, routes, router_weight, capacity):
    picked, probs = route_probs(tokens, routes, router_weight)
    slot_table, token_table = route_tables(routes, router_weight.shape[1], capacity)
    send_tokens = jnp.dot(token_table, tokens, preferred_element_type=jnp.float32).astype(
        jnp.bfloat16
    )
    send_cot = jnp.dot(token_table, cotangent, preferred_element_type=jnp.float32).astype(
        jnp.bfloat16
    )
    probs_low = probs.astype(jnp.bfloat16).reshape(-1)
    send_weight = jnp.dot(slot_table, probs_low, preferred_element_type=jnp.float32).astype(
        jnp.bfloat16
    )
    return (picked, probs, slot_table, token_table, send_tokens, send_cot, send_weight)


def slot_dot(cot_rows, out_rows):
    return jnp.sum(cot_rows.astype(jnp.float32) * out_rows.astype(jnp.float32), axis=1).astype(
        jnp.bfloat16
    )


def expert_backward(
    input_rows, cot_rows, weight_rows, gate_pre, up_pre, gate_matrix, up_matrix, down_matrix
):
    gate_value = gate_pre.astype(jnp.float32)
    up_value = up_pre.astype(jnp.float32)
    sigmoid_gate = jax.nn.sigmoid(gate_value)
    silu_gate = gate_value * sigmoid_gate
    hidden = (silu_gate * up_value).astype(jnp.bfloat16)
    expert_out = jnp.dot(hidden, down_matrix, preferred_element_type=jnp.float32).astype(
        jnp.bfloat16
    )
    scaled_cot = (weight_rows.astype(jnp.float32)[:, None] * cot_rows.astype(jnp.float32)).astype(
        jnp.bfloat16
    )
    grad_hidden = lax.dot_general(
        scaled_cot, down_matrix, contract_cols, preferred_element_type=jnp.float32
    )
    grad_gate_pre = (
        grad_hidden * up_value * sigmoid_gate * (1.0 + gate_value * (1.0 - sigmoid_gate))
    ).astype(jnp.bfloat16)
    grad_up_pre = (grad_hidden * silu_gate).astype(jnp.bfloat16)
    grad_rows = (
        lax.dot_general(
            grad_gate_pre, gate_matrix, contract_cols, preferred_element_type=jnp.float32
        )
        + lax.dot_general(grad_up_pre, up_matrix, contract_cols, preferred_element_type=jnp.float32)
    ).astype(jnp.bfloat16)
    grad_gate_w = lax.dot_general(
        input_rows, grad_gate_pre, contract_rows, preferred_element_type=jnp.float32
    ).astype(jnp.bfloat16)
    grad_up_w = lax.dot_general(
        input_rows, grad_up_pre, contract_rows, preferred_element_type=jnp.float32
    ).astype(jnp.bfloat16)
    grad_down_w = lax.dot_general(
        hidden, scaled_cot, contract_rows, preferred_element_type=jnp.float32
    ).astype(jnp.bfloat16)
    return (grad_rows, expert_out, grad_gate_w, grad_up_w, grad_down_w)


def finish_block(
    tokens, router_weight, picked, probs, slot_table, token_table, back_rows, route_dot
):
    grad_sum = lax.dot_general(
        token_table, back_rows, contract_rows, preferred_element_type=jnp.float32
    )
    route_grad = lax.dot_general(
        slot_table, route_dot, contract_rows, preferred_element_type=jnp.float32
    ).reshape(probs.shape)
    inner_term = jnp.sum(probs * route_grad, axis=1, keepdims=True)
    chosen_grad = probs * (route_grad - inner_term)
    logit_grad = jnp.sum(
        jnp.where(picked, chosen_grad[:, :, None], jnp.float32(0.0)), axis=1
    ).astype(jnp.bfloat16)
    grad_tokens = (
        grad_sum
        + lax.dot_general(
            logit_grad, router_weight, contract_cols, preferred_element_type=jnp.float32
        )
    ).astype(jnp.bfloat16)
    router_part = lax.dot_general(
        tokens, logit_grad, contract_rows, preferred_element_type=jnp.float32
    )
    return (grad_tokens, router_part)


def expert_local(gate_pre, up_pre, down_matrix):
    last = (((2,), (0,)), ((), ()))
    gate_value = gate_pre.astype(jnp.float32)
    sigmoid_gate = jax.nn.sigmoid(gate_value)
    hidden = (gate_value * sigmoid_gate * up_pre.astype(jnp.float32)).astype(jnp.bfloat16)
    expert_out = lax.dot_general(
        hidden, down_matrix, last, preferred_element_type=jnp.float32
    ).astype(jnp.bfloat16)
    return hidden, expert_out


def expert_from_cot(
    cot_rows, weight_rows, gate_pre, up_pre, gate_matrix, up_matrix, down_matrix, hidden
):
    last_t = (((2,), (1,)), ((), ()))
    grid_rows = (((0, 1), (0, 1)), ((), ()))
    gate_value = gate_pre.astype(jnp.float32)
    up_value = up_pre.astype(jnp.float32)
    sigmoid_gate = jax.nn.sigmoid(gate_value)
    silu_gate = gate_value * sigmoid_gate
    scaled_cot = (
        weight_rows.astype(jnp.float32)[:, :, None] * cot_rows.astype(jnp.float32)
    ).astype(jnp.bfloat16)
    grad_hidden = lax.dot_general(
        scaled_cot, down_matrix, last_t, preferred_element_type=jnp.float32
    )
    grad_gate_pre = (
        grad_hidden * up_value * sigmoid_gate * (1.0 + gate_value * (1.0 - sigmoid_gate))
    ).astype(jnp.bfloat16)
    grad_up_pre = (grad_hidden * silu_gate).astype(jnp.bfloat16)
    grad_rows = (
        lax.dot_general(grad_gate_pre, gate_matrix, last_t, preferred_element_type=jnp.float32)
        + lax.dot_general(grad_up_pre, up_matrix, last_t, preferred_element_type=jnp.float32)
    ).astype(jnp.bfloat16)
    grad_down_w = lax.dot_general(
        hidden, scaled_cot, grid_rows, preferred_element_type=jnp.float32
    ).astype(jnp.bfloat16)
    return (grad_rows, grad_gate_pre, grad_up_pre, grad_down_w)


def body(
    tokens,
    cotangent,
    routes,
    router_weight,
    gate_saved,
    up_saved,
    gate_weight,
    up_weight,
    down_weight,
):
    experts = router_weight.shape[1]
    width = tokens.shape[1]
    capacity = gate_saved.shape[1] // experts
    outer_size = lax.axis_size("outer")
    inner_size = lax.axis_size("inner")
    devices = outer_size * inner_size
    axes = ("outer", "inner")
    picked, probs = route_probs(tokens, routes, router_weight)
    slot_table, token_table = route_tables(routes, experts, capacity)
    grid_table = token_table.reshape(experts, capacity, -1)
    probs_low = probs.astype(jnp.bfloat16).reshape(-1)
    send_weight = jnp.dot(slot_table, probs_low, preferred_element_type=jnp.float32).astype(
        jnp.bfloat16
    )
    weight_row = jnp.pad(send_weight.reshape(experts, capacity), ((0, 0), (0, width - capacity)))
    grid_cot = jnp.dot(grid_table, cotangent, preferred_element_type=jnp.float32).astype(
        jnp.bfloat16
    )
    send_cot = jnp.concatenate([grid_cot, weight_row[:, None, :]], axis=1)
    got_cot_w = lax.all_to_all(send_cot, axes, split_axis=0, concat_axis=0, tiled=True)
    gate_grid = gate_saved[0].reshape(experts, capacity, -1)
    up_grid = up_saved[0].reshape(experts, capacity, -1)
    hidden, expert_out = expert_local(gate_grid, up_grid, down_weight[0])
    got_cot_w, hidden, expert_out = lax.optimization_barrier((got_cot_w, hidden, expert_out))
    got_cot = got_cot_w[:, :capacity, :]
    got_weight = got_cot_w[:, capacity, :capacity]
    grid_tokens = jnp.dot(grid_table, tokens, preferred_element_type=jnp.float32).astype(
        jnp.bfloat16
    )
    got_cot, grid_tokens = lax.optimization_barrier((got_cot, grid_tokens))
    half = width // 2
    got_tokens_a = lax.all_to_all(
        grid_tokens[:, :, :half], axes, split_axis=0, concat_axis=0, tiled=True
    )
    cot_rows = got_cot
    grad_rows, grad_gate_pre, grad_up_pre, grad_down_w = expert_from_cot(
        cot_rows,
        got_weight,
        gate_grid,
        up_grid,
        gate_weight[0],
        up_weight[0],
        down_weight[0],
        hidden,
    )
    slot_route_dot = jnp.sum(
        cot_rows.astype(jnp.float32) * expert_out.astype(jnp.float32), axis=2
    ).astype(jnp.bfloat16)
    dot_row = jnp.pad(slot_route_dot, ((0, 0), (0, half - capacity)))[:, None, :]
    send_b = jnp.concatenate([grid_tokens[:, :, half:], dot_row], axis=1)
    got_b = lax.all_to_all(send_b, axes, split_axis=0, concat_axis=0, tiled=True)
    got_tokens_b = got_b[:, :capacity, :]
    route_dot = got_b[:, capacity, :capacity].reshape(-1)
    route_grad = lax.dot_general(
        slot_table, route_dot, contract_rows, preferred_element_type=jnp.float32
    ).reshape(probs.shape)
    inner_term = jnp.sum(probs * route_grad, axis=1, keepdims=True)
    chosen_grad = probs * (route_grad - inner_term)
    logit_grad = jnp.sum(
        jnp.where(picked, chosen_grad[:, :, None], jnp.float32(0.0)), axis=1
    ).astype(jnp.bfloat16)
    router_part = lax.dot_general(
        tokens, logit_grad, contract_rows, preferred_element_type=jnp.float32
    )
    part_rows = router_part.reshape(devices, 1, -1)
    part_rounded = lax.reduce_precision(part_rows, exponent_bits=8, mantissa_bits=7)
    part_high = part_rounded.astype(jnp.bfloat16)
    part_low = (part_rows - part_rounded).astype(jnp.bfloat16)
    send_back = jnp.concatenate([grad_rows, part_high, part_low], axis=1)
    got_back = lax.all_to_all(send_back, axes, split_axis=0, concat_axis=0, tiled=True)
    back_rows = got_back[:, :capacity, :]
    got_parts = got_back[:, capacity, :].astype(jnp.float32) + got_back[:, capacity + 1, :].astype(
        jnp.float32
    )
    chunk_sum = jnp.sum(got_parts, axis=0, keepdims=True)
    spread = jnp.broadcast_to(chunk_sum, got_parts.shape)
    got_sums = lax.all_to_all(spread, axes, split_axis=0, concat_axis=0, tiled=True)
    total_tokens = tokens.shape[0] * devices
    grad_router = got_sums.reshape(router_part.shape) * (1.0 / math.sqrt(total_tokens))
    grid_rows = (((0, 1), (0, 1)), ((), ()))

    def by_rows(pre):
        return jnp.concatenate(
            [
                lax.dot_general(got_tokens_a, pre, grid_rows, preferred_element_type=jnp.float32),
                lax.dot_general(got_tokens_b, pre, grid_rows, preferred_element_type=jnp.float32),
            ],
            axis=0,
        ).astype(jnp.bfloat16)

    grad_gate_w = by_rows(grad_gate_pre)
    grad_up_w = by_rows(grad_up_pre)
    grad_sum = lax.dot_general(
        grid_table, back_rows, (((0, 1), (0, 1)), ((), ())), preferred_element_type=jnp.float32
    )
    grad_tokens = (
        grad_sum
        + lax.dot_general(
            logit_grad, router_weight, contract_cols, preferred_element_type=jnp.float32
        )
    ).astype(jnp.bfloat16)
    return (grad_tokens, grad_gate_w[None], grad_up_w[None], grad_down_w[None], grad_router)


def solution(mesh):
    in_specs = (
        P(("outer", "inner"), None),
        P(("outer", "inner"), None),
        P(("outer", "inner"), None),
        P(),
        P(("outer", "inner"), None, None),
        P(("outer", "inner"), None, None),
        P(("outer", "inner"), None, None),
        P(("outer", "inner"), None, None),
        P(("outer", "inner"), None, None),
    )
    out_specs = (
        P(("outer", "inner"), None),
        P(("outer", "inner"), None, None),
        P(("outer", "inner"), None, None),
        P(("outer", "inner"), None, None),
        P(),
    )
    return jax.shard_map(body, mesh=mesh, in_specs=in_specs, out_specs=out_specs, check_vma=False)
```

```python
import math

import jax
import jax.numpy as jnp
from jax import lax
from jax.sharding import PartitionSpec as P

contract_rows = (((0,), (0,)), ((), ()))
contract_cols = (((1,), (1,)), ((), ()))


def route_tables(routes, experts, capacity):
    flat_routes = routes.reshape(-1)
    onehot = (flat_routes[:, None] == jnp.arange(experts, dtype=jnp.int32)[None, :]).astype(
        jnp.int32
    )
    pairs = flat_routes.shape[0]
    lower = (
        jnp.arange(pairs, dtype=jnp.int32)[:, None] > jnp.arange(pairs, dtype=jnp.int32)[None, :]
    ).astype(jnp.bfloat16)
    earlier = jnp.dot(
        lower, onehot.astype(jnp.bfloat16), preferred_element_type=jnp.float32
    ).astype(jnp.int32)
    position = jnp.sum(earlier * onehot, axis=1)
    target = flat_routes * capacity + position
    slot_table = (
        jnp.arange(experts * capacity, dtype=jnp.int32)[:, None] == target[None, :]
    ).astype(jnp.bfloat16)
    pair_token = jnp.arange(pairs, dtype=jnp.int32) // routes.shape[1]
    token_code = jnp.stack(
        [pair_token // 16, pair_token % 16, jnp.ones_like(pair_token)], axis=1
    ).astype(jnp.bfloat16)
    slot_code = jnp.dot(slot_table, token_code, preferred_element_type=jnp.float32)
    slot_token = (slot_code[:, 0] * 16.0 + slot_code[:, 1]).astype(jnp.int32)
    filled = slot_code[:, 2] > 0.5
    token_table = (
        (slot_token[:, None] == jnp.arange(routes.shape[0], dtype=jnp.int32)[None, :])
        & filled[:, None]
    ).astype(jnp.bfloat16)
    return (slot_table, token_table)


def route_probs(tokens, routes, router_weight):
    router_logits = jnp.dot(tokens, router_weight, preferred_element_type=jnp.float32)
    picked = (
        routes[:, :, None] == jnp.arange(router_weight.shape[1], dtype=jnp.int32)[None, None, :]
    )
    chosen = jnp.sum(jnp.where(picked, router_logits[:, None, :], jnp.float32(0.0)), axis=2)
    exp_terms = jnp.exp(chosen)
    return (picked, exp_terms / jnp.sum(exp_terms, axis=1, keepdims=True))


def dispatch_block(tokens, cotangent, routes, router_weight, capacity):
    picked, probs = route_probs(tokens, routes, router_weight)
    slot_table, token_table = route_tables(routes, router_weight.shape[1], capacity)
    send_tokens = jnp.dot(token_table, tokens, preferred_element_type=jnp.float32).astype(
        jnp.bfloat16
    )
    send_cot = jnp.dot(token_table, cotangent, preferred_element_type=jnp.float32).astype(
        jnp.bfloat16
    )
    probs_low = probs.astype(jnp.bfloat16).reshape(-1)
    send_weight = jnp.dot(slot_table, probs_low, preferred_element_type=jnp.float32).astype(
        jnp.bfloat16
    )
    return (picked, probs, slot_table, token_table, send_tokens, send_cot, send_weight)


def slot_dot(cot_rows, out_rows):
    return jnp.sum(cot_rows.astype(jnp.float32) * out_rows.astype(jnp.float32), axis=1).astype(
        jnp.bfloat16
    )


def expert_backward(
    input_rows, cot_rows, weight_rows, gate_pre, up_pre, gate_matrix, up_matrix, down_matrix
):
    gate_value = gate_pre.astype(jnp.float32)
    up_value = up_pre.astype(jnp.float32)
    sigmoid_gate = jax.nn.sigmoid(gate_value)
    silu_gate = gate_value * sigmoid_gate
    hidden = (silu_gate * up_value).astype(jnp.bfloat16)
    expert_out = jnp.dot(hidden, down_matrix, preferred_element_type=jnp.float32).astype(
        jnp.bfloat16
    )
    scaled_cot = (weight_rows.astype(jnp.float32)[:, None] * cot_rows.astype(jnp.float32)).astype(
        jnp.bfloat16
    )
    grad_hidden = lax.dot_general(
        scaled_cot, down_matrix, contract_cols, preferred_element_type=jnp.float32
    )
    grad_gate_pre = (
        grad_hidden * up_value * sigmoid_gate * (1.0 + gate_value * (1.0 - sigmoid_gate))
    ).astype(jnp.bfloat16)
    grad_up_pre = (grad_hidden * silu_gate).astype(jnp.bfloat16)
    grad_rows = (
        lax.dot_general(
            grad_gate_pre, gate_matrix, contract_cols, preferred_element_type=jnp.float32
        )
        + lax.dot_general(grad_up_pre, up_matrix, contract_cols, preferred_element_type=jnp.float32)
    ).astype(jnp.bfloat16)
    grad_gate_w = lax.dot_general(
        input_rows, grad_gate_pre, contract_rows, preferred_element_type=jnp.float32
    ).astype(jnp.bfloat16)
    grad_up_w = lax.dot_general(
        input_rows, grad_up_pre, contract_rows, preferred_element_type=jnp.float32
    ).astype(jnp.bfloat16)
    grad_down_w = lax.dot_general(
        hidden, scaled_cot, contract_rows, preferred_element_type=jnp.float32
    ).astype(jnp.bfloat16)
    return (grad_rows, expert_out, grad_gate_w, grad_up_w, grad_down_w)


def finish_block(
    tokens, router_weight, picked, probs, slot_table, token_table, back_rows, route_dot
):
    grad_sum = lax.dot_general(
        token_table, back_rows, contract_rows, preferred_element_type=jnp.float32
    )
    route_grad = lax.dot_general(
        slot_table, route_dot, contract_rows, preferred_element_type=jnp.float32
    ).reshape(probs.shape)
    inner_term = jnp.sum(probs * route_grad, axis=1, keepdims=True)
    chosen_grad = probs * (route_grad - inner_term)
    logit_grad = jnp.sum(
        jnp.where(picked, chosen_grad[:, :, None], jnp.float32(0.0)), axis=1
    ).astype(jnp.bfloat16)
    grad_tokens = (
        grad_sum
        + lax.dot_general(
            logit_grad, router_weight, contract_cols, preferred_element_type=jnp.float32
        )
    ).astype(jnp.bfloat16)
    router_part = lax.dot_general(
        tokens, logit_grad, contract_rows, preferred_element_type=jnp.float32
    )
    return (grad_tokens, router_part)


def expert_local(gate_pre, up_pre, down_matrix):
    last = (((2,), (0,)), ((), ()))
    gate_value = gate_pre.astype(jnp.float32)
    sigmoid_gate = jax.nn.sigmoid(gate_value)
    hidden = (gate_value * sigmoid_gate * up_pre.astype(jnp.float32)).astype(jnp.bfloat16)
    expert_out = lax.dot_general(
        hidden, down_matrix, last, preferred_element_type=jnp.float32
    ).astype(jnp.bfloat16)
    return hidden, expert_out


def expert_from_cot(
    cot_rows, weight_rows, gate_pre, up_pre, gate_matrix, up_matrix, down_matrix, hidden
):
    last_t = (((2,), (1,)), ((), ()))
    grid_rows = (((0, 1), (0, 1)), ((), ()))
    gate_value = gate_pre.astype(jnp.float32)
    up_value = up_pre.astype(jnp.float32)
    sigmoid_gate = jax.nn.sigmoid(gate_value)
    silu_gate = gate_value * sigmoid_gate
    scaled_cot = (
        weight_rows.astype(jnp.float32)[:, :, None] * cot_rows.astype(jnp.float32)
    ).astype(jnp.bfloat16)
    grad_hidden = lax.dot_general(
        scaled_cot, down_matrix, last_t, preferred_element_type=jnp.float32
    )
    grad_gate_pre = (
        grad_hidden * up_value * sigmoid_gate * (1.0 + gate_value * (1.0 - sigmoid_gate))
    ).astype(jnp.bfloat16)
    grad_up_pre = (grad_hidden * silu_gate).astype(jnp.bfloat16)
    grad_rows = (
        lax.dot_general(grad_gate_pre, gate_matrix, last_t, preferred_element_type=jnp.float32)
        + lax.dot_general(grad_up_pre, up_matrix, last_t, preferred_element_type=jnp.float32)
    ).astype(jnp.bfloat16)
    grad_down_w = lax.dot_general(
        hidden, scaled_cot, grid_rows, preferred_element_type=jnp.float32
    ).astype(jnp.bfloat16)
    return (grad_rows, grad_gate_pre, grad_up_pre, grad_down_w)


def body(
    tokens,
    cotangent,
    routes,
    router_weight,
    gate_saved,
    up_saved,
    gate_weight,
    up_weight,
    down_weight,
):
    experts = router_weight.shape[1]
    width = tokens.shape[1]
    capacity = gate_saved.shape[1] // experts
    outer_size = lax.axis_size("outer")
    inner_size = lax.axis_size("inner")
    devices = outer_size * inner_size
    axes = ("outer", "inner")
    picked, probs = route_probs(tokens, routes, router_weight)
    slot_table, token_table = route_tables(routes, experts, capacity)
    grid_table = token_table.reshape(experts, capacity, -1)
    probs_low = probs.astype(jnp.bfloat16).reshape(-1)
    send_weight = jnp.dot(slot_table, probs_low, preferred_element_type=jnp.float32).astype(
        jnp.bfloat16
    )
    weight_rows = jnp.pad(send_weight.reshape(experts, capacity), ((0, 0), (0, width - capacity)))
    cot_ext = jnp.concatenate([cotangent, weight_rows], axis=0)
    pick_weight = (
        jnp.arange(experts, dtype=jnp.int32)[:, None] == jnp.arange(experts, dtype=jnp.int32)[None, :]
    ).astype(jnp.bfloat16)
    table_ext = jnp.concatenate(
        [
            jnp.pad(grid_table, ((0, 0), (0, 0), (0, experts))),
            jnp.pad(pick_weight, ((0, 0), (grid_table.shape[2], 0)))[:, None, :],
        ],
        axis=1,
    )
    send_cot = jnp.dot(table_ext, cot_ext, preferred_element_type=jnp.float32).astype(jnp.bfloat16)
    got_cot_w = lax.all_to_all(send_cot, axes, split_axis=0, concat_axis=0, tiled=True)
    gate_grid = gate_saved[0].reshape(experts, capacity, -1)
    up_grid = up_saved[0].reshape(experts, capacity, -1)
    hidden, expert_out = expert_local(gate_grid, up_grid, down_weight[0])
    got_cot_w, hidden, expert_out = lax.optimization_barrier((got_cot_w, hidden, expert_out))
    got_cot = got_cot_w[:, :capacity, :]
    got_weight = got_cot_w[:, capacity, :capacity]
    grid_tokens = jnp.dot(grid_table, tokens, preferred_element_type=jnp.float32).astype(
        jnp.bfloat16
    )
    got_cot, grid_tokens = lax.optimization_barrier((got_cot, grid_tokens))
    half = width // 2
    got_tokens_a = lax.all_to_all(
        grid_tokens[:, :, :half], axes, split_axis=0, concat_axis=0, tiled=True
    )
    cot_rows = got_cot
    grad_rows, grad_gate_pre, grad_up_pre, grad_down_w = expert_from_cot(
        cot_rows,
        got_weight,
        gate_grid,
        up_grid,
        gate_weight[0],
        up_weight[0],
        down_weight[0],
        hidden,
    )
    slot_route_dot = jnp.sum(
        cot_rows.astype(jnp.float32) * expert_out.astype(jnp.float32), axis=2
    ).astype(jnp.bfloat16)
    dot_row = jnp.pad(slot_route_dot, ((0, 0), (0, half - capacity)))[:, None, :]
    send_b = jnp.concatenate([grid_tokens[:, :, half:], dot_row], axis=1)
    got_b = lax.all_to_all(send_b, axes, split_axis=0, concat_axis=0, tiled=True)
    got_tokens_b = got_b[:, :capacity, :]
    route_dot = got_b[:, capacity, :capacity].reshape(-1)
    route_grad = lax.dot_general(
        slot_table, route_dot, contract_rows, preferred_element_type=jnp.float32
    ).reshape(probs.shape)
    inner_term = jnp.sum(probs * route_grad, axis=1, keepdims=True)
    chosen_grad = probs * (route_grad - inner_term)
    logit_grad = jnp.sum(
        jnp.where(picked, chosen_grad[:, :, None], jnp.float32(0.0)), axis=1
    ).astype(jnp.bfloat16)
    router_part = lax.dot_general(
        tokens, logit_grad, contract_rows, preferred_element_type=jnp.float32
    )
    part_rows = router_part.reshape(devices, 1, -1)
    part_rounded = lax.reduce_precision(part_rows, exponent_bits=8, mantissa_bits=7)
    part_high = part_rounded.astype(jnp.bfloat16)
    part_low = (part_rows - part_rounded).astype(jnp.bfloat16)
    send_back = jnp.concatenate([grad_rows, part_high, part_low], axis=1)
    got_back = lax.all_to_all(send_back, axes, split_axis=0, concat_axis=0, tiled=True)
    back_rows = got_back[:, :capacity, :]
    got_parts = got_back[:, capacity, :].astype(jnp.float32) + got_back[:, capacity + 1, :].astype(
        jnp.float32
    )
    chunk_sum = jnp.sum(got_parts, axis=0, keepdims=True)
    spread = jnp.broadcast_to(chunk_sum, got_parts.shape)
    got_sums = lax.all_to_all(spread, axes, split_axis=0, concat_axis=0, tiled=True)
    total_tokens = tokens.shape[0] * devices
    grad_router = got_sums.reshape(router_part.shape) * (1.0 / math.sqrt(total_tokens))
    grid_rows = (((0, 1), (0, 1)), ((), ()))

    def by_rows(pre):
        return jnp.concatenate(
            [
                lax.dot_general(got_tokens_a, pre, grid_rows, preferred_element_type=jnp.float32),
                lax.dot_general(got_tokens_b, pre, grid_rows, preferred_element_type=jnp.float32),
            ],
            axis=0,
        ).astype(jnp.bfloat16)

    grad_gate_w = by_rows(grad_gate_pre)
    grad_up_w = by_rows(grad_up_pre)
    grad_sum = lax.dot_general(
        grid_table, back_rows, (((0, 1), (0, 1)), ((), ())), preferred_element_type=jnp.float32
    )
    grad_tokens = (
        grad_sum
        + lax.dot_general(
            logit_grad, router_weight, contract_cols, preferred_element_type=jnp.float32
        )
    ).astype(jnp.bfloat16)
    return (grad_tokens, grad_gate_w[None], grad_up_w[None], grad_down_w[None], grad_router)


def solution(mesh):
    in_specs = (
        P(("outer", "inner"), None),
        P(("outer", "inner"), None),
        P(("outer", "inner"), None),
        P(),
        P(("outer", "inner"), None, None),
        P(("outer", "inner"), None, None),
        P(("outer", "inner"), None, None),
        P(("outer", "inner"), None, None),
        P(("outer", "inner"), None, None),
    )
    out_specs = (
        P(("outer", "inner"), None),
        P(("outer", "inner"), None, None),
        P(("outer", "inner"), None, None),
        P(("outer", "inner"), None, None),
        P(),
    )
    return jax.shard_map(body, mesh=mesh, in_specs=in_specs, out_specs=out_specs, check_vma=False)
```

```python
import math

import jax
import jax.numpy as jnp
from jax import lax
from jax.sharding import PartitionSpec as P

contract_rows = (((0,), (0,)), ((), ()))
contract_cols = (((1,), (1,)), ((), ()))


def route_tables(routes, experts, capacity):
    flat_routes = routes.reshape(-1)
    onehot = (flat_routes[:, None] == jnp.arange(experts, dtype=jnp.int32)[None, :]).astype(
        jnp.int32
    )
    pairs = flat_routes.shape[0]
    lower = (
        jnp.arange(pairs, dtype=jnp.int32)[:, None] > jnp.arange(pairs, dtype=jnp.int32)[None, :]
    ).astype(jnp.bfloat16)
    earlier = jnp.dot(
        lower, onehot.astype(jnp.bfloat16), preferred_element_type=jnp.float32
    ).astype(jnp.int32)
    position = jnp.sum(earlier * onehot, axis=1)
    target = flat_routes * capacity + position
    slot_table = (
        jnp.arange(experts * capacity, dtype=jnp.int32)[:, None] == target[None, :]
    ).astype(jnp.bfloat16)
    pair_token = jnp.arange(pairs, dtype=jnp.int32) // routes.shape[1]
    token_code = jnp.stack(
        [pair_token // 16, pair_token % 16, jnp.ones_like(pair_token)], axis=1
    ).astype(jnp.bfloat16)
    slot_code = jnp.dot(slot_table, token_code, preferred_element_type=jnp.float32)
    slot_token = (slot_code[:, 0] * 16.0 + slot_code[:, 1]).astype(jnp.int32)
    filled = slot_code[:, 2] > 0.5
    token_table = (
        (slot_token[:, None] == jnp.arange(routes.shape[0], dtype=jnp.int32)[None, :])
        & filled[:, None]
    ).astype(jnp.bfloat16)
    return (slot_table, token_table)


def route_probs(tokens, routes, router_weight):
    router_logits = jnp.dot(tokens, router_weight, preferred_element_type=jnp.float32)
    picked = (
        routes[:, :, None] == jnp.arange(router_weight.shape[1], dtype=jnp.int32)[None, None, :]
    )
    chosen = jnp.sum(jnp.where(picked, router_logits[:, None, :], jnp.float32(0.0)), axis=2)
    exp_terms = jnp.exp(chosen)
    return (picked, exp_terms / jnp.sum(exp_terms, axis=1, keepdims=True))


def dispatch_block(tokens, cotangent, routes, router_weight, capacity):
    picked, probs = route_probs(tokens, routes, router_weight)
    slot_table, token_table = route_tables(routes, router_weight.shape[1], capacity)
    send_tokens = jnp.dot(token_table, tokens, preferred_element_type=jnp.float32).astype(
        jnp.bfloat16
    )
    send_cot = jnp.dot(token_table, cotangent, preferred_element_type=jnp.float32).astype(
        jnp.bfloat16
    )
    probs_low = probs.astype(jnp.bfloat16).reshape(-1)
    send_weight = jnp.dot(slot_table, probs_low, preferred_element_type=jnp.float32).astype(
        jnp.bfloat16
    )
    return (picked, probs, slot_table, token_table, send_tokens, send_cot, send_weight)


def slot_dot(cot_rows, out_rows):
    return jnp.sum(cot_rows.astype(jnp.float32) * out_rows.astype(jnp.float32), axis=1).astype(
        jnp.bfloat16
    )


def expert_backward(
    input_rows, cot_rows, weight_rows, gate_pre, up_pre, gate_matrix, up_matrix, down_matrix
):
    gate_value = gate_pre.astype(jnp.float32)
    up_value = up_pre.astype(jnp.float32)
    sigmoid_gate = jax.nn.sigmoid(gate_value)
    silu_gate = gate_value * sigmoid_gate
    hidden = (silu_gate * up_value).astype(jnp.bfloat16)
    expert_out = jnp.dot(hidden, down_matrix, preferred_element_type=jnp.float32).astype(
        jnp.bfloat16
    )
    scaled_cot = (weight_rows.astype(jnp.float32)[:, None] * cot_rows.astype(jnp.float32)).astype(
        jnp.bfloat16
    )
    grad_hidden = lax.dot_general(
        scaled_cot, down_matrix, contract_cols, preferred_element_type=jnp.float32
    )
    grad_gate_pre = (
        grad_hidden * up_value * sigmoid_gate * (1.0 + gate_value * (1.0 - sigmoid_gate))
    ).astype(jnp.bfloat16)
    grad_up_pre = (grad_hidden * silu_gate).astype(jnp.bfloat16)
    grad_rows = (
        lax.dot_general(
            grad_gate_pre, gate_matrix, contract_cols, preferred_element_type=jnp.float32
        )
        + lax.dot_general(grad_up_pre, up_matrix, contract_cols, preferred_element_type=jnp.float32)
    ).astype(jnp.bfloat16)
    grad_gate_w = lax.dot_general(
        input_rows, grad_gate_pre, contract_rows, preferred_element_type=jnp.float32
    ).astype(jnp.bfloat16)
    grad_up_w = lax.dot_general(
        input_rows, grad_up_pre, contract_rows, preferred_element_type=jnp.float32
    ).astype(jnp.bfloat16)
    grad_down_w = lax.dot_general(
        hidden, scaled_cot, contract_rows, preferred_element_type=jnp.float32
    ).astype(jnp.bfloat16)
    return (grad_rows, expert_out, grad_gate_w, grad_up_w, grad_down_w)


def finish_block(
    tokens, router_weight, picked, probs, slot_table, token_table, back_rows, route_dot
):
    grad_sum = lax.dot_general(
        token_table, back_rows, contract_rows, preferred_element_type=jnp.float32
    )
    route_grad = lax.dot_general(
        slot_table, route_dot, contract_rows, preferred_element_type=jnp.float32
    ).reshape(probs.shape)
    inner_term = jnp.sum(probs * route_grad, axis=1, keepdims=True)
    chosen_grad = probs * (route_grad - inner_term)
    logit_grad = jnp.sum(
        jnp.where(picked, chosen_grad[:, :, None], jnp.float32(0.0)), axis=1
    ).astype(jnp.bfloat16)
    grad_tokens = (
        grad_sum
        + lax.dot_general(
            logit_grad, router_weight, contract_cols, preferred_element_type=jnp.float32
        )
    ).astype(jnp.bfloat16)
    router_part = lax.dot_general(
        tokens, logit_grad, contract_rows, preferred_element_type=jnp.float32
    )
    return (grad_tokens, router_part)


def expert_local(gate_pre, up_pre, down_matrix):
    last = (((2,), (0,)), ((), ()))
    gate_value = gate_pre.astype(jnp.float32)
    sigmoid_gate = jax.nn.sigmoid(gate_value)
    hidden = (gate_value * sigmoid_gate * up_pre.astype(jnp.float32)).astype(jnp.bfloat16)
    expert_out = lax.dot_general(
        hidden, down_matrix, last, preferred_element_type=jnp.float32
    ).astype(jnp.bfloat16)
    return hidden, expert_out


def expert_from_cot(
    cot_rows, weight_rows, gate_pre, up_pre, gate_matrix, up_matrix, down_matrix, hidden
):
    last_t = (((2,), (1,)), ((), ()))
    grid_rows = (((0, 1), (0, 1)), ((), ()))
    gate_value = gate_pre.astype(jnp.float32)
    up_value = up_pre.astype(jnp.float32)
    sigmoid_gate = jax.nn.sigmoid(gate_value)
    silu_gate = gate_value * sigmoid_gate
    scaled_cot = (
        weight_rows.astype(jnp.float32)[:, :, None] * cot_rows.astype(jnp.float32)
    ).astype(jnp.bfloat16)
    grad_hidden = lax.dot_general(
        scaled_cot, down_matrix, last_t, preferred_element_type=jnp.float32
    )
    grad_gate_pre = (
        grad_hidden * up_value * sigmoid_gate * (1.0 + gate_value * (1.0 - sigmoid_gate))
    ).astype(jnp.bfloat16)
    grad_up_pre = (grad_hidden * silu_gate).astype(jnp.bfloat16)
    grad_rows = (
        lax.dot_general(grad_gate_pre, gate_matrix, last_t, preferred_element_type=jnp.float32)
        + lax.dot_general(grad_up_pre, up_matrix, last_t, preferred_element_type=jnp.float32)
    ).astype(jnp.bfloat16)
    grad_down_w = lax.dot_general(
        hidden, scaled_cot, grid_rows, preferred_element_type=jnp.float32
    ).astype(jnp.bfloat16)
    return (grad_rows, grad_gate_pre, grad_up_pre, grad_down_w)


def body(
    tokens,
    cotangent,
    routes,
    router_weight,
    gate_saved,
    up_saved,
    gate_weight,
    up_weight,
    down_weight,
):
    experts = router_weight.shape[1]
    width = tokens.shape[1]
    capacity = gate_saved.shape[1] // experts
    outer_size = lax.axis_size("outer")
    inner_size = lax.axis_size("inner")
    devices = outer_size * inner_size
    axes = ("outer", "inner")
    picked, probs = route_probs(tokens, routes, router_weight)
    slot_table, token_table = route_tables(routes, experts, capacity)
    grid_table = token_table.reshape(experts, capacity, -1)
    probs_low = probs.astype(jnp.bfloat16).reshape(-1)
    send_weight = jnp.dot(slot_table, probs_low, preferred_element_type=jnp.float32).astype(
        jnp.bfloat16
    )
    weight_rows = jnp.pad(send_weight.reshape(experts, capacity), ((0, 0), (0, width - capacity)))
    cot_ext = jnp.concatenate([cotangent, weight_rows], axis=0)
    pick_weight = (
        jnp.arange(experts, dtype=jnp.int32)[:, None] == jnp.arange(experts, dtype=jnp.int32)[None, :]
    ).astype(jnp.bfloat16)
    table_ext = jnp.concatenate(
        [
            jnp.pad(grid_table, ((0, 0), (0, 0), (0, experts))),
            jnp.pad(pick_weight, ((0, 0), (grid_table.shape[2], 0)))[:, None, :],
        ],
        axis=1,
    )
    send_cot = jnp.dot(table_ext, cot_ext, preferred_element_type=jnp.float32).astype(jnp.bfloat16)
    got_cot_w = lax.all_to_all(send_cot, axes, split_axis=0, concat_axis=0, tiled=True)
    gate_grid = gate_saved[0].reshape(experts, capacity, -1)
    up_grid = up_saved[0].reshape(experts, capacity, -1)
    hidden, expert_out = expert_local(gate_grid, up_grid, down_weight[0])
    got_cot_w, hidden, expert_out = lax.optimization_barrier((got_cot_w, hidden, expert_out))
    got_cot = got_cot_w[:, :capacity, :]
    got_weight = got_cot_w[:, capacity, :capacity]
    half = width // 2
    tokens_a = jnp.dot(grid_table, tokens[:, :half], preferred_element_type=jnp.float32).astype(
        jnp.bfloat16
    )
    tokens_b = jnp.dot(grid_table, tokens[:, half:], preferred_element_type=jnp.float32).astype(
        jnp.bfloat16
    )
    got_cot, tokens_a, tokens_b = lax.optimization_barrier((got_cot, tokens_a, tokens_b))
    got_tokens_a = lax.all_to_all(
        tokens_a, axes, split_axis=0, concat_axis=0, tiled=True
    )
    cot_rows = got_cot
    grad_rows, grad_gate_pre, grad_up_pre, grad_down_w = expert_from_cot(
        cot_rows,
        got_weight,
        gate_grid,
        up_grid,
        gate_weight[0],
        up_weight[0],
        down_weight[0],
        hidden,
    )
    slot_route_dot = jnp.sum(
        cot_rows.astype(jnp.float32) * expert_out.astype(jnp.float32), axis=2
    ).astype(jnp.bfloat16)
    dot_row = jnp.pad(slot_route_dot, ((0, 0), (0, half - capacity)))[:, None, :]
    send_b = jnp.concatenate([tokens_b, dot_row], axis=1)
    got_b = lax.all_to_all(send_b, axes, split_axis=0, concat_axis=0, tiled=True)
    got_tokens_b = got_b[:, :capacity, :]
    route_dot = got_b[:, capacity, :capacity].reshape(-1)
    route_grad = lax.dot_general(
        slot_table, route_dot, contract_rows, preferred_element_type=jnp.float32
    ).reshape(probs.shape)
    inner_term = jnp.sum(probs * route_grad, axis=1, keepdims=True)
    chosen_grad = probs * (route_grad - inner_term)
    logit_grad = jnp.sum(
        jnp.where(picked, chosen_grad[:, :, None], jnp.float32(0.0)), axis=1
    ).astype(jnp.bfloat16)
    router_part = lax.dot_general(
        tokens, logit_grad, contract_rows, preferred_element_type=jnp.float32
    )
    part_rows = router_part.reshape(devices, 1, -1)
    part_rounded = lax.reduce_precision(part_rows, exponent_bits=8, mantissa_bits=7)
    part_high = part_rounded.astype(jnp.bfloat16)
    part_low = (part_rows - part_rounded).astype(jnp.bfloat16)
    send_back = jnp.concatenate([grad_rows, part_high, part_low], axis=1)
    got_back = lax.all_to_all(send_back, axes, split_axis=0, concat_axis=0, tiled=True)
    back_rows = got_back[:, :capacity, :]
    got_parts = got_back[:, capacity, :].astype(jnp.float32) + got_back[:, capacity + 1, :].astype(
        jnp.float32
    )
    chunk_sum = jnp.sum(got_parts, axis=0, keepdims=True)
    spread = jnp.broadcast_to(chunk_sum, got_parts.shape)
    got_sums = lax.all_to_all(spread, axes, split_axis=0, concat_axis=0, tiled=True)
    total_tokens = tokens.shape[0] * devices
    grad_router = got_sums.reshape(router_part.shape) * (1.0 / math.sqrt(total_tokens))
    grid_rows = (((0, 1), (0, 1)), ((), ()))

    def by_rows(pre):
        return jnp.concatenate(
            [
                lax.dot_general(got_tokens_a, pre, grid_rows, preferred_element_type=jnp.float32),
                lax.dot_general(got_tokens_b, pre, grid_rows, preferred_element_type=jnp.float32),
            ],
            axis=0,
        ).astype(jnp.bfloat16)

    grad_gate_w = by_rows(grad_gate_pre)
    grad_up_w = by_rows(grad_up_pre)
    grad_sum = lax.dot_general(
        grid_table, back_rows, (((0, 1), (0, 1)), ((), ())), preferred_element_type=jnp.float32
    )
    grad_tokens = (
        grad_sum
        + lax.dot_general(
            logit_grad, router_weight, contract_cols, preferred_element_type=jnp.float32
        )
    ).astype(jnp.bfloat16)
    return (grad_tokens, grad_gate_w[None], grad_up_w[None], grad_down_w[None], grad_router)


def solution(mesh):
    in_specs = (
        P(("outer", "inner"), None),
        P(("outer", "inner"), None),
        P(("outer", "inner"), None),
        P(),
        P(("outer", "inner"), None, None),
        P(("outer", "inner"), None, None),
        P(("outer", "inner"), None, None),
        P(("outer", "inner"), None, None),
        P(("outer", "inner"), None, None),
    )
    out_specs = (
        P(("outer", "inner"), None),
        P(("outer", "inner"), None, None),
        P(("outer", "inner"), None, None),
        P(("outer", "inner"), None, None),
        P(),
    )
    return jax.shard_map(body, mesh=mesh, in_specs=in_specs, out_specs=out_specs, check_vma=False)
```

```python
import math

import jax
import jax.numpy as jnp
from jax import lax
from jax.sharding import PartitionSpec as P

contract_rows = (((0,), (0,)), ((), ()))
contract_cols = (((1,), (1,)), ((), ()))


def route_tables(routes, experts, capacity):
    flat_routes = routes.reshape(-1)
    onehot = (flat_routes[:, None] == jnp.arange(experts, dtype=jnp.int32)[None, :]).astype(
        jnp.int32
    )
    pairs = flat_routes.shape[0]
    lower = (
        jnp.arange(pairs, dtype=jnp.int32)[:, None] > jnp.arange(pairs, dtype=jnp.int32)[None, :]
    ).astype(jnp.bfloat16)
    earlier = jnp.dot(
        lower, onehot.astype(jnp.bfloat16), preferred_element_type=jnp.float32
    ).astype(jnp.int32)
    position = jnp.sum(earlier * onehot, axis=1)
    target = flat_routes * capacity + position
    slot_table = (
        jnp.arange(experts * capacity, dtype=jnp.int32)[:, None] == target[None, :]
    ).astype(jnp.bfloat16)
    pair_token = jnp.arange(pairs, dtype=jnp.int32) // routes.shape[1]
    token_code = jnp.stack(
        [pair_token // 16, pair_token % 16, jnp.ones_like(pair_token)], axis=1
    ).astype(jnp.bfloat16)
    slot_code = jnp.dot(slot_table, token_code, preferred_element_type=jnp.float32)
    slot_token = (slot_code[:, 0] * 16.0 + slot_code[:, 1]).astype(jnp.int32)
    filled = slot_code[:, 2] > 0.5
    token_table = (
        (slot_token[:, None] == jnp.arange(routes.shape[0], dtype=jnp.int32)[None, :])
        & filled[:, None]
    ).astype(jnp.bfloat16)
    return (slot_table, token_table)


def route_probs(tokens, routes, router_weight):
    router_logits = jnp.dot(tokens, router_weight, preferred_element_type=jnp.float32)
    picked = (
        routes[:, :, None] == jnp.arange(router_weight.shape[1], dtype=jnp.int32)[None, None, :]
    )
    chosen = jnp.sum(jnp.where(picked, router_logits[:, None, :], jnp.float32(0.0)), axis=2)
    exp_terms = jnp.exp(chosen)
    return (picked, exp_terms / jnp.sum(exp_terms, axis=1, keepdims=True))


def dispatch_block(tokens, cotangent, routes, router_weight, capacity):
    picked, probs = route_probs(tokens, routes, router_weight)
    slot_table, token_table = route_tables(routes, router_weight.shape[1], capacity)
    send_tokens = jnp.dot(token_table, tokens, preferred_element_type=jnp.float32).astype(
        jnp.bfloat16
    )
    send_cot = jnp.dot(token_table, cotangent, preferred_element_type=jnp.float32).astype(
        jnp.bfloat16
    )
    probs_low = probs.astype(jnp.bfloat16).reshape(-1)
    send_weight = jnp.dot(slot_table, probs_low, preferred_element_type=jnp.float32).astype(
        jnp.bfloat16
    )
    return (picked, probs, slot_table, token_table, send_tokens, send_cot, send_weight)


def slot_dot(cot_rows, out_rows):
    return jnp.sum(cot_rows.astype(jnp.float32) * out_rows.astype(jnp.float32), axis=1).astype(
        jnp.bfloat16
    )


def expert_backward(
    input_rows, cot_rows, weight_rows, gate_pre, up_pre, gate_matrix, up_matrix, down_matrix
):
    gate_value = gate_pre.astype(jnp.float32)
    up_value = up_pre.astype(jnp.float32)
    sigmoid_gate = jax.nn.sigmoid(gate_value)
    silu_gate = gate_value * sigmoid_gate
    hidden = (silu_gate * up_value).astype(jnp.bfloat16)
    expert_out = jnp.dot(hidden, down_matrix, preferred_element_type=jnp.float32).astype(
        jnp.bfloat16
    )
    scaled_cot = (weight_rows.astype(jnp.float32)[:, None] * cot_rows.astype(jnp.float32)).astype(
        jnp.bfloat16
    )
    grad_hidden = lax.dot_general(
        scaled_cot, down_matrix, contract_cols, preferred_element_type=jnp.float32
    )
    grad_gate_pre = (
        grad_hidden * up_value * sigmoid_gate * (1.0 + gate_value * (1.0 - sigmoid_gate))
    ).astype(jnp.bfloat16)
    grad_up_pre = (grad_hidden * silu_gate).astype(jnp.bfloat16)
    grad_rows = (
        lax.dot_general(
            grad_gate_pre, gate_matrix, contract_cols, preferred_element_type=jnp.float32
        )
        + lax.dot_general(grad_up_pre, up_matrix, contract_cols, preferred_element_type=jnp.float32)
    ).astype(jnp.bfloat16)
    grad_gate_w = lax.dot_general(
        input_rows, grad_gate_pre, contract_rows, preferred_element_type=jnp.float32
    ).astype(jnp.bfloat16)
    grad_up_w = lax.dot_general(
        input_rows, grad_up_pre, contract_rows, preferred_element_type=jnp.float32
    ).astype(jnp.bfloat16)
    grad_down_w = lax.dot_general(
        hidden, scaled_cot, contract_rows, preferred_element_type=jnp.float32
    ).astype(jnp.bfloat16)
    return (grad_rows, expert_out, grad_gate_w, grad_up_w, grad_down_w)


def finish_block(
    tokens, router_weight, picked, probs, slot_table, token_table, back_rows, route_dot
):
    grad_sum = lax.dot_general(
        token_table, back_rows, contract_rows, preferred_element_type=jnp.float32
    )
    route_grad = lax.dot_general(
        slot_table, route_dot, contract_rows, preferred_element_type=jnp.float32
    ).reshape(probs.shape)
    inner_term = jnp.sum(probs * route_grad, axis=1, keepdims=True)
    chosen_grad = probs * (route_grad - inner_term)
    logit_grad = jnp.sum(
        jnp.where(picked, chosen_grad[:, :, None], jnp.float32(0.0)), axis=1
    ).astype(jnp.bfloat16)
    grad_tokens = (
        grad_sum
        + lax.dot_general(
            logit_grad, router_weight, contract_cols, preferred_element_type=jnp.float32
        )
    ).astype(jnp.bfloat16)
    router_part = lax.dot_general(
        tokens, logit_grad, contract_rows, preferred_element_type=jnp.float32
    )
    return (grad_tokens, router_part)


def expert_local(gate_pre, up_pre, down_matrix):
    last = (((2,), (0,)), ((), ()))
    gate_value = gate_pre.astype(jnp.float32)
    sigmoid_gate = jax.nn.sigmoid(gate_value)
    hidden = (gate_value * sigmoid_gate * up_pre.astype(jnp.float32)).astype(jnp.bfloat16)
    expert_out = lax.dot_general(
        hidden, down_matrix, last, preferred_element_type=jnp.float32
    ).astype(jnp.bfloat16)
    return hidden, expert_out


def expert_from_cot(
    cot_rows, weight_rows, gate_pre, up_pre, gate_matrix, up_matrix, down_matrix, hidden
):
    last_t = (((2,), (1,)), ((), ()))
    grid_rows = (((0, 1), (0, 1)), ((), ()))
    gate_value = gate_pre.astype(jnp.float32)
    up_value = up_pre.astype(jnp.float32)
    sigmoid_gate = jax.nn.sigmoid(gate_value)
    silu_gate = gate_value * sigmoid_gate
    scaled_cot = (
        weight_rows.astype(jnp.float32)[:, :, None] * cot_rows.astype(jnp.float32)
    ).astype(jnp.bfloat16)
    grad_hidden = lax.dot_general(
        scaled_cot, down_matrix, last_t, preferred_element_type=jnp.float32
    )
    grad_gate_pre = (
        grad_hidden * up_value * sigmoid_gate * (1.0 + gate_value * (1.0 - sigmoid_gate))
    ).astype(jnp.bfloat16)
    grad_up_pre = (grad_hidden * silu_gate).astype(jnp.bfloat16)
    grad_rows = (
        lax.dot_general(grad_gate_pre, gate_matrix, last_t, preferred_element_type=jnp.float32)
        + lax.dot_general(grad_up_pre, up_matrix, last_t, preferred_element_type=jnp.float32)
    ).astype(jnp.bfloat16)
    grad_down_w = lax.dot_general(
        hidden, scaled_cot, grid_rows, preferred_element_type=jnp.float32
    ).astype(jnp.bfloat16)
    return (grad_rows, grad_gate_pre, grad_up_pre, grad_down_w)


def body(
    tokens,
    cotangent,
    routes,
    router_weight,
    gate_saved,
    up_saved,
    gate_weight,
    up_weight,
    down_weight,
):
    experts = router_weight.shape[1]
    width = tokens.shape[1]
    capacity = gate_saved.shape[1] // experts
    outer_size = lax.axis_size("outer")
    inner_size = lax.axis_size("inner")
    devices = outer_size * inner_size
    axes = ("outer", "inner")
    picked, probs = route_probs(tokens, routes, router_weight)
    slot_table, token_table = route_tables(routes, experts, capacity)
    grid_table = token_table.reshape(experts, capacity, -1)
    probs_low = probs.astype(jnp.bfloat16).reshape(-1)
    send_weight = jnp.dot(slot_table, probs_low, preferred_element_type=jnp.float32).astype(
        jnp.bfloat16
    )
    weight_rows = jnp.pad(send_weight.reshape(experts, capacity), ((0, 0), (0, width - capacity)))
    cot_ext = jnp.concatenate([cotangent, weight_rows], axis=0)
    pick_weight = (
        jnp.arange(experts, dtype=jnp.int32)[:, None] == jnp.arange(experts, dtype=jnp.int32)[None, :]
    ).astype(jnp.bfloat16)
    table_ext = jnp.concatenate(
        [
            jnp.pad(grid_table, ((0, 0), (0, 0), (0, experts))),
            jnp.pad(pick_weight, ((0, 0), (grid_table.shape[2], 0)))[:, None, :],
        ],
        axis=1,
    )
    send_cot = jnp.dot(table_ext, cot_ext, preferred_element_type=jnp.float32).astype(jnp.bfloat16)
    got_cot_w = lax.all_to_all(send_cot, axes, split_axis=0, concat_axis=0, tiled=True)
    gate_grid = gate_saved[0].reshape(experts, capacity, -1)
    up_grid = up_saved[0].reshape(experts, capacity, -1)
    hidden, expert_out = expert_local(gate_grid, up_grid, down_weight[0])
    got_cot_w, hidden, expert_out = lax.optimization_barrier((got_cot_w, hidden, expert_out))
    got_cot = got_cot_w[:, :capacity, :]
    got_weight = got_cot_w[:, capacity, :capacity]
    half = width // 2
    tokens_a = jnp.dot(grid_table, tokens[:, :half], preferred_element_type=jnp.float32).astype(
        jnp.bfloat16
    )
    tokens_b = jnp.dot(grid_table, tokens[:, half:], preferred_element_type=jnp.float32).astype(
        jnp.bfloat16
    )
    got_cot, tokens_a, tokens_b = lax.optimization_barrier((got_cot, tokens_a, tokens_b))
    got_tokens_a = lax.all_to_all(
        tokens_a, axes, split_axis=0, concat_axis=0, tiled=True
    )
    cot_rows = got_cot
    grad_rows, grad_gate_pre, grad_up_pre, grad_down_w = expert_from_cot(
        cot_rows,
        got_weight,
        gate_grid,
        up_grid,
        gate_weight[0],
        up_weight[0],
        down_weight[0],
        hidden,
    )
    slot_route_dot = jnp.sum(
        cot_rows.astype(jnp.float32) * expert_out.astype(jnp.float32), axis=2
    ).astype(jnp.bfloat16)
    dot_row = jnp.pad(slot_route_dot, ((0, 0), (0, half - capacity)))[:, None, :]
    send_b = jnp.concatenate([tokens_b, dot_row], axis=1)
    got_b = lax.all_to_all(send_b, axes, split_axis=0, concat_axis=0, tiled=True)
    got_tokens_b = got_b[:, :capacity, :]
    route_dot = got_b[:, capacity, :capacity].reshape(-1)
    route_grad = lax.dot_general(
        slot_table, route_dot, contract_rows, preferred_element_type=jnp.float32
    ).reshape(probs.shape)
    inner_term = jnp.sum(probs * route_grad, axis=1, keepdims=True)
    chosen_grad = probs * (route_grad - inner_term)
    logit_grad = jnp.sum(
        jnp.where(picked, chosen_grad[:, :, None], jnp.float32(0.0)), axis=1
    ).astype(jnp.bfloat16)
    router_part = lax.dot_general(
        tokens, logit_grad, contract_rows, preferred_element_type=jnp.float32
    )
    part_rows = router_part.reshape(devices, 1, -1)
    part_rounded = lax.reduce_precision(part_rows, exponent_bits=8, mantissa_bits=7)
    part_high = part_rounded.astype(jnp.bfloat16)
    part_low = (part_rows - part_rounded).astype(jnp.bfloat16)
    send_back = jnp.concatenate([grad_rows, part_high, part_low], axis=1)
    got_back = lax.all_to_all(send_back, axes, split_axis=0, concat_axis=0, tiled=True)
    back_rows = got_back[:, :capacity, :]
    got_parts = got_back[:, capacity, :].astype(jnp.float32) + got_back[:, capacity + 1, :].astype(
        jnp.float32
    )
    total_tokens = tokens.shape[0] * devices
    chunk_sum = jnp.sum(got_parts, axis=0, keepdims=True) * (1.0 / math.sqrt(total_tokens))
    spread = jnp.broadcast_to(chunk_sum, got_parts.shape)
    got_sums = lax.all_to_all(spread, axes, split_axis=0, concat_axis=0, tiled=True)
    grad_router = got_sums.reshape(router_part.shape)
    grid_rows = (((0, 1), (0, 1)), ((), ()))

    def by_rows(pre):
        return jnp.concatenate(
            [
                lax.dot_general(got_tokens_a, pre, grid_rows, preferred_element_type=jnp.float32),
                lax.dot_general(got_tokens_b, pre, grid_rows, preferred_element_type=jnp.float32),
            ],
            axis=0,
        ).astype(jnp.bfloat16)

    grad_gate_w = by_rows(grad_gate_pre)
    grad_up_w = by_rows(grad_up_pre)
    grad_sum = lax.dot_general(
        grid_table, back_rows, (((0, 1), (0, 1)), ((), ())), preferred_element_type=jnp.float32
    )
    grad_tokens = (
        grad_sum
        + lax.dot_general(
            logit_grad, router_weight, contract_cols, preferred_element_type=jnp.float32
        )
    ).astype(jnp.bfloat16)
    return (grad_tokens, grad_gate_w[None], grad_up_w[None], grad_down_w[None], grad_router)


def solution(mesh):
    in_specs = (
        P(("outer", "inner"), None),
        P(("outer", "inner"), None),
        P(("outer", "inner"), None),
        P(),
        P(("outer", "inner"), None, None),
        P(("outer", "inner"), None, None),
        P(("outer", "inner"), None, None),
        P(("outer", "inner"), None, None),
        P(("outer", "inner"), None, None),
    )
    out_specs = (
        P(("outer", "inner"), None),
        P(("outer", "inner"), None, None),
        P(("outer", "inner"), None, None),
        P(("outer", "inner"), None, None),
        P(),
    )
    return jax.shard_map(body, mesh=mesh, in_specs=in_specs, out_specs=out_specs, check_vma=False)
```
